256 devices in a mesh: wide: 64 (over y_lo, z, x), narrow: 4 (over y_hi, core).
Axes of the slice: x: 4, y: 4 (y_hi: 2, y_lo: 2; y = y_hi * 2 + y_lo), z: 8, core: 2. Of those that a mesh axis runs over, the one named last changes fastest.
Arguments:
- concentration: float32 [3, 512, 256, 128], P(None, 'wide', 'narrow'), may hold values from 0.5 to 2
- potential: float32 [512, 256, 128], P('wide', 'narrow'), may hold values from -6 to 6
- permittivity: float32 [512, 256, 128], P('wide', 'narrow'), may hold values from 1 to 10
- diffusivity: float32 [3], replicated, may hold values from 0.02 to 0.1
- valence: int32 [3], replicated, may hold values from -2 to 2
- charge_pos: float32 [3, 524288], P(None, ('wide', 'narrow')), may hold values from 0 to 1
- charge_q: float32 [1, 524288], P(None, ('wide', 'narrow')), may hold values from -64 to 64
- charge_tile: int32 [1, 524288], P(None, ('wide', 'narrow')), may hold values from 0 to 15
- near_index: int32 [64, 4, 512], P('wide', 'narrow'), may hold values from 0 to 65535
- brick_mask: int32 [64, 4], P('wide', 'narrow'), may hold values 0 or 1
Outputs:
- species_out: float32 [3, 512, 256, 128], P(None, 'wide', 'narrow')
- potential_out: float32 [512, 256, 128], P('wide', 'narrow')
The draws below stay inside these ranges and needn't reach their ends.
Inputs may be any that keep to these rules, and one draw needn't show every extreme that they name: `near_index`: an index of a node of the brick. `charge_tile`: a tile of the whole y range.
All inputs are finite; a program needn't handle non-finite values. No bound on the sum of `brick_mask` on one device may be relied on, other than what follows from the above.
Results may differ from the reference program's by a relative error of at most 0.0003.
Values sent between devices are 32-bit elements; how exact they have to be, the bound alone decides.
No kernel may reach another device: no remote copies, remote signals or barrier semaphores. Data moves between devices by JAX's collectives and lax.ppermute only.
A program may use at most 64 MiB of HBM per device.

```python
import math
import jax
import jax.numpy as jnp
from jax import lax

NX = 128
CY = 64
CZ = 8
SPECIES = 3
NEAR_DEV = 512
CH_DEV = 2048
STEPS = 2
SWEEPS = 6
NY = 256
NZ = 512
SLABS = 64
BANDS = 4
TILES = 16
TILE_ROWS = 16
CHARGES = 524288


def place_ends(array, rng, low, largest):
    shape = array.shape
    place = [jax.random.randint(jax.random.fold_in(rng, axis), (), 0, shape[axis]) for axis in range(len(shape))]
    array = array.at[tuple(place)].set(low)
    longest = shape.index(max(shape))
    place[longest] = (place[longest] + 1) % shape[longest]
    return array.at[tuple(place)].set(largest)


def steps_of(stream_key, extent, pieces, smallest, high):
    def one(axis_at, shards_of):
        heights = jax.random.uniform(jax.random.fold_in(jax.random.fold_in(stream_key, 6), axis_at), (shards_of,), jnp.float32, smallest / len(pieces), high / len(pieces))
        return jnp.repeat(jnp.exp(heights), extent[axis_at] // shards_of).reshape((-1,) + (1,) * (len(extent) - axis_at - 1))

    loudness = one(*pieces[0])
    for cut in pieces[1:]:
        loudness = loudness * one(*cut)
    return loudness


def normal_values(key, shape, spread, most, cuts=(), held_as=jnp.bfloat16):
    loudness = steps_of(key, shape, cuts, -0.22, 0.18) if cuts else 1.0
    drawn = jax.random.normal(key, shape, jnp.float32) * spread * loudness
    return jnp.minimum(jnp.maximum(drawn, -most), most).astype(held_as)


def setup_inputs(seed: int = 0) -> dict:
    key_of = jax.random.split(jax.random.key(seed), 11)
    concentration = jnp.clip(jnp.exp(math.log(2.0) - 1.3862944 * jax.random.uniform(key_of[0], (SPECIES, NZ, NY, NX), jnp.float32) ** steps_of(key_of[0], (SPECIES, NZ, NY, NX), ((1, 64), (2, 4)), -0.2, 0.2)), 0.5, 2.0)
    potential = normal_values(key_of[1], (NZ, NY, NX), 1.0, 6.0, ((0, 64), (1, 4)), jnp.float32)
    permittivity = jnp.clip(jnp.exp(math.log(10.0) - 2.3025851 * jax.random.uniform(key_of[2], (NZ, NY, NX), jnp.float32) ** steps_of(key_of[2], (NZ, NY, NX), ((0, 64), (1, 4)), -0.2, 0.2)), 1.0, 10.0)
    diffusivity = jnp.clip(jnp.exp(jax.random.uniform(key_of[3], (SPECIES,), jnp.float32, math.log(0.02), math.log(0.1))), 0.02, 0.1)
    valence = jax.random.randint(key_of[4], (SPECIES,), -2, 3).astype(jnp.int32)
    charge_pos = jnp.clip(1.0 * jax.random.uniform(key_of[5], (3, CHARGES), jnp.float32) ** steps_of(key_of[5], (3, CHARGES), ((1, 256),), -0.2, 0.2), 0.0, 1.0)
    charge_q = normal_values(key_of[6], (1, CHARGES), 10.0, 64.0, ((1, 256),), jnp.float32)
    charge_tile = place_ends(jax.random.randint(key_of[7], (1, CHARGES), 0, TILES), jax.random.fold_in(key_of[7], 1), 0, TILES - 1).astype(jnp.int32)
    near_index = place_ends(jax.random.randint(key_of[8], (SLABS, BANDS, NEAR_DEV), 0, CZ * CY * NX), jax.random.fold_in(key_of[8], 1), 0, (CZ * CY * NX) - 1).astype(jnp.int32)
    brick_mask = place_ends((jax.random.randint(key_of[9], (SLABS, BANDS), 0, 4) < 3).astype(jnp.int32), jax.random.fold_in(key_of[9], 1), 0, 1)
    return dict(concentration=concentration, potential=potential, permittivity=permittivity, diffusivity=diffusivity, valence=valence, charge_pos=charge_pos, charge_q=charge_q, charge_tile=charge_tile, near_index=near_index, brick_mask=brick_mask)


def relax(field_pad, perm_pad, source):
    centre = field_pad[1:-1, 1:-1]
    perm_centre = perm_pad[1:-1, 1:-1]
    numer = source
    denom = jnp.zeros_like(source)
    pairs = ((field_pad[2:, 1:-1], perm_pad[2:, 1:-1]), (field_pad[:-2, 1:-1], perm_pad[:-2, 1:-1]), (field_pad[1:-1, 2:], perm_pad[1:-1, 2:]), (field_pad[1:-1, :-2], perm_pad[1:-1, :-2]))
    for other_field, other_perm in pairs:
        weight = 0.5 * (perm_centre + other_perm)
        numer = numer + weight * other_field
        denom = denom + weight
    zeros_edge = jnp.zeros_like(centre[..., :1])
    upper_field = jnp.concatenate([centre[..., 1:], zeros_edge], axis=-1)
    lower_field = jnp.concatenate([zeros_edge, centre[..., :-1]], axis=-1)
    upper_perm = jnp.concatenate([perm_centre[..., 1:], perm_centre[..., -1:]], axis=-1)
    lower_perm = jnp.concatenate([perm_centre[..., :1], perm_centre[..., :-1]], axis=-1)
    for other_field, other_perm in ((upper_field, upper_perm), (lower_field, lower_perm)):
        weight = 0.5 * (perm_centre + other_perm)
        numer = numer + weight * other_field
        denom = denom + weight
    return numer / denom

def transport(species_pad, field_pad, diffusivity, charge_num):
    centre = species_pad[:, 1:-1, 1:-1]
    field_centre = field_pad[1:-1, 1:-1]
    drift = charge_num[:, None, None, None]
    total = jnp.zeros_like(centre)
    pairs = ((species_pad[:, 2:, 1:-1], field_pad[2:, 1:-1]), (species_pad[:, :-2, 1:-1], field_pad[:-2, 1:-1]), (species_pad[:, 1:-1, 2:], field_pad[1:-1, 2:]), (species_pad[:, 1:-1, :-2], field_pad[1:-1, :-2]))
    for other, other_field in pairs:
        total = total + (centre - other) - drift * 0.5 * (centre + other) * (other_field - field_centre)
    left = centre[..., :-1]
    right = centre[..., 1:]
    across = left - right - drift * 0.5 * (left + right) * (field_centre[..., 1:] - field_centre[..., :-1])
    zeros_edge = jnp.zeros_like(centre[..., :1])
    total = total + jnp.concatenate([across, zeros_edge], axis=-1)
    total = total - jnp.concatenate([zeros_edge, across], axis=-1)
    return centre - diffusivity[:, None, None, None] * total

def pair_field(node_z, node_y, node_x, node_tile, block, slab_float, depth, rows_total, width, tile_rows, tiles_all):
    charge_x = block[0] * width
    charge_y = (block[4] + block[1]) * tile_rows
    charge_z = (slab_float + block[2]) * depth
    strength = block[3]
    label = block[4]

    def one_block(nodes):
        pos_z, pos_y, pos_x, pos_tile = nodes
        offset_z = pos_z[:, None] - charge_z[None, :]
        offset_y = pos_y[:, None] - charge_y[None, :]
        offset_y = offset_y - rows_total * jnp.floor(offset_y / rows_total + 0.5)
        offset_x = pos_x[:, None] - charge_x[None, :]
        distance = jnp.sqrt(offset_z * offset_z + offset_y * offset_y + offset_x * offset_x)
        tile_gap = jnp.mod(pos_tile[:, None] - label[None, :], tiles_all)
        adjacent = (tile_gap == 0.0) | (tile_gap == 1.0) | (tile_gap == tiles_all - 1.0)
        term = strength[None, :] * jnp.exp(-distance / tile_rows) / jnp.sqrt(distance * distance + 1.0)
        return lax.optimization_barrier(jnp.sum(jnp.where(adjacent, term, 0.0), axis=1))
    shaped = tuple((arr.reshape(-1, 128) for arr in (node_z, node_y, node_x, node_tile)))
    return lax.map(one_block, shaped).reshape(-1)

def wrapped(field):
    return jnp.pad(field, [(0, 0)] * (field.ndim - 3) + [(1, 1), (1, 1), (0, 0)], mode='wrap')

def reference(concentration, potential, permittivity, diffusivity, valence, charge_pos, charge_q, charge_tile, near_index, brick_mask):
    charges = jnp.concatenate([charge_pos, charge_q, charge_tile.astype(jnp.float32)], axis=0)
    per_slab = BANDS * CH_DEV

    def one_slab(slab):
        block = lax.dynamic_slice_in_dim(charges, (slab * per_slab).astype(jnp.int32), per_slab, 1)
        index = lax.dynamic_index_in_dim(near_index, slab, 0, keepdims=False)
        band = jnp.arange(BANDS, dtype=jnp.int32)[:, None]
        local_z = index // (CY * NX)
        local_y = index // NX % CY
        local_x = index % NX
        global_z = slab * CZ + local_z
        global_y = band * CY + local_y
        node_tile = (global_y // TILE_ROWS).astype(jnp.float32)
        values = pair_field(global_z.astype(jnp.float32).reshape(-1), global_y.astype(jnp.float32).reshape(-1), local_x.astype(jnp.float32).reshape(-1), node_tile.reshape(-1), block, slab.astype(jnp.float32), CZ, float(NY), NX, float(TILE_ROWS), float(TILES))
        mask = lax.dynamic_index_in_dim(brick_mask, slab, 0, keepdims=False).astype(jnp.float32)
        values = values * jnp.repeat(mask, NEAR_DEV)
        flat = ((global_z * NY + global_y) * NX + local_x).reshape(-1).astype(jnp.int32)
        return (values, flat)
    values, flat = lax.map(one_slab, jnp.arange(SLABS, dtype=jnp.int32))
    electrode = jnp.zeros((NZ * NY * NX,), jnp.float32).at[flat.reshape(-1)].add(values.reshape(-1))
    electrode = electrode.reshape(NZ, NY, NX)
    charge_num = valence.astype(jnp.float32)
    perm_pad = wrapped(permittivity)
    field = potential
    species = concentration
    for step in range(STEPS):
        source = lax.optimization_barrier(jnp.sum(charge_num[:, None, None, None] * species, axis=0)) + electrode
        for sweep in range(SWEEPS):
            field = relax(wrapped(field), perm_pad, source)
        species = transport(wrapped(species), wrapped(field), diffusivity, charge_num)
    return (species, field)
```

```python
import jax
import jax.numpy as jnp
from jax import lax
from jax.sharding import PartitionSpec as P

TILES_DEV = 4
STEPS = 2
SWEEPS = 6


def with_halo(cells, sides, width):
    for axis, dim in sides:
        count = lax.axis_size(axis)
        head = lax.slice_in_dim(cells, 0, width, axis=dim)
        tail = lax.slice_in_dim(cells, cells.shape[dim] - width, cells.shape[dim], axis=dim)
        cells = jnp.concatenate(
            [
                lax.ppermute(tail, axis, [(i, (i + 1) % count) for i in range(count)]),
                cells,
                lax.ppermute(head, axis, [((i + 1) % count, i) for i in range(count)]),
            ],
            axis=dim,
        )
    return cells


def relax(field_pad, perm_pad, source):
    centre = field_pad[1:-1, 1:-1]
    perm_centre = perm_pad[1:-1, 1:-1]
    numer = source
    denom = jnp.zeros_like(source)
    pairs = (
        (field_pad[2:, 1:-1], perm_pad[2:, 1:-1]),
        (field_pad[:-2, 1:-1], perm_pad[:-2, 1:-1]),
        (field_pad[1:-1, 2:], perm_pad[1:-1, 2:]),
        (field_pad[1:-1, :-2], perm_pad[1:-1, :-2]),
    )
    for other_field, other_perm in pairs:
        weight = 0.5 * (perm_centre + other_perm)
        numer = numer + weight * other_field
        denom = denom + weight
    zeros_edge = jnp.zeros_like(centre[..., :1])
    upper_field = jnp.concatenate([centre[..., 1:], zeros_edge], axis=-1)
    lower_field = jnp.concatenate([zeros_edge, centre[..., :-1]], axis=-1)
    upper_perm = jnp.concatenate([perm_centre[..., 1:], perm_centre[..., -1:]], axis=-1)
    lower_perm = jnp.concatenate([perm_centre[..., :1], perm_centre[..., :-1]], axis=-1)
    for other_field, other_perm in ((upper_field, upper_perm), (lower_field, lower_perm)):
        weight = 0.5 * (perm_centre + other_perm)
        numer = numer + weight * other_field
        denom = denom + weight
    return numer / denom


def transport(species_pad, field_pad, diffusivity, charge_num):
    centre = species_pad[:, 1:-1, 1:-1]
    field_centre = field_pad[1:-1, 1:-1]
    drift = charge_num[:, None, None, None]
    total = jnp.zeros_like(centre)
    pairs = (
        (species_pad[:, 2:, 1:-1], field_pad[2:, 1:-1]),
        (species_pad[:, :-2, 1:-1], field_pad[:-2, 1:-1]),
        (species_pad[:, 1:-1, 2:], field_pad[1:-1, 2:]),
        (species_pad[:, 1:-1, :-2], field_pad[1:-1, :-2]),
    )
    for other, other_field in pairs:
        total = (
            total + (centre - other) - drift * 0.5 * (centre + other) * (other_field - field_centre)
        )
    left = centre[..., :-1]
    right = centre[..., 1:]
    across = (
        left
        - right
        - drift * 0.5 * (left + right) * (field_centre[..., 1:] - field_centre[..., :-1])
    )
    zeros_edge = jnp.zeros_like(centre[..., :1])
    total = total + jnp.concatenate([across, zeros_edge], axis=-1)
    total = total - jnp.concatenate([zeros_edge, across], axis=-1)
    return centre - diffusivity[:, None, None, None] * total


def pair_field(
    node_z,
    node_y,
    node_x,
    node_tile,
    block,
    slab_float,
    depth,
    rows_total,
    width,
    tile_rows,
    tiles_all,
):
    charge_x = block[0] * width
    charge_y = (block[4] + block[1]) * tile_rows
    charge_z = (slab_float + block[2]) * depth
    strength = block[3]
    label = block[4]

    def one_block(nodes):
        pos_z, pos_y, pos_x, pos_tile = nodes
        offset_z = pos_z[:, None] - charge_z[None, :]
        offset_y = pos_y[:, None] - charge_y[None, :]
        offset_y = offset_y - rows_total * jnp.floor(offset_y / rows_total + 0.5)
        offset_x = pos_x[:, None] - charge_x[None, :]
        distance = jnp.sqrt(offset_z * offset_z + offset_y * offset_y + offset_x * offset_x)
        tile_gap = jnp.mod(pos_tile[:, None] - label[None, :], tiles_all)
        adjacent = (tile_gap == 0.0) | (tile_gap == 1.0) | (tile_gap == tiles_all - 1.0)
        term = (
            strength[None, :] * jnp.exp(-distance / tile_rows) / jnp.sqrt(distance * distance + 1.0)
        )
        return jnp.sum(jnp.where(adjacent, term, 0.0), axis=1)

    shaped = tuple((arr.reshape(-1, 128) for arr in (node_z, node_y, node_x, node_tile)))
    return lax.map(one_block, shaped).reshape(-1)


def ring(x, axis, shift):
    count = lax.axis_size(axis)
    return lax.ppermute(x, axis, [(i, (i + shift) % count) for i in range(count)])


def deep_halo(items, axis_z, axis_y):
    for back, axis in ((3, axis_z), (2, axis_y)):
        tops, bots = [], []
        for a, w in items:
            dim = a.ndim - back
            n = a.shape[dim]
            tops.append(lax.slice_in_dim(a, n - w, n, axis=dim))
            bots.append(lax.slice_in_dim(a, 0, w, axis=dim))
        minor = items[0][0].shape[-1]
        top = jnp.concatenate([t.reshape(-1, minor) for t in tops], axis=0)
        bot = jnp.concatenate([b.reshape(-1, minor) for b in bots], axis=0)
        below = ring(top, axis, 1)
        above = ring(bot, axis, -1)
        out, at = [], 0
        for (a, w), t in zip(items, tops):
            size = t.size // minor
            lo = below[at:at + size].reshape(t.shape)
            hi = above[at:at + size].reshape(t.shape)
            at += size
            out.append((jnp.concatenate([lo, a, hi], axis=a.ndim - back), w))
        items = out
    return [a for a, _ in items]


def box(a, have, want):
    cut = have - want
    if cut == 0:
        return a
    return a[..., cut:a.shape[-3] - cut, cut:a.shape[-2] - cut, :]


def per_device(
    concentration,
    potential,
    permittivity,
    diffusivity,
    valence,
    charge_pos,
    charge_q,
    charge_tile,
    near_index,
    brick_mask,
):
    depth, height, width = potential.shape
    bands = lax.axis_size("narrow")
    rows_total = float(height * bands)
    tiles_all = float(TILES_DEV * bands)
    tile_rows = height // TILES_DEV
    slab = lax.axis_index("wide")
    band = lax.axis_index("narrow")
    index = near_index[0, 0]
    local_z = index // (height * width)
    local_y = index // width % height
    local_x = index % width
    global_z = slab * depth + local_z
    global_y = band * height + local_y
    node_z = global_z.astype(jnp.float32)
    node_y = global_y.astype(jnp.float32)
    node_x = local_x.astype(jnp.float32)
    node_tile = (global_y // tile_rows).astype(jnp.float32)
    slab_float = slab.astype(jnp.float32)
    charges = jnp.concatenate([charge_pos, charge_q, charge_tile.astype(jnp.float32)], axis=0)
    values = pair_field(
        node_z,
        node_y,
        node_x,
        node_tile,
        lax.all_gather(charges, "narrow", axis=1, tiled=True),
        slab_float,
        depth,
        rows_total,
        width,
        float(tile_rows),
        tiles_all,
    )
    values = values * brick_mask[0, 0].astype(jnp.float32)
    electrode = jnp.zeros((depth * height * width,), jnp.float32).at[index].add(values)
    electrode = electrode.reshape(depth, height, width)
    charge_num = valence.astype(jnp.float32)
    deep = SWEEPS + 1
    field = potential
    species = concentration
    perm_ext = None
    for step in range(STEPS):
        source = jnp.sum(charge_num[:, None, None, None] * species, axis=0) + electrode
        items = [(field, deep), (source, deep - 1), (species, 1)]
        if perm_ext is None:
            items.append((permittivity, deep))
        got = deep_halo(items, "wide", "narrow")
        field_e, source_e, species_e = got[0], got[1], got[2]
        if perm_ext is None:
            perm_ext = got[3]
        have = deep
        for sweep in range(SWEEPS):
            field_e = relax(field_e, box(perm_ext, deep, have), box(source_e, deep - 1, have - 1))
            have -= 1
        species = transport(species_e, field_e, diffusivity, charge_num)
        field = field_e[1:-1, 1:-1]
    return (species, field)


def solution(mesh):
    in_specs = (
        P(None, "wide", "narrow", None),
        P("wide", "narrow", None),
        P("wide", "narrow", None),
        P(),
        P(),
        P(None, ("wide", "narrow")),
        P(None, ("wide", "narrow")),
        P(None, ("wide", "narrow")),
        P("wide", "narrow", None),
        P("wide", "narrow"),
    )
    out_specs = (P(None, "wide", "narrow", None), P("wide", "narrow", None))
    return jax.shard_map(
        per_device, mesh=mesh, in_specs=in_specs, out_specs=out_specs, check_vma=False
    )
```

```python
import jax
import jax.numpy as jnp
from jax import lax
from jax.sharding import PartitionSpec as P
from jax.experimental import pallas as pl
from jax.experimental.pallas import tpu as pltpu

TILES_DEV = 4
STEPS = 2
SWEEPS = 6


def with_halo(cells, sides, width):
    for axis, dim in sides:
        count = lax.axis_size(axis)
        head = lax.slice_in_dim(cells, 0, width, axis=dim)
        tail = lax.slice_in_dim(cells, cells.shape[dim] - width, cells.shape[dim], axis=dim)
        cells = jnp.concatenate(
            [
                lax.ppermute(tail, axis, [(i, (i + 1) % count) for i in range(count)]),
                cells,
                lax.ppermute(head, axis, [((i + 1) % count, i) for i in range(count)]),
            ],
            axis=dim,
        )
    return cells


def relax(field_pad, perm_pad, source):
    centre = field_pad[1:-1, 1:-1]
    perm_centre = perm_pad[1:-1, 1:-1]
    numer = source
    denom = jnp.zeros_like(source)
    pairs = (
        (field_pad[2:, 1:-1], perm_pad[2:, 1:-1]),
        (field_pad[:-2, 1:-1], perm_pad[:-2, 1:-1]),
        (field_pad[1:-1, 2:], perm_pad[1:-1, 2:]),
        (field_pad[1:-1, :-2], perm_pad[1:-1, :-2]),
    )
    for other_field, other_perm in pairs:
        weight = 0.5 * (perm_centre + other_perm)
        numer = numer + weight * other_field
        denom = denom + weight
    zeros_edge = jnp.zeros_like(centre[..., :1])
    upper_field = jnp.concatenate([centre[..., 1:], zeros_edge], axis=-1)
    lower_field = jnp.concatenate([zeros_edge, centre[..., :-1]], axis=-1)
    upper_perm = jnp.concatenate([perm_centre[..., 1:], perm_centre[..., -1:]], axis=-1)
    lower_perm = jnp.concatenate([perm_centre[..., :1], perm_centre[..., :-1]], axis=-1)
    for other_field, other_perm in ((upper_field, upper_perm), (lower_field, lower_perm)):
        weight = 0.5 * (perm_centre + other_perm)
        numer = numer + weight * other_field
        denom = denom + weight
    return numer / denom


def transport(species_pad, field_pad, diffusivity, charge_num):
    centre = species_pad[:, 1:-1, 1:-1]
    field_centre = field_pad[1:-1, 1:-1]
    drift = charge_num[:, None, None, None]
    total = jnp.zeros_like(centre)
    pairs = (
        (species_pad[:, 2:, 1:-1], field_pad[2:, 1:-1]),
        (species_pad[:, :-2, 1:-1], field_pad[:-2, 1:-1]),
        (species_pad[:, 1:-1, 2:], field_pad[1:-1, 2:]),
        (species_pad[:, 1:-1, :-2], field_pad[1:-1, :-2]),
    )
    for other, other_field in pairs:
        total = (
            total + (centre - other) - drift * 0.5 * (centre + other) * (other_field - field_centre)
        )
    left = centre[..., :-1]
    right = centre[..., 1:]
    across = (
        left
        - right
        - drift * 0.5 * (left + right) * (field_centre[..., 1:] - field_centre[..., :-1])
    )
    zeros_edge = jnp.zeros_like(centre[..., :1])
    total = total + jnp.concatenate([across, zeros_edge], axis=-1)
    total = total - jnp.concatenate([zeros_edge, across], axis=-1)
    return centre - diffusivity[:, None, None, None] * total


def pair_field(
    node_z,
    node_y,
    node_x,
    node_tile,
    block,
    slab_float,
    depth,
    rows_total,
    width,
    tile_rows,
    tiles_all,
):
    charge_x = block[0] * width
    charge_y = (block[4] + block[1]) * tile_rows
    charge_z = (slab_float + block[2]) * depth
    strength = block[3]
    label = block[4]

    def one_block(nodes):
        pos_z, pos_y, pos_x, pos_tile = nodes
        offset_z = pos_z[:, None] - charge_z[None, :]
        offset_y = pos_y[:, None] - charge_y[None, :]
        offset_y = offset_y - rows_total * jnp.floor(offset_y / rows_total + 0.5)
        offset_x = pos_x[:, None] - charge_x[None, :]
        distance = jnp.sqrt(offset_z * offset_z + offset_y * offset_y + offset_x * offset_x)
        tile_gap = jnp.mod(pos_tile[:, None] - label[None, :], tiles_all)
        adjacent = (tile_gap == 0.0) | (tile_gap == 1.0) | (tile_gap == tiles_all - 1.0)
        term = (
            strength[None, :] * jnp.exp(-distance / tile_rows) / jnp.sqrt(distance * distance + 1.0)
        )
        return jnp.sum(jnp.where(adjacent, term, 0.0), axis=1)

    shaped = tuple((arr.reshape(-1, 128) for arr in (node_z, node_y, node_x, node_tile)))
    return lax.map(one_block, shaped).reshape(-1)


def ring(x, axis, shift):
    count = lax.axis_size(axis)
    return lax.ppermute(x, axis, [(i, (i + shift) % count) for i in range(count)])


def deep_halo(items, axis_z, axis_y):
    for back, axis, pick in ((3, axis_z, 1), (2, axis_y, 2)):
        tops, bots = [], []
        for item in items:
            a, w = item[0], item[pick]
            dim = a.ndim - back
            n = a.shape[dim]
            tops.append(lax.slice_in_dim(a, n - w, n, axis=dim))
            bots.append(lax.slice_in_dim(a, 0, w, axis=dim))
        minor = items[0][0].shape[-1]
        top = jnp.concatenate([t.reshape(-1, minor) for t in tops], axis=0)
        bot = jnp.concatenate([t.reshape(-1, minor) for t in bots], axis=0)
        below = ring(top, axis, 1)
        above = ring(bot, axis, -1)
        out, at = [], 0
        for item, t in zip(items, tops):
            a = item[0]
            size = t.size // minor
            lo = below[at:at + size].reshape(t.shape)
            hi = above[at:at + size].reshape(t.shape)
            at += size
            out.append((jnp.concatenate([lo, a, hi], axis=a.ndim - back),) + tuple(item[1:]))
        items = out
    return [item[0] for item in items]


def step_kernel(dif_ref, val_ref, f_ref, p_ref, s_ref, c_ref, fo_ref, co_ref, fa, fb, w_ref):
    planes, rows, lanes = f_ref.shape
    species, inner = c_ref.shape[0], c_ref.shape[1] - 2
    hz = (planes - inner) // 2
    hy = (rows - co_ref.shape[2]) // 2
    out_rows = co_ref.shape[2]
    lane = lax.broadcasted_iota(jnp.int32, (rows, lanes), 1)
    top = lane == lanes - 1
    bot = lane == 0

    def ysh(a, d):
        return pltpu.roll(a, (-d) % rows, 0)

    def xsh(a, d):
        return pltpu.roll(a, (-d) % lanes, 1)

    def weights(z, carry):
        pc = p_ref[z]
        ws = (
            0.5 * (pc + p_ref[z + 1]),
            0.5 * (pc + p_ref[z - 1]),
            0.5 * (pc + ysh(pc, 1)),
            0.5 * (pc + ysh(pc, -1)),
            0.5 * (pc + jnp.where(top, pc, xsh(pc, 1))),
            0.5 * (pc + jnp.where(bot, pc, xsh(pc, -1))),
        )
        den = jnp.zeros_like(pc)
        for k, w in enumerate(ws):
            w_ref[k, z] = w
            den = den + w
        w_ref[6, z] = den
        return carry

    lax.fori_loop(1, planes - 1, weights, 0)
    bufs = (fa, fb)
    sweeps = hz - 1
    for k in range(sweeps):
        rd = f_ref if k == 0 else bufs[(k - 1) % 2]
        wr = bufs[k % 2]

        def sweep(z, carry, rd=rd, wr=wr):
            fc = rd[z]
            numer = s_ref[z]
            numer = numer + w_ref[0, z] * rd[z + 1]
            numer = numer + w_ref[1, z] * rd[z - 1]
            numer = numer + w_ref[2, z] * ysh(fc, 1)
            numer = numer + w_ref[3, z] * ysh(fc, -1)
            numer = numer + w_ref[4, z] * jnp.where(top, 0.0, xsh(fc, 1))
            numer = numer + w_ref[5, z] * jnp.where(bot, 0.0, xsh(fc, -1))
            wr[z] = numer / w_ref[6, z]
            return carry

        lax.fori_loop(k + 1, planes - k - 1, sweep, 0)
    final = bufs[(sweeps - 1) % 2]

    def move(z, carry):
        zf = z + hz
        fc = final[zf]
        fo_ref[z] = fc[hy:hy + out_rows]
        pairs_field = (final[zf + 1], final[zf - 1], ysh(fc, 1), ysh(fc, -1))
        fr = xsh(fc, 1)
        for s in range(species):
            drift = val_ref[s]
            c = c_ref[s, z + 1]
            others = (c_ref[s, z + 2], c_ref[s, z], ysh(c, 1), ysh(c, -1))
            total = jnp.zeros_like(c)
            for other, other_field in zip(others, pairs_field):
                total = total + (c - other) - drift * 0.5 * (c + other) * (other_field - fc)
            right = xsh(c, 1)
            across = c - right - drift * 0.5 * (c + right) * (fr - fc)
            across = jnp.where(top, 0.0, across)
            total = total + across
            total = total - xsh(across, -1)
            new = c - dif_ref[s] * total
            co_ref[s, z] = new[hy:hy + out_rows]
        return carry

    lax.fori_loop(0, inner, move, 0)


def time_step(diffusivity, charge_num, field_e, perm_e, source_e, species_e):
    planes, rows, lanes = field_e.shape
    species, inner = species_e.shape[0], species_e.shape[1] - 2
    out_rows = rows - 2 * (SWEEPS + 2)
    smem = pl.BlockSpec(memory_space=pltpu.SMEM)
    vmem = pl.BlockSpec(memory_space=pltpu.VMEM)
    points = planes * rows * lanes
    return pl.pallas_call(
        step_kernel,
        out_shape=(
            jax.ShapeDtypeStruct((inner, out_rows, lanes), jnp.float32),
            jax.ShapeDtypeStruct((species, inner, out_rows, lanes), jnp.float32),
        ),
        in_specs=[smem, smem, vmem, vmem, vmem, vmem],
        out_specs=(vmem, vmem),
        scratch_shapes=[
            pltpu.VMEM((planes, rows, lanes), jnp.float32),
            pltpu.VMEM((planes, rows, lanes), jnp.float32),
            pltpu.VMEM((7, planes, rows, lanes), jnp.float32),
        ],
        cost_estimate=pl.CostEstimate(
            flops=points * (20 * SWEEPS + 20) + species_e.size * 30,
            transcendentals=0,
            bytes_accessed=4 * (3 * points + species_e.size + inner * out_rows * lanes * (species + 1)),
        ),
    )(diffusivity, charge_num, field_e, perm_e, source_e, species_e)


def box(a, have, want):
    cut = have - want
    if cut == 0:
        return a
    return a[..., cut:a.shape[-3] - cut, cut:a.shape[-2] - cut, :]


def per_device(
    concentration,
    potential,
    permittivity,
    diffusivity,
    valence,
    charge_pos,
    charge_q,
    charge_tile,
    near_index,
    brick_mask,
):
    depth, height, width = potential.shape
    bands = lax.axis_size("narrow")
    rows_total = float(height * bands)
    tiles_all = float(TILES_DEV * bands)
    tile_rows = height // TILES_DEV
    slab = lax.axis_index("wide")
    band = lax.axis_index("narrow")
    index = near_index[0, 0]
    local_z = index // (height * width)
    local_y = index // width % height
    local_x = index % width
    global_z = slab * depth + local_z
    global_y = band * height + local_y
    node_z = global_z.astype(jnp.float32)
    node_y = global_y.astype(jnp.float32)
    node_x = local_x.astype(jnp.float32)
    node_tile = (global_y // tile_rows).astype(jnp.float32)
    slab_float = slab.astype(jnp.float32)
    charges = jnp.concatenate([charge_pos, charge_q, charge_tile.astype(jnp.float32)], axis=0)
    values = pair_field(
        node_z,
        node_y,
        node_x,
        node_tile,
        lax.all_gather(charges, "narrow", axis=1, tiled=True),
        slab_float,
        depth,
        rows_total,
        width,
        float(tile_rows),
        tiles_all,
    )
    values = values * brick_mask[0, 0].astype(jnp.float32)
    electrode = jnp.zeros((depth * height * width,), jnp.float32).at[index].add(values)
    electrode = electrode.reshape(depth, height, width)
    charge_num = valence.astype(jnp.float32)
    deep = SWEEPS + 1
    wide_y = SWEEPS + 2
    field = potential
    species = concentration
    perm_ext = None
    for step in range(STEPS):
        source = jnp.sum(charge_num[:, None, None, None] * species, axis=0) + electrode
        items = [(field, deep, wide_y), (source, deep, wide_y), (species, 1, wide_y)]
        if perm_ext is None:
            items.append((permittivity, deep, wide_y))
        got = deep_halo(items, "wide", "narrow")
        if perm_ext is None:
            perm_ext = got[3]
        field, species = time_step(diffusivity, charge_num, got[0], perm_ext, got[1], got[2])
    return (species, field)


def solution(mesh):
    in_specs = (
        P(None, "wide", "narrow", None),
        P("wide", "narrow", None),
        P("wide", "narrow", None),
        P(),
        P(),
        P(None, ("wide", "narrow")),
        P(None, ("wide", "narrow")),
        P(None, ("wide", "narrow")),
        P("wide", "narrow", None),
        P("wide", "narrow"),
    )
    out_specs = (P(None, "wide", "narrow", None), P("wide", "narrow", None))
    return jax.shard_map(
        per_device, mesh=mesh, in_specs=in_specs, out_specs=out_specs, check_vma=False
    )
```

```python
import jax
import jax.numpy as jnp
from jax import lax
from jax.sharding import PartitionSpec as P
from jax.experimental import pallas as pl
from jax.experimental.pallas import tpu as pltpu

TILES_DEV = 4
STEPS = 2
SWEEPS = 6


def with_halo(cells, sides, width):
    for axis, dim in sides:
        count = lax.axis_size(axis)
        head = lax.slice_in_dim(cells, 0, width, axis=dim)
        tail = lax.slice_in_dim(cells, cells.shape[dim] - width, cells.shape[dim], axis=dim)
        cells = jnp.concatenate(
            [
                lax.ppermute(tail, axis, [(i, (i + 1) % count) for i in range(count)]),
                cells,
                lax.ppermute(head, axis, [((i + 1) % count, i) for i in range(count)]),
            ],
            axis=dim,
        )
    return cells


def relax(field_pad, perm_pad, source):
    centre = field_pad[1:-1, 1:-1]
    perm_centre = perm_pad[1:-1, 1:-1]
    numer = source
    denom = jnp.zeros_like(source)
    pairs = (
        (field_pad[2:, 1:-1], perm_pad[2:, 1:-1]),
        (field_pad[:-2, 1:-1], perm_pad[:-2, 1:-1]),
        (field_pad[1:-1, 2:], perm_pad[1:-1, 2:]),
        (field_pad[1:-1, :-2], perm_pad[1:-1, :-2]),
    )
    for other_field, other_perm in pairs:
        weight = 0.5 * (perm_centre + other_perm)
        numer = numer + weight * other_field
        denom = denom + weight
    zeros_edge = jnp.zeros_like(centre[..., :1])
    upper_field = jnp.concatenate([centre[..., 1:], zeros_edge], axis=-1)
    lower_field = jnp.concatenate([zeros_edge, centre[..., :-1]], axis=-1)
    upper_perm = jnp.concatenate([perm_centre[..., 1:], perm_centre[..., -1:]], axis=-1)
    lower_perm = jnp.concatenate([perm_centre[..., :1], perm_centre[..., :-1]], axis=-1)
    for other_field, other_perm in ((upper_field, upper_perm), (lower_field, lower_perm)):
        weight = 0.5 * (perm_centre + other_perm)
        numer = numer + weight * other_field
        denom = denom + weight
    return numer / denom


def transport(species_pad, field_pad, diffusivity, charge_num):
    centre = species_pad[:, 1:-1, 1:-1]
    field_centre = field_pad[1:-1, 1:-1]
    drift = charge_num[:, None, None, None]
    total = jnp.zeros_like(centre)
    pairs = (
        (species_pad[:, 2:, 1:-1], field_pad[2:, 1:-1]),
        (species_pad[:, :-2, 1:-1], field_pad[:-2, 1:-1]),
        (species_pad[:, 1:-1, 2:], field_pad[1:-1, 2:]),
        (species_pad[:, 1:-1, :-2], field_pad[1:-1, :-2]),
    )
    for other, other_field in pairs:
        total = (
            total + (centre - other) - drift * 0.5 * (centre + other) * (other_field - field_centre)
        )
    left = centre[..., :-1]
    right = centre[..., 1:]
    across = (
        left
        - right
        - drift * 0.5 * (left + right) * (field_centre[..., 1:] - field_centre[..., :-1])
    )
    zeros_edge = jnp.zeros_like(centre[..., :1])
    total = total + jnp.concatenate([across, zeros_edge], axis=-1)
    total = total - jnp.concatenate([zeros_edge, across], axis=-1)
    return centre - diffusivity[:, None, None, None] * total


def pair_field(
    node_z,
    node_y,
    node_x,
    node_tile,
    block,
    slab_float,
    depth,
    rows_total,
    width,
    tile_rows,
    tiles_all,
):
    charge_x = block[0] * width
    charge_y = (block[4] + block[1]) * tile_rows
    charge_z = (slab_float + block[2]) * depth
    strength = block[3]
    label = block[4]

    def one_block(nodes):
        pos_z, pos_y, pos_x, pos_tile = nodes
        offset_z = pos_z[:, None] - charge_z[None, :]
        offset_y = pos_y[:, None] - charge_y[None, :]
        offset_y = offset_y - rows_total * jnp.floor(offset_y / rows_total + 0.5)
        offset_x = pos_x[:, None] - charge_x[None, :]
        distance = jnp.sqrt(offset_z * offset_z + offset_y * offset_y + offset_x * offset_x)
        tile_gap = jnp.mod(pos_tile[:, None] - label[None, :], tiles_all)
        adjacent = (tile_gap == 0.0) | (tile_gap == 1.0) | (tile_gap == tiles_all - 1.0)
        term = (
            strength[None, :] * jnp.exp(-distance / tile_rows) / jnp.sqrt(distance * distance + 1.0)
        )
        return jnp.sum(jnp.where(adjacent, term, 0.0), axis=1)

    half = node_z.shape[0] // 2
    parts = [one_block(tuple(arr[k * half:(k + 1) * half] for arr in (node_z, node_y, node_x, node_tile))) for k in range(2)]
    return jnp.concatenate(parts)


def ring(x, axis, shift):
    count = lax.axis_size(axis)
    return lax.ppermute(x, axis, [(i, (i + shift) % count) for i in range(count)])


def deep_halo(items, axis_z, axis_y):
    for back, axis, pick in ((3, axis_z, 1), (2, axis_y, 2)):
        tops, bots = [], []
        for item in items:
            a, w = item[0], item[pick]
            dim = a.ndim - back
            n = a.shape[dim]
            tops.append(lax.slice_in_dim(a, n - w, n, axis=dim))
            bots.append(lax.slice_in_dim(a, 0, w, axis=dim))
        minor = items[0][0].shape[-1]
        top = jnp.concatenate([t.reshape(-1, minor) for t in tops], axis=0)
        bot = jnp.concatenate([t.reshape(-1, minor) for t in bots], axis=0)
        below = ring(top, axis, 1)
        above = ring(bot, axis, -1)
        out, at = [], 0
        for item, t in zip(items, tops):
            a = item[0]
            size = t.size // minor
            lo = below[at:at + size].reshape(t.shape)
            hi = above[at:at + size].reshape(t.shape)
            at += size
            out.append((jnp.concatenate([lo, a, hi], axis=a.ndim - back),) + tuple(item[1:]))
        items = out
    return [item[0] for item in items]


def step_kernel(dif_ref, val_ref, f_ref, p_ref, s_ref, c_ref, fo_ref, co_ref, fa, fb, w_ref):
    planes, rows, lanes = f_ref.shape
    species, inner = c_ref.shape[0], c_ref.shape[1] - 2
    hz = (planes - inner) // 2
    hy = (rows - co_ref.shape[2]) // 2
    out_rows = co_ref.shape[2]
    lane = lax.broadcasted_iota(jnp.int32, (rows, lanes), 1)
    top = lane == lanes - 1
    bot = lane == 0

    def ysh(a, d):
        return pltpu.roll(a, (-d) % rows, 0)

    def xsh(a, d):
        return pltpu.roll(a, (-d) % lanes, 1)

    def weights(z, carry):
        pc = p_ref[z]
        ws = (
            0.5 * (pc + p_ref[z + 1]),
            0.5 * (pc + p_ref[z - 1]),
            0.5 * (pc + ysh(pc, 1)),
            0.5 * (pc + ysh(pc, -1)),
            0.5 * (pc + jnp.where(top, pc, xsh(pc, 1))),
            0.5 * (pc + jnp.where(bot, pc, xsh(pc, -1))),
        )
        den = jnp.zeros_like(pc)
        for k, w in enumerate(ws):
            w_ref[k, z] = w
            den = den + w
        w_ref[6, z] = den
        return carry

    lax.fori_loop(1, planes - 1, weights, 0)
    bufs = (fa, fb)
    sweeps = hz - 1
    for k in range(sweeps):
        rd = f_ref if k == 0 else bufs[(k - 1) % 2]
        wr = bufs[k % 2]

        def sweep(z, carry, rd=rd, wr=wr):
            fc = rd[z]
            numer = s_ref[z]
            numer = numer + w_ref[0, z] * rd[z + 1]
            numer = numer + w_ref[1, z] * rd[z - 1]
            numer = numer + w_ref[2, z] * ysh(fc, 1)
            numer = numer + w_ref[3, z] * ysh(fc, -1)
            numer = numer + w_ref[4, z] * jnp.where(top, 0.0, xsh(fc, 1))
            numer = numer + w_ref[5, z] * jnp.where(bot, 0.0, xsh(fc, -1))
            wr[z] = numer / w_ref[6, z]
            return carry

        lax.fori_loop(k + 1, planes - k - 1, sweep, 0)
    final = bufs[(sweeps - 1) % 2]

    def move(z, carry):
        zf = z + hz
        fc = final[zf]
        fo_ref[z] = fc[hy:hy + out_rows]
        pairs_field = (final[zf + 1], final[zf - 1], ysh(fc, 1), ysh(fc, -1))
        fr = xsh(fc, 1)
        for s in range(species):
            drift = val_ref[s]
            c = c_ref[s, z + 1]
            others = (c_ref[s, z + 2], c_ref[s, z], ysh(c, 1), ysh(c, -1))
            total = jnp.zeros_like(c)
            for other, other_field in zip(others, pairs_field):
                total = total + (c - other) - drift * 0.5 * (c + other) * (other_field - fc)
            right = xsh(c, 1)
            across = c - right - drift * 0.5 * (c + right) * (fr - fc)
            across = jnp.where(top, 0.0, across)
            total = total + across
            total = total - xsh(across, -1)
            new = c - dif_ref[s] * total
            co_ref[s, z] = new[hy:hy + out_rows]
        return carry

    lax.fori_loop(0, inner, move, 0)


def time_step(diffusivity, charge_num, field_e, perm_e, source_e, species_e):
    planes, rows, lanes = field_e.shape
    species, inner = species_e.shape[0], species_e.shape[1] - 2
    out_rows = rows - 2 * (SWEEPS + 2)
    smem = pl.BlockSpec(memory_space=pltpu.SMEM)
    vmem = pl.BlockSpec(memory_space=pltpu.VMEM)
    points = planes * rows * lanes
    return pl.pallas_call(
        step_kernel,
        out_shape=(
            jax.ShapeDtypeStruct((inner, out_rows, lanes), jnp.float32),
            jax.ShapeDtypeStruct((species, inner, out_rows, lanes), jnp.float32),
        ),
        in_specs=[smem, smem, vmem, vmem, vmem, vmem],
        out_specs=(vmem, vmem),
        scratch_shapes=[
            pltpu.VMEM((planes, rows, lanes), jnp.float32),
            pltpu.VMEM((planes, rows, lanes), jnp.float32),
            pltpu.VMEM((7, planes, rows, lanes), jnp.float32),
        ],
        cost_estimate=pl.CostEstimate(
            flops=points * (20 * SWEEPS + 20) + species_e.size * 30,
            transcendentals=0,
            bytes_accessed=4 * (3 * points + species_e.size + inner * out_rows * lanes * (species + 1)),
        ),
    )(diffusivity, charge_num, field_e, perm_e, source_e, species_e)


def box(a, have, want):
    cut = have - want
    if cut == 0:
        return a
    return a[..., cut:a.shape[-3] - cut, cut:a.shape[-2] - cut, :]


def per_device(
    concentration,
    potential,
    permittivity,
    diffusivity,
    valence,
    charge_pos,
    charge_q,
    charge_tile,
    near_index,
    brick_mask,
):
    depth, height, width = potential.shape
    bands = lax.axis_size("narrow")
    rows_total = float(height * bands)
    tiles_all = float(TILES_DEV * bands)
    tile_rows = height // TILES_DEV
    slab = lax.axis_index("wide")
    band = lax.axis_index("narrow")
    index = near_index[0, 0]
    local_z = index // (height * width)
    local_y = index // width % height
    local_x = index % width
    global_z = slab * depth + local_z
    global_y = band * height + local_y
    node_z = global_z.astype(jnp.float32)
    node_y = global_y.astype(jnp.float32)
    node_x = local_x.astype(jnp.float32)
    node_tile = (global_y // tile_rows).astype(jnp.float32)
    slab_float = slab.astype(jnp.float32)
    deep = SWEEPS + 1
    wide_y = SWEEPS + 2
    first = deep_halo(
        [(potential, deep, wide_y), (permittivity, deep, wide_y), (concentration, 1, wide_y)],
        "wide",
        "narrow",
    )
    charges = jnp.concatenate([charge_pos, charge_q, charge_tile.astype(jnp.float32)], axis=0)
    values = pair_field(
        node_z,
        node_y,
        node_x,
        node_tile,
        lax.all_gather(charges, "narrow", axis=1, tiled=True),
        slab_float,
        depth,
        rows_total,
        width,
        float(tile_rows),
        tiles_all,
    )
    values = values * brick_mask[0, 0].astype(jnp.float32)
    electrode = jnp.zeros((depth * height * width,), jnp.float32).at[index].add(values)
    electrode = electrode.reshape(depth, height, width)
    charge_num = valence.astype(jnp.float32)
    field = potential
    species = concentration
    perm_ext = first[1]
    for step in range(STEPS):
        source = jnp.sum(charge_num[:, None, None, None] * species, axis=0) + electrode
        if step == 0:
            field_e, species_e = first[0], first[2]
            (source_e,) = deep_halo([(source, deep, wide_y)], "wide", "narrow")
        else:
            field_e, source_e, species_e = deep_halo(
                [(field, deep, wide_y), (source, deep, wide_y), (species, 1, wide_y)], "wide", "narrow"
            )
        field, species = time_step(diffusivity, charge_num, field_e, perm_ext, source_e, species_e)
    return (species, field)


def solution(mesh):
    in_specs = (
        P(None, "wide", "narrow", None),
        P("wide", "narrow", None),
        P("wide", "narrow", None),
        P(),
        P(),
        P(None, ("wide", "narrow")),
        P(None, ("wide", "narrow")),
        P(None, ("wide", "narrow")),
        P("wide", "narrow", None),
        P("wide", "narrow"),
    )
    out_specs = (P(None, "wide", "narrow", None), P("wide", "narrow", None))
    return jax.shard_map(
        per_device, mesh=mesh, in_specs=in_specs, out_specs=out_specs, check_vma=False
    )
```

```python
import jax
import jax.numpy as jnp
from jax import lax
from jax.sharding import PartitionSpec as P
from jax.experimental import pallas as pl
from jax.experimental.pallas import tpu as pltpu

TILES_DEV = 4
STEPS = 2
SWEEPS = 6


def with_halo(cells, sides, width):
    for axis, dim in sides:
        count = lax.axis_size(axis)
        head = lax.slice_in_dim(cells, 0, width, axis=dim)
        tail = lax.slice_in_dim(cells, cells.shape[dim] - width, cells.shape[dim], axis=dim)
        cells = jnp.concatenate(
            [
                lax.ppermute(tail, axis, [(i, (i + 1) % count) for i in range(count)]),
                cells,
                lax.ppermute(head, axis, [((i + 1) % count, i) for i in range(count)]),
            ],
            axis=dim,
        )
    return cells


def relax(field_pad, perm_pad, source):
    centre = field_pad[1:-1, 1:-1]
    perm_centre = perm_pad[1:-1, 1:-1]
    numer = source
    denom = jnp.zeros_like(source)
    pairs = (
        (field_pad[2:, 1:-1], perm_pad[2:, 1:-1]),
        (field_pad[:-2, 1:-1], perm_pad[:-2, 1:-1]),
        (field_pad[1:-1, 2:], perm_pad[1:-1, 2:]),
        (field_pad[1:-1, :-2], perm_pad[1:-1, :-2]),
    )
    for other_field, other_perm in pairs:
        weight = 0.5 * (perm_centre + other_perm)
        numer = numer + weight * other_field
        denom = denom + weight
    zeros_edge = jnp.zeros_like(centre[..., :1])
    upper_field = jnp.concatenate([centre[..., 1:], zeros_edge], axis=-1)
    lower_field = jnp.concatenate([zeros_edge, centre[..., :-1]], axis=-1)
    upper_perm = jnp.concatenate([perm_centre[..., 1:], perm_centre[..., -1:]], axis=-1)
    lower_perm = jnp.concatenate([perm_centre[..., :1], perm_centre[..., :-1]], axis=-1)
    for other_field, other_perm in ((upper_field, upper_perm), (lower_field, lower_perm)):
        weight = 0.5 * (perm_centre + other_perm)
        numer = numer + weight * other_field
        denom = denom + weight
    return numer / denom


def transport(species_pad, field_pad, diffusivity, charge_num):
    centre = species_pad[:, 1:-1, 1:-1]
    field_centre = field_pad[1:-1, 1:-1]
    drift = charge_num[:, None, None, None]
    total = jnp.zeros_like(centre)
    pairs = (
        (species_pad[:, 2:, 1:-1], field_pad[2:, 1:-1]),
        (species_pad[:, :-2, 1:-1], field_pad[:-2, 1:-1]),
        (species_pad[:, 1:-1, 2:], field_pad[1:-1, 2:]),
        (species_pad[:, 1:-1, :-2], field_pad[1:-1, :-2]),
    )
    for other, other_field in pairs:
        total = (
            total + (centre - other) - drift * 0.5 * (centre + other) * (other_field - field_centre)
        )
    left = centre[..., :-1]
    right = centre[..., 1:]
    across = (
        left
        - right
        - drift * 0.5 * (left + right) * (field_centre[..., 1:] - field_centre[..., :-1])
    )
    zeros_edge = jnp.zeros_like(centre[..., :1])
    total = total + jnp.concatenate([across, zeros_edge], axis=-1)
    total = total - jnp.concatenate([zeros_edge, across], axis=-1)
    return centre - diffusivity[:, None, None, None] * total


def pair_field(
    node_z,
    node_y,
    node_x,
    node_tile,
    block,
    slab_float,
    depth,
    rows_total,
    width,
    tile_rows,
    tiles_all,
):
    charge_x = block[0] * width
    charge_y = (block[4] + block[1]) * tile_rows
    charge_z = (slab_float + block[2]) * depth
    strength = block[3]
    label = block[4]

    def one_block(nodes):
        pos_z, pos_y, pos_x, pos_tile = nodes
        offset_z = pos_z[:, None] - charge_z[None, :]
        offset_y = pos_y[:, None] - charge_y[None, :]
        offset_y = offset_y - rows_total * jnp.floor(offset_y / rows_total + 0.5)
        offset_x = pos_x[:, None] - charge_x[None, :]
        distance = jnp.sqrt(offset_z * offset_z + offset_y * offset_y + offset_x * offset_x)
        tile_gap = jnp.mod(pos_tile[:, None] - label[None, :], tiles_all)
        adjacent = (tile_gap == 0.0) | (tile_gap == 1.0) | (tile_gap == tiles_all - 1.0)
        term = (
            strength[None, :] * jnp.exp(-distance / tile_rows) / jnp.sqrt(distance * distance + 1.0)
        )
        return jnp.sum(jnp.where(adjacent, term, 0.0), axis=1)

    half = node_z.shape[0] // 2
    parts = [one_block(tuple(arr[k * half:(k + 1) * half] for arr in (node_z, node_y, node_x, node_tile))) for k in range(2)]
    return jnp.concatenate(parts)


def ring(x, axis, shift):
    count = lax.axis_size(axis)
    return lax.ppermute(x, axis, [(i, (i + shift) % count) for i in range(count)])


def deep_halo(items, axis_z, axis_y):
    for back, axis, pick in ((3, axis_z, 1), (2, axis_y, 2)):
        tops, bots = [], []
        for item in items:
            a, w = item[0], item[pick]
            dim = a.ndim - back
            n = a.shape[dim]
            tops.append(lax.slice_in_dim(a, n - w, n, axis=dim))
            bots.append(lax.slice_in_dim(a, 0, w, axis=dim))
        minor = items[0][0].shape[-1]
        top = jnp.concatenate([t.reshape(-1, minor) for t in tops], axis=0)
        bot = jnp.concatenate([t.reshape(-1, minor) for t in bots], axis=0)
        below = ring(top, axis, 1)
        above = ring(bot, axis, -1)
        out, at = [], 0
        for item, t in zip(items, tops):
            a = item[0]
            size = t.size // minor
            lo = below[at:at + size].reshape(t.shape)
            hi = above[at:at + size].reshape(t.shape)
            at += size
            out.append((jnp.concatenate([lo, a, hi], axis=a.ndim - back),) + tuple(item[1:]))
        items = out
    return [item[0] for item in items]


def step_kernel(dif_ref, val_ref, f_ref, p_ref, s_ref, c_ref, fo_ref, co_ref, fa, fb, w_ref):
    planes, rows, lanes = f_ref.shape
    species, inner = c_ref.shape[0], c_ref.shape[1] - 2
    hz = (planes - inner) // 2
    hy = (rows - co_ref.shape[2]) // 2
    out_rows = co_ref.shape[2]
    lane = lax.broadcasted_iota(jnp.int32, (rows, lanes), 1)
    top = lane == lanes - 1
    bot = lane == 0

    def ysh(a, d):
        return pltpu.roll(a, (-d) % rows, 0)

    def xsh(a, d):
        return pltpu.roll(a, (-d) % lanes, 1)

    def weights(z, carry):
        pc = p_ref[z]
        ws = (
            0.5 * (pc + p_ref[z + 1]),
            0.5 * (pc + p_ref[z - 1]),
            0.5 * (pc + ysh(pc, 1)),
            0.5 * (pc + ysh(pc, -1)),
            0.5 * (pc + jnp.where(top, pc, xsh(pc, 1))),
            0.5 * (pc + jnp.where(bot, pc, xsh(pc, -1))),
        )
        den = jnp.zeros_like(pc)
        for k, w in enumerate(ws):
            w_ref[k, z] = w
            den = den + w
        w_ref[6, z] = 1.0 / den
        return carry

    lax.fori_loop(1, planes - 1, weights, 0)
    bufs = (fa, fb)
    sweeps = hz - 1
    for k in range(sweeps):
        rd = f_ref if k == 0 else bufs[(k - 1) % 2]
        wr = bufs[k % 2]

        def sweep(z, carry, rd=rd, wr=wr):
            fc = rd[z]
            numer = s_ref[z]
            numer = numer + w_ref[0, z] * rd[z + 1]
            numer = numer + w_ref[1, z] * rd[z - 1]
            numer = numer + w_ref[2, z] * ysh(fc, 1)
            numer = numer + w_ref[3, z] * ysh(fc, -1)
            numer = numer + w_ref[4, z] * jnp.where(top, 0.0, xsh(fc, 1))
            numer = numer + w_ref[5, z] * jnp.where(bot, 0.0, xsh(fc, -1))
            wr[z] = numer * w_ref[6, z]
            return carry

        lax.fori_loop(k + 1, planes - k - 1, sweep, 0)
    final = bufs[(sweeps - 1) % 2]

    def move(z, carry):
        zf = z + hz
        fc = final[zf]
        fo_ref[z] = fc[hy:hy + out_rows]
        pairs_field = (final[zf + 1], final[zf - 1], ysh(fc, 1), ysh(fc, -1))
        fr = xsh(fc, 1)
        for s in range(species):
            drift = val_ref[s]
            c = c_ref[s, z + 1]
            others = (c_ref[s, z + 2], c_ref[s, z], ysh(c, 1), ysh(c, -1))
            total = jnp.zeros_like(c)
            for other, other_field in zip(others, pairs_field):
                total = total + (c - other) - drift * 0.5 * (c + other) * (other_field - fc)
            right = xsh(c, 1)
            across = c - right - drift * 0.5 * (c + right) * (fr - fc)
            across = jnp.where(top, 0.0, across)
            total = total + across
            total = total - xsh(across, -1)
            new = c - dif_ref[s] * total
            co_ref[s, z] = new[hy:hy + out_rows]
        return carry

    lax.fori_loop(0, inner, move, 0)


def time_step(diffusivity, charge_num, field_e, perm_e, source_e, species_e):
    planes, rows, lanes = field_e.shape
    species, inner = species_e.shape[0], species_e.shape[1] - 2
    out_rows = rows - 2 * (SWEEPS + 2)
    smem = pl.BlockSpec(memory_space=pltpu.SMEM)
    vmem = pl.BlockSpec(memory_space=pltpu.VMEM)
    points = planes * rows * lanes
    return pl.pallas_call(
        step_kernel,
        out_shape=(
            jax.ShapeDtypeStruct((inner, out_rows, lanes), jnp.float32),
            jax.ShapeDtypeStruct((species, inner, out_rows, lanes), jnp.float32),
        ),
        in_specs=[smem, smem, vmem, vmem, vmem, vmem],
        out_specs=(vmem, vmem),
        scratch_shapes=[
            pltpu.VMEM((planes, rows, lanes), jnp.float32),
            pltpu.VMEM((planes, rows, lanes), jnp.float32),
            pltpu.VMEM((7, planes, rows, lanes), jnp.float32),
        ],
        cost_estimate=pl.CostEstimate(
            flops=points * (20 * SWEEPS + 20) + species_e.size * 30,
            transcendentals=0,
            bytes_accessed=4 * (3 * points + species_e.size + inner * out_rows * lanes * (species + 1)),
        ),
    )(diffusivity, charge_num, field_e, perm_e, source_e, species_e)


def box(a, have, want):
    cut = have - want
    if cut == 0:
        return a
    return a[..., cut:a.shape[-3] - cut, cut:a.shape[-2] - cut, :]


def per_device(
    concentration,
    potential,
    permittivity,
    diffusivity,
    valence,
    charge_pos,
    charge_q,
    charge_tile,
    near_index,
    brick_mask,
):
    depth, height, width = potential.shape
    bands = lax.axis_size("narrow")
    rows_total = float(height * bands)
    tiles_all = float(TILES_DEV * bands)
    tile_rows = height // TILES_DEV
    slab = lax.axis_index("wide")
    band = lax.axis_index("narrow")
    index = near_index[0, 0]
    local_z = index // (height * width)
    local_y = index // width % height
    local_x = index % width
    global_z = slab * depth + local_z
    global_y = band * height + local_y
    node_z = global_z.astype(jnp.float32)
    node_y = global_y.astype(jnp.float32)
    node_x = local_x.astype(jnp.float32)
    node_tile = (global_y // tile_rows).astype(jnp.float32)
    slab_float = slab.astype(jnp.float32)
    deep = SWEEPS + 1
    wide_y = SWEEPS + 2
    charges = jnp.concatenate([charge_pos, charge_q, charge_tile.astype(jnp.float32)], axis=0)
    gathered = lax.all_gather(charges, "narrow", axis=1, tiled=True)
    gathered, potential, permittivity, concentration = lax.optimization_barrier(
        (gathered, potential, permittivity, concentration)
    )
    first = deep_halo(
        [(potential, deep, wide_y), (permittivity, deep, wide_y), (concentration, 1, wide_y)],
        "wide",
        "narrow",
    )
    values = pair_field(
        node_z,
        node_y,
        node_x,
        node_tile,
        gathered,
        slab_float,
        depth,
        rows_total,
        width,
        float(tile_rows),
        tiles_all,
    )
    values = values * brick_mask[0, 0].astype(jnp.float32)
    electrode = jnp.zeros((depth * height * width,), jnp.float32).at[index].add(values)
    electrode = electrode.reshape(depth, height, width)
    charge_num = valence.astype(jnp.float32)
    field = potential
    species = concentration
    perm_ext = first[1]
    for step in range(STEPS):
        source = jnp.sum(charge_num[:, None, None, None] * species, axis=0) + electrode
        if step == 0:
            field_e, species_e = first[0], first[2]
            (source_e,) = deep_halo([(source, deep, wide_y)], "wide", "narrow")
        else:
            field_e, source_e, species_e = deep_halo(
                [(field, deep, wide_y), (source, deep, wide_y), (species, 1, wide_y)], "wide", "narrow"
            )
        field, species = time_step(diffusivity, charge_num, field_e, perm_ext, source_e, species_e)
    return (species, field)


def solution(mesh):
    in_specs = (
        P(None, "wide", "narrow", None),
        P("wide", "narrow", None),
        P("wide", "narrow", None),
        P(),
        P(),
        P(None, ("wide", "narrow")),
        P(None, ("wide", "narrow")),
        P(None, ("wide", "narrow")),
        P("wide", "narrow", None),
        P("wide", "narrow"),
    )
    out_specs = (P(None, "wide", "narrow", None), P("wide", "narrow", None))
    return jax.shard_map(
        per_device, mesh=mesh, in_specs=in_specs, out_specs=out_specs, check_vma=False
    )
```

```python
import jax
import jax.numpy as jnp
from jax import lax
from jax.sharding import PartitionSpec as P
from jax.experimental import pallas as pl
from jax.experimental.pallas import tpu as pltpu

TILES_DEV = 4
STEPS = 2
SWEEPS = 6


def with_halo(cells, sides, width):
    for axis, dim in sides:
        count = lax.axis_size(axis)
        head = lax.slice_in_dim(cells, 0, width, axis=dim)
        tail = lax.slice_in_dim(cells, cells.shape[dim] - width, cells.shape[dim], axis=dim)
        cells = jnp.concatenate(
            [
                lax.ppermute(tail, axis, [(i, (i + 1) % count) for i in range(count)]),
                cells,
                lax.ppermute(head, axis, [((i + 1) % count, i) for i in range(count)]),
            ],
            axis=dim,
        )
    return cells


def relax(field_pad, perm_pad, source):
    centre = field_pad[1:-1, 1:-1]
    perm_centre = perm_pad[1:-1, 1:-1]
    numer = source
    denom = jnp.zeros_like(source)
    pairs = (
        (field_pad[2:, 1:-1], perm_pad[2:, 1:-1]),
        (field_pad[:-2, 1:-1], perm_pad[:-2, 1:-1]),
        (field_pad[1:-1, 2:], perm_pad[1:-1, 2:]),
        (field_pad[1:-1, :-2], perm_pad[1:-1, :-2]),
    )
    for other_field, other_perm in pairs:
        weight = 0.5 * (perm_centre + other_perm)
        numer = numer + weight * other_field
        denom = denom + weight
    zeros_edge = jnp.zeros_like(centre[..., :1])
    upper_field = jnp.concatenate([centre[..., 1:], zeros_edge], axis=-1)
    lower_field = jnp.concatenate([zeros_edge, centre[..., :-1]], axis=-1)
    upper_perm = jnp.concatenate([perm_centre[..., 1:], perm_centre[..., -1:]], axis=-1)
    lower_perm = jnp.concatenate([perm_centre[..., :1], perm_centre[..., :-1]], axis=-1)
    for other_field, other_perm in ((upper_field, upper_perm), (lower_field, lower_perm)):
        weight = 0.5 * (perm_centre + other_perm)
        numer = numer + weight * other_field
        denom = denom + weight
    return numer / denom


def transport(species_pad, field_pad, diffusivity, charge_num):
    centre = species_pad[:, 1:-1, 1:-1]
    field_centre = field_pad[1:-1, 1:-1]
    drift = charge_num[:, None, None, None]
    total = jnp.zeros_like(centre)
    pairs = (
        (species_pad[:, 2:, 1:-1], field_pad[2:, 1:-1]),
        (species_pad[:, :-2, 1:-1], field_pad[:-2, 1:-1]),
        (species_pad[:, 1:-1, 2:], field_pad[1:-1, 2:]),
        (species_pad[:, 1:-1, :-2], field_pad[1:-1, :-2]),
    )
    for other, other_field in pairs:
        total = (
            total + (centre - other) - drift * 0.5 * (centre + other) * (other_field - field_centre)
        )
    left = centre[..., :-1]
    right = centre[..., 1:]
    across = (
        left
        - right
        - drift * 0.5 * (left + right) * (field_centre[..., 1:] - field_centre[..., :-1])
    )
    zeros_edge = jnp.zeros_like(centre[..., :1])
    total = total + jnp.concatenate([across, zeros_edge], axis=-1)
    total = total - jnp.concatenate([zeros_edge, across], axis=-1)
    return centre - diffusivity[:, None, None, None] * total


def pair_field(
    node_z,
    node_y,
    node_x,
    node_tile,
    block,
    slab_float,
    depth,
    rows_total,
    width,
    tile_rows,
    tiles_all,
):
    charge_x = block[0] * width
    charge_y = (block[4] + block[1]) * tile_rows
    charge_z = (slab_float + block[2]) * depth
    strength = block[3]
    label = block[4]

    def one_block(nodes):
        pos_z, pos_y, pos_x, pos_tile = nodes
        offset_z = pos_z[:, None] - charge_z[None, :]
        offset_y = pos_y[:, None] - charge_y[None, :]
        offset_y = offset_y - rows_total * jnp.floor(offset_y / rows_total + 0.5)
        offset_x = pos_x[:, None] - charge_x[None, :]
        distance = jnp.sqrt(offset_z * offset_z + offset_y * offset_y + offset_x * offset_x)
        tile_gap = jnp.mod(pos_tile[:, None] - label[None, :], tiles_all)
        adjacent = (tile_gap == 0.0) | (tile_gap == 1.0) | (tile_gap == tiles_all - 1.0)
        term = (
            strength[None, :] * jnp.exp(-distance / tile_rows) / jnp.sqrt(distance * distance + 1.0)
        )
        return jnp.sum(jnp.where(adjacent, term, 0.0), axis=1)

    half = node_z.shape[0] // 2
    parts = [one_block(tuple(arr[k * half:(k + 1) * half] for arr in (node_z, node_y, node_x, node_tile))) for k in range(2)]
    return jnp.concatenate(parts)


def ring(x, axis, shift):
    count = lax.axis_size(axis)
    return lax.ppermute(x, axis, [(i, (i + shift) % count) for i in range(count)])


def deep_halo(items, axis_z, axis_y):
    for back, axis, pick in ((3, axis_z, 1), (2, axis_y, 2)):
        tops, bots = [], []
        for item in items:
            a, w = item[0], item[pick]
            dim = a.ndim - back
            n = a.shape[dim]
            tops.append(lax.slice_in_dim(a, n - w, n, axis=dim))
            bots.append(lax.slice_in_dim(a, 0, w, axis=dim))
        minor = items[0][0].shape[-1]
        top = jnp.concatenate([t.reshape(-1, minor) for t in tops], axis=0)
        bot = jnp.concatenate([t.reshape(-1, minor) for t in bots], axis=0)
        below = ring(top, axis, 1)
        above = ring(bot, axis, -1)
        out, at = [], 0
        for item, t in zip(items, tops):
            a = item[0]
            size = t.size // minor
            lo = below[at:at + size].reshape(t.shape)
            hi = above[at:at + size].reshape(t.shape)
            at += size
            out.append((jnp.concatenate([lo, a, hi], axis=a.ndim - back),) + tuple(item[1:]))
        items = out
    return [item[0] for item in items]


def step_kernel(
    dif_ref, val_ref, f_hbm, p_hbm, s_hbm, c_hbm, fo_ref, co_ref, f_ref, p_ref, s_ref, c_ref, fa, fb, w_ref, sems
):
    copies = [
        pltpu.make_async_copy(src, dst, sems.at[k])
        for k, (src, dst) in enumerate(((p_hbm, p_ref), (f_hbm, f_ref), (s_hbm, s_ref), (c_hbm, c_ref)))
    ]
    for copy in copies:
        copy.start()
    planes, rows, lanes = f_ref.shape
    species, inner = c_ref.shape[0], c_ref.shape[1] - 2
    hz = (planes - inner) // 2
    hy = (rows - co_ref.shape[2]) // 2
    out_rows = co_ref.shape[2]
    lane = lax.broadcasted_iota(jnp.int32, (rows, lanes), 1)
    top = lane == lanes - 1
    bot = lane == 0

    def ysh(a, d):
        return pltpu.roll(a, (-d) % rows, 0)

    def xsh(a, d):
        return pltpu.roll(a, (-d) % lanes, 1)

    def weights(z, carry):
        pc = p_ref[z]
        ws = (
            0.5 * (pc + p_ref[z + 1]),
            0.5 * (pc + p_ref[z - 1]),
            0.5 * (pc + ysh(pc, 1)),
            0.5 * (pc + ysh(pc, -1)),
            0.5 * (pc + jnp.where(top, pc, xsh(pc, 1))),
            0.5 * (pc + jnp.where(bot, pc, xsh(pc, -1))),
        )
        den = jnp.zeros_like(pc)
        for k, w in enumerate(ws):
            w_ref[k, z] = w
            den = den + w
        w_ref[6, z] = 1.0 / den
        return carry

    copies[0].wait()
    lax.fori_loop(1, planes - 1, weights, 0)
    copies[1].wait()
    copies[2].wait()
    bufs = (fa, fb)
    sweeps = hz - 1
    for k in range(sweeps):
        rd = f_ref if k == 0 else bufs[(k - 1) % 2]
        wr = bufs[k % 2]

        def sweep(z, carry, rd=rd, wr=wr):
            fc = rd[z]
            numer = s_ref[z]
            numer = numer + w_ref[0, z] * rd[z + 1]
            numer = numer + w_ref[1, z] * rd[z - 1]
            numer = numer + w_ref[2, z] * ysh(fc, 1)
            numer = numer + w_ref[3, z] * ysh(fc, -1)
            numer = numer + w_ref[4, z] * jnp.where(top, 0.0, xsh(fc, 1))
            numer = numer + w_ref[5, z] * jnp.where(bot, 0.0, xsh(fc, -1))
            wr[z] = numer * w_ref[6, z]
            return carry

        lax.fori_loop(k + 1, planes - k - 1, sweep, 0)
    final = bufs[(sweeps - 1) % 2]
    copies[3].wait()

    def move(z, carry):
        zf = z + hz
        fc = final[zf]
        fo_ref[z] = fc[hy:hy + out_rows]
        pairs_field = (final[zf + 1], final[zf - 1], ysh(fc, 1), ysh(fc, -1))
        fr = xsh(fc, 1)
        for s in range(species):
            drift = val_ref[s]
            c = c_ref[s, z + 1]
            others = (c_ref[s, z + 2], c_ref[s, z], ysh(c, 1), ysh(c, -1))
            total = jnp.zeros_like(c)
            for other, other_field in zip(others, pairs_field):
                total = total + (c - other) - drift * 0.5 * (c + other) * (other_field - fc)
            right = xsh(c, 1)
            across = c - right - drift * 0.5 * (c + right) * (fr - fc)
            across = jnp.where(top, 0.0, across)
            total = total + across
            total = total - xsh(across, -1)
            new = c - dif_ref[s] * total
            co_ref[s, z] = new[hy:hy + out_rows]
        return carry

    lax.fori_loop(0, inner, move, 0)


def time_step(diffusivity, charge_num, field_e, perm_e, source_e, species_e):
    planes, rows, lanes = field_e.shape
    species, inner = species_e.shape[0], species_e.shape[1] - 2
    out_rows = rows - 2 * (SWEEPS + 2)
    smem = pl.BlockSpec(memory_space=pltpu.SMEM)
    vmem = pl.BlockSpec(memory_space=pltpu.VMEM)
    hbm = pl.BlockSpec(memory_space=pl.ANY)
    points = planes * rows * lanes
    return pl.pallas_call(
        step_kernel,
        out_shape=(
            jax.ShapeDtypeStruct((inner, out_rows, lanes), jnp.float32),
            jax.ShapeDtypeStruct((species, inner, out_rows, lanes), jnp.float32),
        ),
        in_specs=[smem, smem, hbm, hbm, hbm, hbm],
        out_specs=(vmem, vmem),
        scratch_shapes=[
            pltpu.VMEM((planes, rows, lanes), jnp.float32),
            pltpu.VMEM((planes, rows, lanes), jnp.float32),
            pltpu.VMEM((planes, rows, lanes), jnp.float32),
            pltpu.VMEM(species_e.shape, jnp.float32),
            pltpu.VMEM((planes, rows, lanes), jnp.float32),
            pltpu.VMEM((planes, rows, lanes), jnp.float32),
            pltpu.VMEM((7, planes, rows, lanes), jnp.float32),
            pltpu.SemaphoreType.DMA((4,)),
        ],
        cost_estimate=pl.CostEstimate(
            flops=points * (20 * SWEEPS + 20) + species_e.size * 30,
            transcendentals=0,
            bytes_accessed=4 * (3 * points + species_e.size + inner * out_rows * lanes * (species + 1)),
        ),
    )(diffusivity, charge_num, field_e, perm_e, source_e, species_e)


def box(a, have, want):
    cut = have - want
    if cut == 0:
        return a
    return a[..., cut:a.shape[-3] - cut, cut:a.shape[-2] - cut, :]


def per_device(
    concentration,
    potential,
    permittivity,
    diffusivity,
    valence,
    charge_pos,
    charge_q,
    charge_tile,
    near_index,
    brick_mask,
):
    depth, height, width = potential.shape
    bands = lax.axis_size("narrow")
    rows_total = float(height * bands)
    tiles_all = float(TILES_DEV * bands)
    tile_rows = height // TILES_DEV
    slab = lax.axis_index("wide")
    band = lax.axis_index("narrow")
    index = near_index[0, 0]
    local_z = index // (height * width)
    local_y = index // width % height
    local_x = index % width
    global_z = slab * depth + local_z
    global_y = band * height + local_y
    node_z = global_z.astype(jnp.float32)
    node_y = global_y.astype(jnp.float32)
    node_x = local_x.astype(jnp.float32)
    node_tile = (global_y // tile_rows).astype(jnp.float32)
    slab_float = slab.astype(jnp.float32)
    deep = SWEEPS + 1
    wide_y = SWEEPS + 2
    charges = jnp.concatenate([charge_pos, charge_q, charge_tile.astype(jnp.float32)], axis=0)
    gathered = lax.all_gather(charges, "narrow", axis=1, tiled=True)
    gathered, potential, permittivity, concentration = lax.optimization_barrier(
        (gathered, potential, permittivity, concentration)
    )
    first = deep_halo(
        [(potential, deep, wide_y), (permittivity, deep, wide_y), (concentration, 1, wide_y)],
        "wide",
        "narrow",
    )
    values = pair_field(
        node_z,
        node_y,
        node_x,
        node_tile,
        gathered,
        slab_float,
        depth,
        rows_total,
        width,
        float(tile_rows),
        tiles_all,
    )
    values = values * brick_mask[0, 0].astype(jnp.float32)
    electrode = jnp.zeros((depth * height * width,), jnp.float32).at[index].add(values)
    electrode = electrode.reshape(depth, height, width)
    charge_num = valence.astype(jnp.float32)
    field = potential
    species = concentration
    perm_ext = first[1]
    for step in range(STEPS):
        source = jnp.sum(charge_num[:, None, None, None] * species, axis=0) + electrode
        if step == 0:
            field_e, species_e = first[0], first[2]
            (source_e,) = deep_halo([(source, deep, wide_y)], "wide", "narrow")
        else:
            field_e, source_e, species_e = deep_halo(
                [(field, deep, wide_y), (source, deep, wide_y), (species, 1, wide_y)], "wide", "narrow"
            )
        field, species = time_step(diffusivity, charge_num, field_e, perm_ext, source_e, species_e)
    return (species, field)


def solution(mesh):
    in_specs = (
        P(None, "wide", "narrow", None),
        P("wide", "narrow", None),
        P("wide", "narrow", None),
        P(),
        P(),
        P(None, ("wide", "narrow")),
        P(None, ("wide", "narrow")),
        P(None, ("wide", "narrow")),
        P("wide", "narrow", None),
        P("wide", "narrow"),
    )
    out_specs = (P(None, "wide", "narrow", None), P("wide", "narrow", None))
    return jax.shard_map(
        per_device, mesh=mesh, in_specs=in_specs, out_specs=out_specs, check_vma=False
    )
```

```python
import jax
import jax.numpy as jnp
from jax import lax
from jax.sharding import PartitionSpec as P
from jax.experimental import pallas as pl
from jax.experimental.pallas import tpu as pltpu

TILES_DEV = 4
STEPS = 2
SWEEPS = 6


def with_halo(cells, sides, width):
    for axis, dim in sides:
        count = lax.axis_size(axis)
        head = lax.slice_in_dim(cells, 0, width, axis=dim)
        tail = lax.slice_in_dim(cells, cells.shape[dim] - width, cells.shape[dim], axis=dim)
        cells = jnp.concatenate(
            [
                lax.ppermute(tail, axis, [(i, (i + 1) % count) for i in range(count)]),
                cells,
                lax.ppermute(head, axis, [((i + 1) % count, i) for i in range(count)]),
            ],
            axis=dim,
        )
    return cells


def relax(field_pad, perm_pad, source):
    centre = field_pad[1:-1, 1:-1]
    perm_centre = perm_pad[1:-1, 1:-1]
    numer = source
    denom = jnp.zeros_like(source)
    pairs = (
        (field_pad[2:, 1:-1], perm_pad[2:, 1:-1]),
        (field_pad[:-2, 1:-1], perm_pad[:-2, 1:-1]),
        (field_pad[1:-1, 2:], perm_pad[1:-1, 2:]),
        (field_pad[1:-1, :-2], perm_pad[1:-1, :-2]),
    )
    for other_field, other_perm in pairs:
        weight = 0.5 * (perm_centre + other_perm)
        numer = numer + weight * other_field
        denom = denom + weight
    zeros_edge = jnp.zeros_like(centre[..., :1])
    upper_field = jnp.concatenate([centre[..., 1:], zeros_edge], axis=-1)
    lower_field = jnp.concatenate([zeros_edge, centre[..., :-1]], axis=-1)
    upper_perm = jnp.concatenate([perm_centre[..., 1:], perm_centre[..., -1:]], axis=-1)
    lower_perm = jnp.concatenate([perm_centre[..., :1], perm_centre[..., :-1]], axis=-1)
    for other_field, other_perm in ((upper_field, upper_perm), (lower_field, lower_perm)):
        weight = 0.5 * (perm_centre + other_perm)
        numer = numer + weight * other_field
        denom = denom + weight
    return numer / denom


def transport(species_pad, field_pad, diffusivity, charge_num):
    centre = species_pad[:, 1:-1, 1:-1]
    field_centre = field_pad[1:-1, 1:-1]
    drift = charge_num[:, None, None, None]
    total = jnp.zeros_like(centre)
    pairs = (
        (species_pad[:, 2:, 1:-1], field_pad[2:, 1:-1]),
        (species_pad[:, :-2, 1:-1], field_pad[:-2, 1:-1]),
        (species_pad[:, 1:-1, 2:], field_pad[1:-1, 2:]),
        (species_pad[:, 1:-1, :-2], field_pad[1:-1, :-2]),
    )
    for other, other_field in pairs:
        total = (
            total + (centre - other) - drift * 0.5 * (centre + other) * (other_field - field_centre)
        )
    left = centre[..., :-1]
    right = centre[..., 1:]
    across = (
        left
        - right
        - drift * 0.5 * (left + right) * (field_centre[..., 1:] - field_centre[..., :-1])
    )
    zeros_edge = jnp.zeros_like(centre[..., :1])
    total = total + jnp.concatenate([across, zeros_edge], axis=-1)
    total = total - jnp.concatenate([zeros_edge, across], axis=-1)
    return centre - diffusivity[:, None, None, None] * total


def pair_field(
    node_z,
    node_y,
    node_x,
    node_tile,
    block,
    slab_float,
    depth,
    rows_total,
    width,
    tile_rows,
    tiles_all,
):
    charge_x = block[0] * width
    charge_y = (block[4] + block[1]) * tile_rows
    charge_z = (slab_float + block[2]) * depth
    strength = block[3]
    label = block[4]

    def one_block(nodes):
        pos_z, pos_y, pos_x, pos_tile = nodes
        offset_z = pos_z[:, None] - charge_z[None, :]
        offset_y = pos_y[:, None] - charge_y[None, :]
        offset_y = offset_y - rows_total * jnp.floor(offset_y / rows_total + 0.5)
        offset_x = pos_x[:, None] - charge_x[None, :]
        squared = offset_z * offset_z + offset_y * offset_y + offset_x * offset_x
        distance = jnp.sqrt(squared)
        tile_gap = jnp.abs(pos_tile[:, None] - label[None, :])
        adjacent = (tile_gap <= 1.0) | (tile_gap >= tiles_all - 1.0)
        term = strength[None, :] * jnp.exp(-distance / tile_rows) * lax.rsqrt(squared + 1.0)
        return jnp.sum(jnp.where(adjacent, term, 0.0), axis=1)

    half = node_z.shape[0] // 2
    parts = [one_block(tuple(arr[k * half:(k + 1) * half] for arr in (node_z, node_y, node_x, node_tile))) for k in range(2)]
    return jnp.concatenate(parts)


def ring(x, axis, shift):
    count = lax.axis_size(axis)
    return lax.ppermute(x, axis, [(i, (i + shift) % count) for i in range(count)])


def deep_halo(items, axis_z, axis_y):
    for back, axis, pick in ((3, axis_z, 1), (2, axis_y, 2)):
        tops, bots = [], []
        for item in items:
            a, w = item[0], item[pick]
            dim = a.ndim - back
            n = a.shape[dim]
            tops.append(lax.slice_in_dim(a, n - w, n, axis=dim))
            bots.append(lax.slice_in_dim(a, 0, w, axis=dim))
        minor = items[0][0].shape[-1]
        top = jnp.concatenate([t.reshape(-1, minor) for t in tops], axis=0)
        bot = jnp.concatenate([t.reshape(-1, minor) for t in bots], axis=0)
        below = ring(top, axis, 1)
        above = ring(bot, axis, -1)
        out, at = [], 0
        for item, t in zip(items, tops):
            a = item[0]
            size = t.size // minor
            lo = below[at:at + size].reshape(t.shape)
            hi = above[at:at + size].reshape(t.shape)
            at += size
            out.append((jnp.concatenate([lo, a, hi], axis=a.ndim - back),) + tuple(item[1:]))
        items = out
    return [item[0] for item in items]


def step_kernel(
    dif_ref, val_ref, f_hbm, p_hbm, s_hbm, c_hbm, fo_ref, co_ref, f_ref, p_ref, s_ref, c_ref, fa, fb, w_ref, sems
):
    copies = [
        pltpu.make_async_copy(src, dst, sems.at[k])
        for k, (src, dst) in enumerate(((p_hbm, p_ref), (f_hbm, f_ref), (s_hbm, s_ref), (c_hbm, c_ref)))
    ]
    for copy in copies:
        copy.start()
    planes, rows, lanes = f_ref.shape
    species, inner = c_ref.shape[0], c_ref.shape[1] - 2
    hz = (planes - inner) // 2
    hy = (rows - co_ref.shape[2]) // 2
    out_rows = co_ref.shape[2]
    lane = lax.broadcasted_iota(jnp.int32, (rows, lanes), 1)
    top = lane == lanes - 1
    bot = lane == 0

    def ysh(a, d):
        return pltpu.roll(a, (-d) % rows, 0)

    def xsh(a, d):
        return pltpu.roll(a, (-d) % lanes, 1)

    def weights(z, carry):
        pc = p_ref[z]
        ws = (
            0.5 * (pc + p_ref[z + 1]),
            0.5 * (pc + p_ref[z - 1]),
            0.5 * (pc + ysh(pc, 1)),
            0.5 * (pc + ysh(pc, -1)),
            0.5 * (pc + jnp.where(top, pc, xsh(pc, 1))),
            0.5 * (pc + jnp.where(bot, pc, xsh(pc, -1))),
        )
        den = jnp.zeros_like(pc)
        for w in ws:
            den = den + w
        inv = 1.0 / den
        for k in range(4):
            w_ref[k, z] = ws[k] * inv
        w_ref[4, z] = jnp.where(top, 0.0, ws[4]) * inv
        w_ref[5, z] = jnp.where(bot, 0.0, ws[5]) * inv
        w_ref[6, z] = s_ref[z] * inv
        return carry

    copies[0].wait()
    copies[2].wait()
    lax.fori_loop(1, planes - 1, weights, 0)
    copies[1].wait()
    bufs = (fa, fb)
    sweeps = hz - 1
    for k in range(sweeps):
        rd = f_ref if k == 0 else bufs[(k - 1) % 2]
        wr = bufs[k % 2]

        def sweep(z, carry, rd=rd, wr=wr):
            fc = rd[z]
            new = w_ref[6, z]
            new = new + w_ref[0, z] * rd[z + 1]
            new = new + w_ref[1, z] * rd[z - 1]
            new = new + w_ref[2, z] * ysh(fc, 1)
            new = new + w_ref[3, z] * ysh(fc, -1)
            new = new + w_ref[4, z] * xsh(fc, 1)
            new = new + w_ref[5, z] * xsh(fc, -1)
            wr[z] = new
            return carry

        lax.fori_loop(k + 1, planes - k - 1, sweep, 0)
    final = bufs[(sweeps - 1) % 2]
    copies[3].wait()

    def move(z, carry):
        zf = z + hz
        fc = final[zf]
        fo_ref[z] = fc[hy:hy + out_rows]
        pairs_field = (final[zf + 1], final[zf - 1], ysh(fc, 1), ysh(fc, -1))
        fr = xsh(fc, 1)
        for s in range(species):
            drift = val_ref[s]
            c = c_ref[s, z + 1]
            others = (c_ref[s, z + 2], c_ref[s, z], ysh(c, 1), ysh(c, -1))
            total = jnp.zeros_like(c)
            for other, other_field in zip(others, pairs_field):
                total = total + (c - other) - drift * 0.5 * (c + other) * (other_field - fc)
            right = xsh(c, 1)
            across = c - right - drift * 0.5 * (c + right) * (fr - fc)
            across = jnp.where(top, 0.0, across)
            total = total + across
            total = total - xsh(across, -1)
            new = c - dif_ref[s] * total
            co_ref[s, z] = new[hy:hy + out_rows]
        return carry

    lax.fori_loop(0, inner, move, 0)


def time_step(diffusivity, charge_num, field_e, perm_e, source_e, species_e):
    planes, rows, lanes = field_e.shape
    species, inner = species_e.shape[0], species_e.shape[1] - 2
    out_rows = rows - 2 * (SWEEPS + 2)
    smem = pl.BlockSpec(memory_space=pltpu.SMEM)
    vmem = pl.BlockSpec(memory_space=pltpu.VMEM)
    hbm = pl.BlockSpec(memory_space=pl.ANY)
    points = planes * rows * lanes
    return pl.pallas_call(
        step_kernel,
        out_shape=(
            jax.ShapeDtypeStruct((inner, out_rows, lanes), jnp.float32),
            jax.ShapeDtypeStruct((species, inner, out_rows, lanes), jnp.float32),
        ),
        in_specs=[smem, smem, hbm, hbm, hbm, hbm],
        out_specs=(vmem, vmem),
        scratch_shapes=[
            pltpu.VMEM((planes, rows, lanes), jnp.float32),
            pltpu.VMEM((planes, rows, lanes), jnp.float32),
            pltpu.VMEM((planes, rows, lanes), jnp.float32),
            pltpu.VMEM(species_e.shape, jnp.float32),
            pltpu.VMEM((planes, rows, lanes), jnp.float32),
            pltpu.VMEM((planes, rows, lanes), jnp.float32),
            pltpu.VMEM((7, planes, rows, lanes), jnp.float32),
            pltpu.SemaphoreType.DMA((4,)),
        ],
        cost_estimate=pl.CostEstimate(
            flops=points * (20 * SWEEPS + 20) + species_e.size * 30,
            transcendentals=0,
            bytes_accessed=4 * (3 * points + species_e.size + inner * out_rows * lanes * (species + 1)),
        ),
    )(diffusivity, charge_num, field_e, perm_e, source_e, species_e)


def box(a, have, want):
    cut = have - want
    if cut == 0:
        return a
    return a[..., cut:a.shape[-3] - cut, cut:a.shape[-2] - cut, :]


def per_device(
    concentration,
    potential,
    permittivity,
    diffusivity,
    valence,
    charge_pos,
    charge_q,
    charge_tile,
    near_index,
    brick_mask,
):
    depth, height, width = potential.shape
    bands = lax.axis_size("narrow")
    rows_total = float(height * bands)
    tiles_all = float(TILES_DEV * bands)
    tile_rows = height // TILES_DEV
    slab = lax.axis_index("wide")
    band = lax.axis_index("narrow")
    index = near_index[0, 0]
    local_z = index // (height * width)
    local_y = index // width % height
    local_x = index % width
    global_z = slab * depth + local_z
    global_y = band * height + local_y
    node_z = global_z.astype(jnp.float32)
    node_y = global_y.astype(jnp.float32)
    node_x = local_x.astype(jnp.float32)
    node_tile = (global_y // tile_rows).astype(jnp.float32)
    slab_float = slab.astype(jnp.float32)
    deep = SWEEPS + 1
    wide_y = SWEEPS + 2
    charges = jnp.concatenate([charge_pos, charge_q, charge_tile.astype(jnp.float32)], axis=0)
    gathered = lax.all_gather(charges, "narrow", axis=1, tiled=True)
    gathered, potential, permittivity, concentration = lax.optimization_barrier(
        (gathered, potential, permittivity, concentration)
    )
    first = deep_halo(
        [(potential, deep, wide_y), (permittivity, deep, wide_y), (concentration, 1, wide_y)],
        "wide",
        "narrow",
    )
    values = pair_field(
        node_z,
        node_y,
        node_x,
        node_tile,
        gathered,
        slab_float,
        depth,
        rows_total,
        width,
        float(tile_rows),
        tiles_all,
    )
    values = values * brick_mask[0, 0].astype(jnp.float32)
    electrode = jnp.zeros((depth * height * width,), jnp.float32).at[index].add(values)
    electrode = electrode.reshape(depth, height, width)
    charge_num = valence.astype(jnp.float32)
    field = potential
    species = concentration
    perm_ext = first[1]
    for step in range(STEPS):
        source = jnp.sum(charge_num[:, None, None, None] * species, axis=0) + electrode
        if step == 0:
            field_e, species_e = first[0], first[2]
            (source_e,) = deep_halo([(source, deep, wide_y)], "wide", "narrow")
        else:
            field_e, source_e, species_e = deep_halo(
                [(field, deep, wide_y), (source, deep, wide_y), (species, 1, wide_y)], "wide", "narrow"
            )
        field, species = time_step(diffusivity, charge_num, field_e, perm_ext, source_e, species_e)
    return (species, field)


def solution(mesh):
    in_specs = (
        P(None, "wide", "narrow", None),
        P("wide", "narrow", None),
        P("wide", "narrow", None),
        P(),
        P(),
        P(None, ("wide", "narrow")),
        P(None, ("wide", "narrow")),
        P(None, ("wide", "narrow")),
        P("wide", "narrow", None),
        P("wide", "narrow"),
    )
    out_specs = (P(None, "wide", "narrow", None), P("wide", "narrow", None))
    return jax.shard_map(
        per_device, mesh=mesh, in_specs=in_specs, out_specs=out_specs, check_vma=False
    )
```

```python
import jax
import jax.numpy as jnp
from jax import lax
from jax.sharding import PartitionSpec as P
from jax.experimental import pallas as pl
from jax.experimental.pallas import tpu as pltpu

TILES_DEV = 4
STEPS = 2
SWEEPS = 6


def with_halo(cells, sides, width):
    for axis, dim in sides:
        count = lax.axis_size(axis)
        head = lax.slice_in_dim(cells, 0, width, axis=dim)
        tail = lax.slice_in_dim(cells, cells.shape[dim] - width, cells.shape[dim], axis=dim)
        cells = jnp.concatenate(
            [
                lax.ppermute(tail, axis, [(i, (i + 1) % count) for i in range(count)]),
                cells,
                lax.ppermute(head, axis, [((i + 1) % count, i) for i in range(count)]),
            ],
            axis=dim,
        )
    return cells


def relax(field_pad, perm_pad, source):
    centre = field_pad[1:-1, 1:-1]
    perm_centre = perm_pad[1:-1, 1:-1]
    numer = source
    denom = jnp.zeros_like(source)
    pairs = (
        (field_pad[2:, 1:-1], perm_pad[2:, 1:-1]),
        (field_pad[:-2, 1:-1], perm_pad[:-2, 1:-1]),
        (field_pad[1:-1, 2:], perm_pad[1:-1, 2:]),
        (field_pad[1:-1, :-2], perm_pad[1:-1, :-2]),
    )
    for other_field, other_perm in pairs:
        weight = 0.5 * (perm_centre + other_perm)
        numer = numer + weight * other_field
        denom = denom + weight
    zeros_edge = jnp.zeros_like(centre[..., :1])
    upper_field = jnp.concatenate([centre[..., 1:], zeros_edge], axis=-1)
    lower_field = jnp.concatenate([zeros_edge, centre[..., :-1]], axis=-1)
    upper_perm = jnp.concatenate([perm_centre[..., 1:], perm_centre[..., -1:]], axis=-1)
    lower_perm = jnp.concatenate([perm_centre[..., :1], perm_centre[..., :-1]], axis=-1)
    for other_field, other_perm in ((upper_field, upper_perm), (lower_field, lower_perm)):
        weight = 0.5 * (perm_centre + other_perm)
        numer = numer + weight * other_field
        denom = denom + weight
    return numer / denom


def transport(species_pad, field_pad, diffusivity, charge_num):
    centre = species_pad[:, 1:-1, 1:-1]
    field_centre = field_pad[1:-1, 1:-1]
    drift = charge_num[:, None, None, None]
    total = jnp.zeros_like(centre)
    pairs = (
        (species_pad[:, 2:, 1:-1], field_pad[2:, 1:-1]),
        (species_pad[:, :-2, 1:-1], field_pad[:-2, 1:-1]),
        (species_pad[:, 1:-1, 2:], field_pad[1:-1, 2:]),
        (species_pad[:, 1:-1, :-2], field_pad[1:-1, :-2]),
    )
    for other, other_field in pairs:
        total = (
            total + (centre - other) - drift * 0.5 * (centre + other) * (other_field - field_centre)
        )
    left = centre[..., :-1]
    right = centre[..., 1:]
    across = (
        left
        - right
        - drift * 0.5 * (left + right) * (field_centre[..., 1:] - field_centre[..., :-1])
    )
    zeros_edge = jnp.zeros_like(centre[..., :1])
    total = total + jnp.concatenate([across, zeros_edge], axis=-1)
    total = total - jnp.concatenate([zeros_edge, across], axis=-1)
    return centre - diffusivity[:, None, None, None] * total


def pair_field(
    node_z,
    node_y,
    node_x,
    node_tile,
    block,
    slab_float,
    depth,
    rows_total,
    width,
    tile_rows,
    tiles_all,
):
    charge_x = block[0] * width
    charge_y = (block[4] + block[1]) * tile_rows
    charge_z = (slab_float + block[2]) * depth
    strength = block[3]
    label = block[4]

    def one_block(nodes):
        pos_z, pos_y, pos_x, pos_tile = nodes
        offset_z = pos_z[:, None] - charge_z[None, :]
        offset_y = pos_y[:, None] - charge_y[None, :]
        offset_y = offset_y - rows_total * jnp.floor(offset_y / rows_total + 0.5)
        offset_x = pos_x[:, None] - charge_x[None, :]
        squared = offset_z * offset_z + offset_y * offset_y + offset_x * offset_x
        distance = jnp.sqrt(squared)
        tile_gap = jnp.abs(pos_tile[:, None] - label[None, :])
        adjacent = (tile_gap <= 1.0) | (tile_gap >= tiles_all - 1.0)
        term = strength[None, :] * jnp.exp(-distance / tile_rows) * lax.rsqrt(squared + 1.0)
        return jnp.sum(jnp.where(adjacent, term, 0.0), axis=1)

    half = node_z.shape[0] // 2
    parts = [one_block(tuple(arr[k * half:(k + 1) * half] for arr in (node_z, node_y, node_x, node_tile))) for k in range(2)]
    return jnp.concatenate(parts)


def ring(x, axis, shift):
    count = lax.axis_size(axis)
    return lax.ppermute(x, axis, [(i, (i + shift) % count) for i in range(count)])


def deep_halo(items, axis_z, axis_y):
    for back, axis, pick in ((3, axis_z, 1), (2, axis_y, 2)):
        tops, bots = [], []
        for item in items:
            a, w = item[0], item[pick]
            dim = a.ndim - back
            n = a.shape[dim]
            tops.append(lax.slice_in_dim(a, n - w, n, axis=dim))
            bots.append(lax.slice_in_dim(a, 0, w, axis=dim))
        minor = items[0][0].shape[-1]
        top = jnp.concatenate([t.reshape(-1, minor) for t in tops], axis=0)
        bot = jnp.concatenate([t.reshape(-1, minor) for t in bots], axis=0)
        below = ring(top, axis, 1)
        above = ring(bot, axis, -1)
        out, at = [], 0
        for item, t in zip(items, tops):
            a = item[0]
            size = t.size // minor
            lo = below[at:at + size].reshape(t.shape)
            hi = above[at:at + size].reshape(t.shape)
            at += size
            out.append((jnp.concatenate([lo, a, hi], axis=a.ndim - back),) + tuple(item[1:]))
        items = out
    return [item[0] for item in items]


def step_kernel(
    dif_ref, val_ref, f_hbm, p_hbm, s_hbm, c_hbm, fo_ref, co_ref, f_ref, p_ref, s_ref, c_ref, fa, fb, w_ref, sems
):
    copies = [
        pltpu.make_async_copy(src, dst, sems.at[k])
        for k, (src, dst) in enumerate(
            ((p_hbm, p_ref), (f_hbm, f_ref.at[:, 8:88, :]), (s_hbm, s_ref), (c_hbm, c_ref))
        )
    ]
    for copy in copies:
        copy.start()
    planes, rows, lanes = p_ref.shape
    species, inner = c_ref.shape[0], c_ref.shape[1] - 2
    hz = (planes - inner) // 2
    hy = (rows - co_ref.shape[2]) // 2
    out_rows = co_ref.shape[2]
    lane = lax.broadcasted_iota(jnp.int32, (rows, lanes), 1)
    top = lane == lanes - 1
    bot = lane == 0

    def ysh(a, d):
        return pltpu.roll(a, (-d) % rows, 0)

    def xsh(a, d):
        return pltpu.roll(a, (-d) % lanes, 1)

    def weights(z, carry):
        pc = p_ref[z]
        ws = (
            0.5 * (pc + p_ref[z + 1]),
            0.5 * (pc + p_ref[z - 1]),
            0.5 * (pc + ysh(pc, 1)),
            0.5 * (pc + ysh(pc, -1)),
            0.5 * (pc + jnp.where(top, pc, xsh(pc, 1))),
            0.5 * (pc + jnp.where(bot, pc, xsh(pc, -1))),
        )
        den = jnp.zeros_like(pc)
        for w in ws:
            den = den + w
        inv = 1.0 / den
        for k in range(4):
            w_ref[k, z] = ws[k] * inv
        w_ref[4, z] = jnp.where(top, 0.0, ws[4]) * inv
        w_ref[5, z] = jnp.where(bot, 0.0, ws[5]) * inv
        w_ref[6, z] = s_ref[z] * inv
        return carry

    copies[0].wait()
    copies[2].wait()
    lax.fori_loop(1, planes - 1, weights, 0, unroll=2)
    copies[1].wait()
    pad = jnp.zeros((planes, 8, lanes), jnp.float32)
    for buf in (f_ref, fa, fb):
        buf[:, 0:8, :] = pad
        buf[:, 88:96, :] = pad
    bufs = (fa, fb)
    sweeps = hz - 1
    for k in range(sweeps):
        rd = f_ref if k == 0 else bufs[(k - 1) % 2]
        wr = bufs[k % 2]

        def sweep(z, carry, rd=rd, wr=wr):
            fc = rd[z, 8:88]
            near_z = (w_ref[6, z] + w_ref[0, z] * rd[z + 1, 8:88]) + w_ref[1, z] * rd[z - 1, 8:88]
            near_y = w_ref[2, z] * rd[z, pl.ds(9, rows)] + w_ref[3, z] * rd[z, pl.ds(7, rows)]
            near_x = w_ref[4, z] * xsh(fc, 1) + w_ref[5, z] * xsh(fc, -1)
            wr[z, 8:88] = near_z + (near_y + near_x)
            return carry

        lax.fori_loop(k + 1, planes - k - 1, sweep, 0, unroll=2)
    final = bufs[(sweeps - 1) % 2]
    copies[3].wait()

    def move(z, carry):
        zf = z + hz
        fc = final[zf, 8:88]
        fo_ref[z] = fc[hy:hy + out_rows]
        pairs_field = (final[zf + 1, 8:88], final[zf - 1, 8:88], ysh(fc, 1), ysh(fc, -1))
        fr = xsh(fc, 1)
        for s in range(species):
            drift = val_ref[s]
            c = c_ref[s, z + 1]
            others = (c_ref[s, z + 2], c_ref[s, z], ysh(c, 1), ysh(c, -1))
            total = jnp.zeros_like(c)
            for other, other_field in zip(others, pairs_field):
                total = total + (c - other) - drift * 0.5 * (c + other) * (other_field - fc)
            right = xsh(c, 1)
            across = c - right - drift * 0.5 * (c + right) * (fr - fc)
            across = jnp.where(top, 0.0, across)
            total = total + across
            total = total - xsh(across, -1)
            new = c - dif_ref[s] * total
            co_ref[s, z] = new[hy:hy + out_rows]
        return carry

    lax.fori_loop(0, inner, move, 0, unroll=2)


def time_step(diffusivity, charge_num, field_e, perm_e, source_e, species_e):
    planes, rows, lanes = field_e.shape
    species, inner = species_e.shape[0], species_e.shape[1] - 2
    out_rows = rows - 2 * (SWEEPS + 2)
    smem = pl.BlockSpec(memory_space=pltpu.SMEM)
    vmem = pl.BlockSpec(memory_space=pltpu.VMEM)
    hbm = pl.BlockSpec(memory_space=pl.ANY)
    points = planes * rows * lanes
    return pl.pallas_call(
        step_kernel,
        out_shape=(
            jax.ShapeDtypeStruct((inner, out_rows, lanes), jnp.float32),
            jax.ShapeDtypeStruct((species, inner, out_rows, lanes), jnp.float32),
        ),
        in_specs=[smem, smem, hbm, hbm, hbm, hbm],
        out_specs=(vmem, vmem),
        scratch_shapes=[
            pltpu.VMEM((planes, rows + 16, lanes), jnp.float32),
            pltpu.VMEM((planes, rows, lanes), jnp.float32),
            pltpu.VMEM((planes, rows, lanes), jnp.float32),
            pltpu.VMEM(species_e.shape, jnp.float32),
            pltpu.VMEM((planes, rows + 16, lanes), jnp.float32),
            pltpu.VMEM((planes, rows + 16, lanes), jnp.float32),
            pltpu.VMEM((7, planes, rows, lanes), jnp.float32),
            pltpu.SemaphoreType.DMA((4,)),
        ],
        cost_estimate=pl.CostEstimate(
            flops=points * (20 * SWEEPS + 20) + species_e.size * 30,
            transcendentals=0,
            bytes_accessed=4 * (3 * points + species_e.size + inner * out_rows * lanes * (species + 1)),
        ),
    )(diffusivity, charge_num, field_e, perm_e, source_e, species_e)


def box(a, have, want):
    cut = have - want
    if cut == 0:
        return a
    return a[..., cut:a.shape[-3] - cut, cut:a.shape[-2] - cut, :]


def per_device(
    concentration,
    potential,
    permittivity,
    diffusivity,
    valence,
    charge_pos,
    charge_q,
    charge_tile,
    near_index,
    brick_mask,
):
    depth, height, width = potential.shape
    bands = lax.axis_size("narrow")
    rows_total = float(height * bands)
    tiles_all = float(TILES_DEV * bands)
    tile_rows = height // TILES_DEV
    slab = lax.axis_index("wide")
    band = lax.axis_index("narrow")
    index = near_index[0, 0]
    local_z = index // (height * width)
    local_y = index // width % height
    local_x = index % width
    global_z = slab * depth + local_z
    global_y = band * height + local_y
    node_z = global_z.astype(jnp.float32)
    node_y = global_y.astype(jnp.float32)
    node_x = local_x.astype(jnp.float32)
    node_tile = (global_y // tile_rows).astype(jnp.float32)
    slab_float = slab.astype(jnp.float32)
    deep = SWEEPS + 1
    wide_y = SWEEPS + 2
    charges = jnp.concatenate([charge_pos, charge_q, charge_tile.astype(jnp.float32)], axis=0)
    gathered = lax.all_gather(charges, "narrow", axis=1, tiled=True)
    gathered, potential, permittivity, concentration = lax.optimization_barrier(
        (gathered, potential, permittivity, concentration)
    )
    first = deep_halo(
        [(potential, deep, wide_y), (permittivity, deep, wide_y), (concentration, 1, wide_y)],
        "wide",
        "narrow",
    )
    values = pair_field(
        node_z,
        node_y,
        node_x,
        node_tile,
        gathered,
        slab_float,
        depth,
        rows_total,
        width,
        float(tile_rows),
        tiles_all,
    )
    values = values * brick_mask[0, 0].astype(jnp.float32)
    electrode = jnp.zeros((depth * height * width,), jnp.float32).at[index].add(values)
    electrode = electrode.reshape(depth, height, width)
    charge_num = valence.astype(jnp.float32)
    field = potential
    species = concentration
    perm_ext = first[1]
    for step in range(STEPS):
        source = jnp.sum(charge_num[:, None, None, None] * species, axis=0) + electrode
        if step == 0:
            field_e, species_e = first[0], first[2]
            (source_e,) = deep_halo([(source, deep, wide_y)], "wide", "narrow")
        else:
            field_e, source_e, species_e = deep_halo(
                [(field, deep, wide_y), (source, deep, wide_y), (species, 1, wide_y)], "wide", "narrow"
            )
        field, species = time_step(diffusivity, charge_num, field_e, perm_ext, source_e, species_e)
    return (species, field)


def solution(mesh):
    in_specs = (
        P(None, "wide", "narrow", None),
        P("wide", "narrow", None),
        P("wide", "narrow", None),
        P(),
        P(),
        P(None, ("wide", "narrow")),
        P(None, ("wide", "narrow")),
        P(None, ("wide", "narrow")),
        P("wide", "narrow", None),
        P("wide", "narrow"),
    )
    out_specs = (P(None, "wide", "narrow", None), P("wide", "narrow", None))
    return jax.shard_map(
        per_device, mesh=mesh, in_specs=in_specs, out_specs=out_specs, check_vma=False
    )
```

```python
import jax
import jax.numpy as jnp
from jax import lax
from jax.sharding import PartitionSpec as P
from jax.experimental import pallas as pl
from jax.experimental.pallas import tpu as pltpu

TILES_DEV = 4
STEPS = 2
SWEEPS = 6


def with_halo(cells, sides, width):
    for axis, dim in sides:
        count = lax.axis_size(axis)
        head = lax.slice_in_dim(cells, 0, width, axis=dim)
        tail = lax.slice_in_dim(cells, cells.shape[dim] - width, cells.shape[dim], axis=dim)
        cells = jnp.concatenate(
            [
                lax.ppermute(tail, axis, [(i, (i + 1) % count) for i in range(count)]),
                cells,
                lax.ppermute(head, axis, [((i + 1) % count, i) for i in range(count)]),
            ],
            axis=dim,
        )
    return cells


def relax(field_pad, perm_pad, source):
    centre = field_pad[1:-1, 1:-1]
    perm_centre = perm_pad[1:-1, 1:-1]
    numer = source
    denom = jnp.zeros_like(source)
    pairs = (
        (field_pad[2:, 1:-1], perm_pad[2:, 1:-1]),
        (field_pad[:-2, 1:-1], perm_pad[:-2, 1:-1]),
        (field_pad[1:-1, 2:], perm_pad[1:-1, 2:]),
        (field_pad[1:-1, :-2], perm_pad[1:-1, :-2]),
    )
    for other_field, other_perm in pairs:
        weight = 0.5 * (perm_centre + other_perm)
        numer = numer + weight * other_field
        denom = denom + weight
    zeros_edge = jnp.zeros_like(centre[..., :1])
    upper_field = jnp.concatenate([centre[..., 1:], zeros_edge], axis=-1)
    lower_field = jnp.concatenate([zeros_edge, centre[..., :-1]], axis=-1)
    upper_perm = jnp.concatenate([perm_centre[..., 1:], perm_centre[..., -1:]], axis=-1)
    lower_perm = jnp.concatenate([perm_centre[..., :1], perm_centre[..., :-1]], axis=-1)
    for other_field, other_perm in ((upper_field, upper_perm), (lower_field, lower_perm)):
        weight = 0.5 * (perm_centre + other_perm)
        numer = numer + weight * other_field
        denom = denom + weight
    return numer / denom


def transport(species_pad, field_pad, diffusivity, charge_num):
    centre = species_pad[:, 1:-1, 1:-1]
    field_centre = field_pad[1:-1, 1:-1]
    drift = charge_num[:, None, None, None]
    total = jnp.zeros_like(centre)
    pairs = (
        (species_pad[:, 2:, 1:-1], field_pad[2:, 1:-1]),
        (species_pad[:, :-2, 1:-1], field_pad[:-2, 1:-1]),
        (species_pad[:, 1:-1, 2:], field_pad[1:-1, 2:]),
        (species_pad[:, 1:-1, :-2], field_pad[1:-1, :-2]),
    )
    for other, other_field in pairs:
        total = (
            total + (centre - other) - drift * 0.5 * (centre + other) * (other_field - field_centre)
        )
    left = centre[..., :-1]
    right = centre[..., 1:]
    across = (
        left
        - right
        - drift * 0.5 * (left + right) * (field_centre[..., 1:] - field_centre[..., :-1])
    )
    zeros_edge = jnp.zeros_like(centre[..., :1])
    total = total + jnp.concatenate([across, zeros_edge], axis=-1)
    total = total - jnp.concatenate([zeros_edge, across], axis=-1)
    return centre - diffusivity[:, None, None, None] * total


def pair_field(
    node_z,
    node_y,
    node_x,
    node_tile,
    block,
    slab_float,
    depth,
    rows_total,
    width,
    tile_rows,
    tiles_all,
):
    charge_x = block[0] * width
    charge_y = (block[4] + block[1]) * tile_rows
    charge_z = (slab_float + block[2]) * depth
    strength = block[3]
    label = block[4]

    def one_block(nodes):
        pos_z, pos_y, pos_x, pos_tile = nodes
        offset_z = pos_z[:, None] - charge_z[None, :]
        offset_y = pos_y[:, None] - charge_y[None, :]
        offset_y = offset_y - rows_total * jnp.floor(offset_y / rows_total + 0.5)
        offset_x = pos_x[:, None] - charge_x[None, :]
        squared = offset_z * offset_z + offset_y * offset_y + offset_x * offset_x
        distance = jnp.sqrt(squared)
        tile_gap = jnp.abs(pos_tile[:, None] - label[None, :])
        adjacent = (tile_gap <= 1.0) | (tile_gap >= tiles_all - 1.0)
        term = strength[None, :] * jnp.exp(-distance / tile_rows) * lax.rsqrt(squared + 1.0)
        return jnp.sum(jnp.where(adjacent, term, 0.0), axis=1)

    half = node_z.shape[0] // 2
    parts = [one_block(tuple(arr[k * half:(k + 1) * half] for arr in (node_z, node_y, node_x, node_tile))) for k in range(2)]
    return jnp.concatenate(parts)


def ring(x, axis, shift):
    count = lax.axis_size(axis)
    return lax.ppermute(x, axis, [(i, (i + shift) % count) for i in range(count)])


def deep_halo(items, axis_z, axis_y):
    for back, axis, pick in ((3, axis_z, 1), (2, axis_y, 2)):
        tops, bots = [], []
        for item in items:
            a, w = item[0], item[pick]
            dim = a.ndim - back
            n = a.shape[dim]
            tops.append(lax.slice_in_dim(a, n - w, n, axis=dim))
            bots.append(lax.slice_in_dim(a, 0, w, axis=dim))
        minor = items[0][0].shape[-1]
        top = jnp.concatenate([t.reshape(-1, minor) for t in tops], axis=0)
        bot = jnp.concatenate([t.reshape(-1, minor) for t in bots], axis=0)
        below = ring(top, axis, 1)
        above = ring(bot, axis, -1)
        out, at = [], 0
        for item, t in zip(items, tops):
            a = item[0]
            size = t.size // minor
            lo = below[at:at + size].reshape(t.shape)
            hi = above[at:at + size].reshape(t.shape)
            at += size
            out.append((jnp.concatenate([lo, a, hi], axis=a.ndim - back),) + tuple(item[1:]))
        items = out
    return [item[0] for item in items]


def step_kernel(
    dif_ref, val_ref, f_hbm, p_hbm, s_hbm, c_hbm, fo_ref, co_ref, f_ref, p_ref, s_ref, c_ref, fa, fb, w_ref, sems
):
    copies = [
        pltpu.make_async_copy(src, dst, sems.at[k])
        for k, (src, dst) in enumerate(
            ((p_hbm, p_ref), (f_hbm, f_ref.at[:, 8:88, :]), (s_hbm, s_ref), (c_hbm, c_ref))
        )
    ]
    for copy in copies:
        copy.start()
    planes, rows, lanes = p_ref.shape
    species, inner = c_ref.shape[0], c_ref.shape[1] - 2
    hz = (planes - inner) // 2
    hy = (rows - co_ref.shape[2]) // 2
    out_rows = co_ref.shape[2]
    lane = lax.broadcasted_iota(jnp.int32, (rows, lanes), 1)
    top = lane == lanes - 1
    bot = lane == 0

    def ysh(a, d):
        return pltpu.roll(a, (-d) % rows, 0)

    def xsh(a, d):
        return pltpu.roll(a, (-d) % lanes, 1)

    def weights(z, carry):
        pc = p_ref[z]
        ws = (
            0.5 * (pc + p_ref[z + 1]),
            0.5 * (pc + p_ref[z - 1]),
            0.5 * (pc + ysh(pc, 1)),
            0.5 * (pc + ysh(pc, -1)),
            0.5 * (pc + jnp.where(top, pc, xsh(pc, 1))),
            0.5 * (pc + jnp.where(bot, pc, xsh(pc, -1))),
        )
        den = jnp.zeros_like(pc)
        for w in ws:
            den = den + w
        inv = 1.0 / den
        for k in range(4):
            w_ref[k, z] = ws[k] * inv
        w_ref[4, z] = jnp.where(top, 0.0, ws[4]) * inv
        w_ref[5, z] = jnp.where(bot, 0.0, ws[5]) * inv
        w_ref[6, z] = s_ref[z - 1] * inv
        return carry

    copies[0].wait()
    copies[2].wait()
    lax.fori_loop(1, planes - 1, weights, 0, unroll=2)
    copies[1].wait()
    pad = jnp.zeros((planes, 8, lanes), jnp.float32)
    for buf in (f_ref, fa, fb):
        buf[:, 0:8, :] = pad
        buf[:, 88:96, :] = pad
    bufs = (fa, fb)
    sweeps = hz - 1
    for k in range(sweeps):
        rd = f_ref if k == 0 else bufs[(k - 1) % 2]
        wr = bufs[k % 2]

        def sweep(z, carry, rd=rd, wr=wr):
            fc = rd[z, 8:88]
            near_z = (w_ref[6, z] + w_ref[0, z] * rd[z + 1, 8:88]) + w_ref[1, z] * rd[z - 1, 8:88]
            near_y = w_ref[2, z] * rd[z, pl.ds(9, rows)] + w_ref[3, z] * rd[z, pl.ds(7, rows)]
            near_x = w_ref[4, z] * xsh(fc, 1) + w_ref[5, z] * xsh(fc, -1)
            wr[z, 8:88] = near_z + (near_y + near_x)
            return carry

        lax.fori_loop(k + 1, planes - k - 1, sweep, 0, unroll=2)
    final = bufs[(sweeps - 1) % 2]
    copies[3].wait()

    def move(z, carry):
        zf = z + hz
        fc = final[zf, 8:88]
        fo_ref[z] = fc[hy:hy + out_rows]
        pairs_field = (final[zf + 1, 8:88], final[zf - 1, 8:88], ysh(fc, 1), ysh(fc, -1))
        fr = xsh(fc, 1)
        for s in range(species):
            drift = val_ref[s]
            c = c_ref[s, z + 1]
            others = (c_ref[s, z + 2], c_ref[s, z], ysh(c, 1), ysh(c, -1))
            total = jnp.zeros_like(c)
            for other, other_field in zip(others, pairs_field):
                total = total + (c - other) - drift * 0.5 * (c + other) * (other_field - fc)
            right = xsh(c, 1)
            across = c - right - drift * 0.5 * (c + right) * (fr - fc)
            across = jnp.where(top, 0.0, across)
            total = total + across
            total = total - xsh(across, -1)
            new = c - dif_ref[s] * total
            co_ref[s, z] = new[hy:hy + out_rows]
        return carry

    lax.fori_loop(0, inner, move, 0, unroll=2)


def time_step(diffusivity, charge_num, field_e, perm_e, source_e, species_e):
    planes, rows, lanes = field_e.shape
    species, inner = species_e.shape[0], species_e.shape[1] - 2
    out_rows = rows - 2 * (SWEEPS + 2)
    smem = pl.BlockSpec(memory_space=pltpu.SMEM)
    vmem = pl.BlockSpec(memory_space=pltpu.VMEM)
    hbm = pl.BlockSpec(memory_space=pl.ANY)
    points = planes * rows * lanes
    return pl.pallas_call(
        step_kernel,
        out_shape=(
            jax.ShapeDtypeStruct((inner, out_rows, lanes), jnp.float32),
            jax.ShapeDtypeStruct((species, inner, out_rows, lanes), jnp.float32),
        ),
        in_specs=[smem, smem, hbm, hbm, hbm, hbm],
        out_specs=(vmem, vmem),
        scratch_shapes=[
            pltpu.VMEM((planes, rows + 16, lanes), jnp.float32),
            pltpu.VMEM((planes, rows, lanes), jnp.float32),
            pltpu.VMEM(source_e.shape, jnp.float32),
            pltpu.VMEM(species_e.shape, jnp.float32),
            pltpu.VMEM((planes, rows + 16, lanes), jnp.float32),
            pltpu.VMEM((planes, rows + 16, lanes), jnp.float32),
            pltpu.VMEM((7, planes, rows, lanes), jnp.float32),
            pltpu.SemaphoreType.DMA((4,)),
        ],
        cost_estimate=pl.CostEstimate(
            flops=points * (20 * SWEEPS + 20) + species_e.size * 30,
            transcendentals=0,
            bytes_accessed=4 * (3 * points + species_e.size + inner * out_rows * lanes * (species + 1)),
        ),
    )(diffusivity, charge_num, field_e, perm_e, source_e, species_e)


def box(a, have, want):
    cut = have - want
    if cut == 0:
        return a
    return a[..., cut:a.shape[-3] - cut, cut:a.shape[-2] - cut, :]


def per_device(
    concentration,
    potential,
    permittivity,
    diffusivity,
    valence,
    charge_pos,
    charge_q,
    charge_tile,
    near_index,
    brick_mask,
):
    depth, height, width = potential.shape
    bands = lax.axis_size("narrow")
    rows_total = float(height * bands)
    tiles_all = float(TILES_DEV * bands)
    tile_rows = height // TILES_DEV
    slab = lax.axis_index("wide")
    band = lax.axis_index("narrow")
    index = near_index[0, 0]
    local_z = index // (height * width)
    local_y = index // width % height
    local_x = index % width
    global_z = slab * depth + local_z
    global_y = band * height + local_y
    node_z = global_z.astype(jnp.float32)
    node_y = global_y.astype(jnp.float32)
    node_x = local_x.astype(jnp.float32)
    node_tile = (global_y // tile_rows).astype(jnp.float32)
    slab_float = slab.astype(jnp.float32)
    deep = SWEEPS + 1
    wide_y = SWEEPS + 2
    charges = jnp.concatenate([charge_pos, charge_q, charge_tile.astype(jnp.float32)], axis=0)
    gathered = lax.all_gather(charges, "narrow", axis=1, tiled=True)
    gathered, potential, permittivity, concentration = lax.optimization_barrier(
        (gathered, potential, permittivity, concentration)
    )
    first = deep_halo(
        [(potential, deep, wide_y), (permittivity, deep, wide_y), (concentration, 1, wide_y)],
        "wide",
        "narrow",
    )
    values = pair_field(
        node_z,
        node_y,
        node_x,
        node_tile,
        gathered,
        slab_float,
        depth,
        rows_total,
        width,
        float(tile_rows),
        tiles_all,
    )
    values = values * brick_mask[0, 0].astype(jnp.float32)
    electrode = jnp.zeros((depth * height * width,), jnp.float32).at[index].add(values)
    electrode = electrode.reshape(depth, height, width)
    charge_num = valence.astype(jnp.float32)
    field = potential
    species = concentration
    perm_ext = first[1]
    for step in range(STEPS):
        source = jnp.sum(charge_num[:, None, None, None] * species, axis=0) + electrode
        if step == 0:
            field_e, species_e = first[0], first[2]
            (source_e,) = deep_halo([(source, deep - 1, wide_y)], "wide", "narrow")
        else:
            field_e, source_e, species_e = deep_halo(
                [(field, deep, wide_y), (source, deep - 1, wide_y), (species, 1, wide_y)], "wide", "narrow"
            )
        field, species = time_step(diffusivity, charge_num, field_e, perm_ext, source_e, species_e)
    return (species, field)


def solution(mesh):
    in_specs = (
        P(None, "wide", "narrow", None),
        P("wide", "narrow", None),
        P("wide", "narrow", None),
        P(),
        P(),
        P(None, ("wide", "narrow")),
        P(None, ("wide", "narrow")),
        P(None, ("wide", "narrow")),
        P("wide", "narrow", None),
        P("wide", "narrow"),
    )
    out_specs = (P(None, "wide", "narrow", None), P("wide", "narrow", None))
    return jax.shard_map(
        per_device, mesh=mesh, in_specs=in_specs, out_specs=out_specs, check_vma=False
    )
```

```python
import functools

import jax
import jax.numpy as jnp
from jax import lax
from jax.sharding import PartitionSpec as P
from jax.experimental import pallas as pl
from jax.experimental.pallas import tpu as pltpu

TILES_DEV = 4
STEPS = 2
SWEEPS = 6


def with_halo(cells, sides, width):
    for axis, dim in sides:
        count = lax.axis_size(axis)
        head = lax.slice_in_dim(cells, 0, width, axis=dim)
        tail = lax.slice_in_dim(cells, cells.shape[dim] - width, cells.shape[dim], axis=dim)
        cells = jnp.concatenate(
            [
                lax.ppermute(tail, axis, [(i, (i + 1) % count) for i in range(count)]),
                cells,
                lax.ppermute(head, axis, [((i + 1) % count, i) for i in range(count)]),
            ],
            axis=dim,
        )
    return cells


def relax(field_pad, perm_pad, source):
    centre = field_pad[1:-1, 1:-1]
    perm_centre = perm_pad[1:-1, 1:-1]
    numer = source
    denom = jnp.zeros_like(source)
    pairs = (
        (field_pad[2:, 1:-1], perm_pad[2:, 1:-1]),
        (field_pad[:-2, 1:-1], perm_pad[:-2, 1:-1]),
        (field_pad[1:-1, 2:], perm_pad[1:-1, 2:]),
        (field_pad[1:-1, :-2], perm_pad[1:-1, :-2]),
    )
    for other_field, other_perm in pairs:
        weight = 0.5 * (perm_centre + other_perm)
        numer = numer + weight * other_field
        denom = denom + weight
    zeros_edge = jnp.zeros_like(centre[..., :1])
    upper_field = jnp.concatenate([centre[..., 1:], zeros_edge], axis=-1)
    lower_field = jnp.concatenate([zeros_edge, centre[..., :-1]], axis=-1)
    upper_perm = jnp.concatenate([perm_centre[..., 1:], perm_centre[..., -1:]], axis=-1)
    lower_perm = jnp.concatenate([perm_centre[..., :1], perm_centre[..., :-1]], axis=-1)
    for other_field, other_perm in ((upper_field, upper_perm), (lower_field, lower_perm)):
        weight = 0.5 * (perm_centre + other_perm)
        numer = numer + weight * other_field
        denom = denom + weight
    return numer / denom


def transport(species_pad, field_pad, diffusivity, charge_num):
    centre = species_pad[:, 1:-1, 1:-1]
    field_centre = field_pad[1:-1, 1:-1]
    drift = charge_num[:, None, None, None]
    total = jnp.zeros_like(centre)
    pairs = (
        (species_pad[:, 2:, 1:-1], field_pad[2:, 1:-1]),
        (species_pad[:, :-2, 1:-1], field_pad[:-2, 1:-1]),
        (species_pad[:, 1:-1, 2:], field_pad[1:-1, 2:]),
        (species_pad[:, 1:-1, :-2], field_pad[1:-1, :-2]),
    )
    for other, other_field in pairs:
        total = (
            total + (centre - other) - drift * 0.5 * (centre + other) * (other_field - field_centre)
        )
    left = centre[..., :-1]
    right = centre[..., 1:]
    across = (
        left
        - right
        - drift * 0.5 * (left + right) * (field_centre[..., 1:] - field_centre[..., :-1])
    )
    zeros_edge = jnp.zeros_like(centre[..., :1])
    total = total + jnp.concatenate([across, zeros_edge], axis=-1)
    total = total - jnp.concatenate([zeros_edge, across], axis=-1)
    return centre - diffusivity[:, None, None, None] * total


def pair_field(
    node_z,
    node_y,
    node_x,
    node_tile,
    block,
    slab_float,
    depth,
    rows_total,
    width,
    tile_rows,
    tiles_all,
):
    charge_x = block[0] * width
    charge_y = (block[4] + block[1]) * tile_rows
    charge_z = (slab_float + block[2]) * depth
    strength = block[3]
    label = block[4]

    def one_block(nodes):
        pos_z, pos_y, pos_x, pos_tile = nodes
        offset_z = pos_z[:, None] - charge_z[None, :]
        offset_y = pos_y[:, None] - charge_y[None, :]
        offset_y = offset_y - rows_total * jnp.floor(offset_y / rows_total + 0.5)
        offset_x = pos_x[:, None] - charge_x[None, :]
        squared = offset_z * offset_z + offset_y * offset_y + offset_x * offset_x
        distance = jnp.sqrt(squared)
        tile_gap = jnp.abs(pos_tile[:, None] - label[None, :])
        adjacent = (tile_gap <= 1.0) | (tile_gap >= tiles_all - 1.0)
        term = strength[None, :] * jnp.exp(-distance / tile_rows) * lax.rsqrt(squared + 1.0)
        return jnp.sum(jnp.where(adjacent, term, 0.0), axis=1)

    half = node_z.shape[0] // 2
    parts = [one_block(tuple(arr[k * half:(k + 1) * half] for arr in (node_z, node_y, node_x, node_tile))) for k in range(2)]
    return jnp.concatenate(parts)


def ring(x, axis, shift):
    count = lax.axis_size(axis)
    return lax.ppermute(x, axis, [(i, (i + shift) % count) for i in range(count)])


def deep_halo(items, axis_z, axis_y):
    minor = items[0][0].shape[-1]
    rows = items[0][0].shape[-2]
    tops, bots = [], []
    for a, wz, _ in items:
        dim = a.ndim - 3
        n = a.shape[dim]
        tops.append(lax.slice_in_dim(a, n - wz, n, axis=dim))
        bots.append(lax.slice_in_dim(a, 0, wz, axis=dim))
    z_lo = ring(jnp.concatenate([t.reshape(-1, minor) for t in tops], axis=0), axis_z, 1)
    z_hi = ring(jnp.concatenate([t.reshape(-1, minor) for t in bots], axis=0), axis_z, -1)
    y_tops, y_bots, z_offs, at = [], [], [], 0
    for (a, wz, wy), t in zip(items, tops):
        size = t.size // minor
        z_offs.append(at // rows)
        ext = jnp.concatenate(
            [z_lo[at:at + size].reshape(t.shape), a, z_hi[at:at + size].reshape(t.shape)], axis=a.ndim - 3
        )
        at += size
        y_tops.append(ext[..., rows - wy:rows, :])
        y_bots.append(ext[..., 0:wy, :])
    wy = items[0][2]
    y_lo = ring(jnp.concatenate([t.reshape(-1, minor) for t in y_tops], axis=0), axis_y, 1)
    y_hi = ring(jnp.concatenate([t.reshape(-1, minor) for t in y_bots], axis=0), axis_y, -1)
    y_offs, at = [], 0
    for t in y_tops:
        y_offs.append(at // wy)
        at += t.size // minor
    bufs = (
        z_lo.reshape(-1, rows, minor),
        z_hi.reshape(-1, rows, minor),
        y_lo.reshape(-1, wy, minor),
        y_hi.reshape(-1, wy, minor),
    )
    return [(a,) + bufs + (zo, yo, wz) for (a, wz, _), zo, yo in zip(items, z_offs, y_offs)]


def step_kernel(plan, dif_ref, val_ref, *refs):
    hbm = refs[:20]
    fo_ref, co_ref, f_ref, p_ref, s_ref, c_ref, fa, fb, w_ref, sems = refs[20:]
    targets = (f_ref, p_ref, s_ref, c_ref)
    copies = [[] for _ in targets]
    count = 0
    for k, (lead, z_off, y_off, wz, r0) in enumerate(plan):
        inner_ref, z_lo, z_hi, y_lo, y_hi = hbm[5 * k:5 * k + 5]
        target = targets[k]
        span = 2 * wz + inner_ref.shape[-3]
        mid = slice(r0 + 8, r0 + 8 + inner_ref.shape[-2])
        moves = [(inner_ref, target.at[..., wz:span - wz, mid, :])]
        for s in range(lead):
            part = target.at[s] if lead > 1 or target.ndim == 4 else target
            zs = slice(z_off + s * wz, z_off + (s + 1) * wz)
            ys = slice(y_off + s * span, y_off + (s + 1) * span)
            moves += [
                (z_lo.at[zs], part.at[0:wz, mid, :]),
                (z_hi.at[zs], part.at[span - wz:span, mid, :]),
                (y_lo.at[ys], part.at[:, r0:r0 + 8, :]),
                (y_hi.at[ys], part.at[:, mid.stop:mid.stop + 8, :]),
            ]
        for src, dst in moves:
            copy = pltpu.make_async_copy(src, dst, sems.at[count])
            copy.start()
            copies[k].append(copy)
            count += 1

    def wait(k):
        for copy in copies[k]:
            copy.wait()

    planes, rows, lanes = p_ref.shape
    species, inner = c_ref.shape[0], c_ref.shape[1] - 2
    hz = (planes - inner) // 2
    hy = (rows - co_ref.shape[2]) // 2
    out_rows = co_ref.shape[2]
    lane = lax.broadcasted_iota(jnp.int32, (rows, lanes), 1)
    top = lane == lanes - 1
    bot = lane == 0

    def ysh(a, d):
        return pltpu.roll(a, (-d) % rows, 0)

    def xsh(a, d):
        return pltpu.roll(a, (-d) % lanes, 1)

    def weights(z, carry):
        pc = p_ref[z]
        ws = (
            0.5 * (pc + p_ref[z + 1]),
            0.5 * (pc + p_ref[z - 1]),
            0.5 * (pc + ysh(pc, 1)),
            0.5 * (pc + ysh(pc, -1)),
            0.5 * (pc + jnp.where(top, pc, xsh(pc, 1))),
            0.5 * (pc + jnp.where(bot, pc, xsh(pc, -1))),
        )
        den = jnp.zeros_like(pc)
        for w in ws:
            den = den + w
        inv = 1.0 / den
        for k in range(4):
            w_ref[k, z] = ws[k] * inv
        w_ref[4, z] = jnp.where(top, 0.0, ws[4]) * inv
        w_ref[5, z] = jnp.where(bot, 0.0, ws[5]) * inv
        w_ref[6, z] = s_ref[z - 1] * inv
        return carry

    wait(1)
    wait(2)
    lax.fori_loop(1, planes - 1, weights, 0, unroll=2)
    wait(0)
    pad = jnp.zeros((planes, 8, lanes), jnp.float32)
    for buf in (f_ref, fa, fb):
        buf[:, 0:8, :] = pad
        buf[:, 88:96, :] = pad
    bufs = (fa, fb)
    sweeps = hz - 1
    for k in range(sweeps):
        rd = f_ref if k == 0 else bufs[(k - 1) % 2]
        wr = bufs[k % 2]

        def sweep(z, carry, rd=rd, wr=wr):
            fc = rd[z, 8:88]
            near_z = (w_ref[6, z] + w_ref[0, z] * rd[z + 1, 8:88]) + w_ref[1, z] * rd[z - 1, 8:88]
            near_y = w_ref[2, z] * rd[z, pl.ds(9, rows)] + w_ref[3, z] * rd[z, pl.ds(7, rows)]
            near_x = w_ref[4, z] * xsh(fc, 1) + w_ref[5, z] * xsh(fc, -1)
            wr[z, 8:88] = near_z + (near_y + near_x)
            return carry

        lax.fori_loop(k + 1, planes - k - 1, sweep, 0, unroll=2)
    final = bufs[(sweeps - 1) % 2]
    wait(3)

    def move(z, carry):
        zf = z + hz
        fc = final[zf, 8:88]
        fo_ref[z] = fc[hy:hy + out_rows]
        pairs_field = (final[zf + 1, 8:88], final[zf - 1, 8:88], ysh(fc, 1), ysh(fc, -1))
        fr = xsh(fc, 1)
        for s in range(species):
            drift = val_ref[s]
            c = c_ref[s, z + 1]
            others = (c_ref[s, z + 2], c_ref[s, z], ysh(c, 1), ysh(c, -1))
            total = jnp.zeros_like(c)
            for other, other_field in zip(others, pairs_field):
                total = total + (c - other) - drift * 0.5 * (c + other) * (other_field - fc)
            right = xsh(c, 1)
            across = c - right - drift * 0.5 * (c + right) * (fr - fc)
            across = jnp.where(top, 0.0, across)
            total = total + across
            total = total - xsh(across, -1)
            new = c - dif_ref[s] * total
            co_ref[s, z] = new[hy:hy + out_rows]
        return carry

    lax.fori_loop(0, inner, move, 0, unroll=2)


def time_step(diffusivity, charge_num, field_p, perm_p, source_p, species_p):
    species, inner, out_rows, lanes = species_p[0].shape
    planes = inner + 2 * field_p[7]
    rows = out_rows + 2 * (SWEEPS + 2)
    plan, operands, boxes = [], [], []
    for pieces, r0 in ((field_p, 8), (perm_p, 0), (source_p, 0), (species_p, 0)):
        inner_arr, z_lo, z_hi, y_lo, y_hi, z_off, y_off, wz = pieces
        lead = inner_arr.shape[0] if inner_arr.ndim == 4 else 1
        plan.append((lead, z_off, y_off, wz, r0))
        operands += [inner_arr, z_lo, z_hi, y_lo, y_hi]
        box_shape = (inner + 2 * wz, rows + 2 * r0, lanes)
        boxes.append(box_shape if inner_arr.ndim == 3 else (lead,) + box_shape)
    smem = pl.BlockSpec(memory_space=pltpu.SMEM)
    vmem = pl.BlockSpec(memory_space=pltpu.VMEM)
    hbm = pl.BlockSpec(memory_space=pl.ANY)
    points = planes * rows * lanes
    moves = sum(1 + 4 * p[0] for p in plan)
    return pl.pallas_call(
        functools.partial(step_kernel, tuple(plan)),
        out_shape=(
            jax.ShapeDtypeStruct((inner, out_rows, lanes), jnp.float32),
            jax.ShapeDtypeStruct((species, inner, out_rows, lanes), jnp.float32),
        ),
        in_specs=[smem, smem] + [hbm] * len(operands),
        out_specs=(vmem, vmem),
        scratch_shapes=[pltpu.VMEM(shape, jnp.float32) for shape in boxes]
        + [
            pltpu.VMEM((planes, rows + 16, lanes), jnp.float32),
            pltpu.VMEM((planes, rows + 16, lanes), jnp.float32),
            pltpu.VMEM((7, planes, rows, lanes), jnp.float32),
            pltpu.SemaphoreType.DMA((moves,)),
        ],
        cost_estimate=pl.CostEstimate(
            flops=points * (20 * SWEEPS + 20) + species * (inner + 2) * rows * lanes * 30,
            transcendentals=0,
            bytes_accessed=4 * (3 * points + inner * out_rows * lanes * (2 * species + 1)),
        ),
    )(diffusivity, charge_num, *operands)


def box(a, have, want):
    cut = have - want
    if cut == 0:
        return a
    return a[..., cut:a.shape[-3] - cut, cut:a.shape[-2] - cut, :]


def per_device(
    concentration,
    potential,
    permittivity,
    diffusivity,
    valence,
    charge_pos,
    charge_q,
    charge_tile,
    near_index,
    brick_mask,
):
    depth, height, width = potential.shape
    bands = lax.axis_size("narrow")
    rows_total = float(height * bands)
    tiles_all = float(TILES_DEV * bands)
    tile_rows = height // TILES_DEV
    slab = lax.axis_index("wide")
    band = lax.axis_index("narrow")
    index = near_index[0, 0]
    local_z = index // (height * width)
    local_y = index // width % height
    local_x = index % width
    global_z = slab * depth + local_z
    global_y = band * height + local_y
    node_z = global_z.astype(jnp.float32)
    node_y = global_y.astype(jnp.float32)
    node_x = local_x.astype(jnp.float32)
    node_tile = (global_y // tile_rows).astype(jnp.float32)
    slab_float = slab.astype(jnp.float32)
    deep = SWEEPS + 1
    wide_y = SWEEPS + 2
    charges = jnp.concatenate([charge_pos, charge_q, charge_tile.astype(jnp.float32)], axis=0)
    gathered = lax.all_gather(charges, "narrow", axis=1, tiled=True)
    gathered, potential, permittivity, concentration = lax.optimization_barrier(
        (gathered, potential, permittivity, concentration)
    )
    first = deep_halo(
        [(potential, deep, wide_y), (permittivity, deep, wide_y), (concentration, 1, wide_y)],
        "wide",
        "narrow",
    )
    values = pair_field(
        node_z,
        node_y,
        node_x,
        node_tile,
        gathered,
        slab_float,
        depth,
        rows_total,
        width,
        float(tile_rows),
        tiles_all,
    )
    values = values * brick_mask[0, 0].astype(jnp.float32)
    electrode = jnp.zeros((depth * height * width,), jnp.float32).at[index].add(values)
    electrode = electrode.reshape(depth, height, width)
    charge_num = valence.astype(jnp.float32)
    field = potential
    species = concentration
    perm_p = first[1]
    for step in range(STEPS):
        source = jnp.sum(charge_num[:, None, None, None] * species, axis=0) + electrode
        if step == 0:
            field_p, species_p = first[0], first[2]
            (source_p,) = deep_halo([(source, deep - 1, wide_y)], "wide", "narrow")
        else:
            field_p, source_p, species_p = deep_halo(
                [(field, deep, wide_y), (source, deep - 1, wide_y), (species, 1, wide_y)], "wide", "narrow"
            )
        field, species = time_step(diffusivity, charge_num, field_p, perm_p, source_p, species_p)
    return (species, field)


def solution(mesh):
    in_specs = (
        P(None, "wide", "narrow", None),
        P("wide", "narrow", None),
        P("wide", "narrow", None),
        P(),
        P(),
        P(None, ("wide", "narrow")),
        P(None, ("wide", "narrow")),
        P(None, ("wide", "narrow")),
        P("wide", "narrow", None),
        P("wide", "narrow"),
    )
    out_specs = (P(None, "wide", "narrow", None), P("wide", "narrow", None))
    return jax.shard_map(
        per_device, mesh=mesh, in_specs=in_specs, out_specs=out_specs, check_vma=False
    )
```

```python
import functools

import jax
import jax.numpy as jnp
from jax import lax
from jax.sharding import PartitionSpec as P
from jax.experimental import pallas as pl
from jax.experimental.pallas import tpu as pltpu

TILES_DEV = 4
STEPS = 2
SWEEPS = 6


def with_halo(cells, sides, width):
    for axis, dim in sides:
        count = lax.axis_size(axis)
        head = lax.slice_in_dim(cells, 0, width, axis=dim)
        tail = lax.slice_in_dim(cells, cells.shape[dim] - width, cells.shape[dim], axis=dim)
        cells = jnp.concatenate(
            [
                lax.ppermute(tail, axis, [(i, (i + 1) % count) for i in range(count)]),
                cells,
                lax.ppermute(head, axis, [((i + 1) % count, i) for i in range(count)]),
            ],
            axis=dim,
        )
    return cells


def relax(field_pad, perm_pad, source):
    centre = field_pad[1:-1, 1:-1]
    perm_centre = perm_pad[1:-1, 1:-1]
    numer = source
    denom = jnp.zeros_like(source)
    pairs = (
        (field_pad[2:, 1:-1], perm_pad[2:, 1:-1]),
        (field_pad[:-2, 1:-1], perm_pad[:-2, 1:-1]),
        (field_pad[1:-1, 2:], perm_pad[1:-1, 2:]),
        (field_pad[1:-1, :-2], perm_pad[1:-1, :-2]),
    )
    for other_field, other_perm in pairs:
        weight = 0.5 * (perm_centre + other_perm)
        numer = numer + weight * other_field
        denom = denom + weight
    zeros_edge = jnp.zeros_like(centre[..., :1])
    upper_field = jnp.concatenate([centre[..., 1:], zeros_edge], axis=-1)
    lower_field = jnp.concatenate([zeros_edge, centre[..., :-1]], axis=-1)
    upper_perm = jnp.concatenate([perm_centre[..., 1:], perm_centre[..., -1:]], axis=-1)
    lower_perm = jnp.concatenate([perm_centre[..., :1], perm_centre[..., :-1]], axis=-1)
    for other_field, other_perm in ((upper_field, upper_perm), (lower_field, lower_perm)):
        weight = 0.5 * (perm_centre + other_perm)
        numer = numer + weight * other_field
        denom = denom + weight
    return numer / denom


def transport(species_pad, field_pad, diffusivity, charge_num):
    centre = species_pad[:, 1:-1, 1:-1]
    field_centre = field_pad[1:-1, 1:-1]
    drift = charge_num[:, None, None, None]
    total = jnp.zeros_like(centre)
    pairs = (
        (species_pad[:, 2:, 1:-1], field_pad[2:, 1:-1]),
        (species_pad[:, :-2, 1:-1], field_pad[:-2, 1:-1]),
        (species_pad[:, 1:-1, 2:], field_pad[1:-1, 2:]),
        (species_pad[:, 1:-1, :-2], field_pad[1:-1, :-2]),
    )
    for other, other_field in pairs:
        total = (
            total + (centre - other) - drift * 0.5 * (centre + other) * (other_field - field_centre)
        )
    left = centre[..., :-1]
    right = centre[..., 1:]
    across = (
        left
        - right
        - drift * 0.5 * (left + right) * (field_centre[..., 1:] - field_centre[..., :-1])
    )
    zeros_edge = jnp.zeros_like(centre[..., :1])
    total = total + jnp.concatenate([across, zeros_edge], axis=-1)
    total = total - jnp.concatenate([zeros_edge, across], axis=-1)
    return centre - diffusivity[:, None, None, None] * total


def pair_field(
    node_z,
    node_y,
    node_x,
    node_tile,
    block,
    slab_float,
    depth,
    rows_total,
    width,
    tile_rows,
    tiles_all,
):
    charge_x = block[0] * width
    charge_y = (block[4] + block[1]) * tile_rows
    charge_z = (slab_float + block[2]) * depth
    strength = block[3]
    label = block[4]

    def one_block(nodes):
        pos_z, pos_y, pos_x, pos_tile = nodes
        offset_z = pos_z[:, None] - charge_z[None, :]
        offset_y = pos_y[:, None] - charge_y[None, :]
        offset_y = offset_y - rows_total * jnp.floor(offset_y / rows_total + 0.5)
        offset_x = pos_x[:, None] - charge_x[None, :]
        squared = offset_z * offset_z + offset_y * offset_y + offset_x * offset_x
        distance = jnp.sqrt(squared)
        tile_gap = jnp.abs(pos_tile[:, None] - label[None, :])
        adjacent = (tile_gap <= 1.0) | (tile_gap >= tiles_all - 1.0)
        term = strength[None, :] * jnp.exp(-distance / tile_rows) * lax.rsqrt(squared + 1.0)
        return jnp.sum(jnp.where(adjacent, term, 0.0), axis=1)

    half = node_z.shape[0] // 2
    parts = [one_block(tuple(arr[k * half:(k + 1) * half] for arr in (node_z, node_y, node_x, node_tile))) for k in range(2)]
    return jnp.concatenate(parts)


def ring(x, axis, shift):
    count = lax.axis_size(axis)
    return lax.ppermute(x, axis, [(i, (i + shift) % count) for i in range(count)])


def deep_halo(items, axis_z, axis_y):
    minor = items[0][0].shape[-1]
    rows = items[0][0].shape[-2]
    tops, bots = [], []
    for a, wz, _ in items:
        dim = a.ndim - 3
        n = a.shape[dim]
        tops.append(lax.slice_in_dim(a, n - wz, n, axis=dim))
        bots.append(lax.slice_in_dim(a, 0, wz, axis=dim))
    z_lo = ring(jnp.concatenate([t.reshape(-1, minor) for t in tops], axis=0), axis_z, 1)
    z_hi = ring(jnp.concatenate([t.reshape(-1, minor) for t in bots], axis=0), axis_z, -1)
    y_tops, y_bots, z_offs, at = [], [], [], 0
    for (a, wz, wy), t in zip(items, tops):
        size = t.size // minor
        z_offs.append(at // rows)
        ext = jnp.concatenate(
            [z_lo[at:at + size].reshape(t.shape), a, z_hi[at:at + size].reshape(t.shape)], axis=a.ndim - 3
        )
        at += size
        y_tops.append(ext[..., rows - wy:rows, :])
        y_bots.append(ext[..., 0:wy, :])
    wy = items[0][2]
    y_lo = ring(jnp.concatenate([t.reshape(-1, minor) for t in y_tops], axis=0), axis_y, 1)
    y_hi = ring(jnp.concatenate([t.reshape(-1, minor) for t in y_bots], axis=0), axis_y, -1)
    y_offs, at = [], 0
    for t in y_tops:
        y_offs.append(at // wy)
        at += t.size // minor
    bufs = (
        z_lo.reshape(-1, rows, minor),
        z_hi.reshape(-1, rows, minor),
        y_lo.reshape(-1, wy, minor),
        y_hi.reshape(-1, wy, minor),
    )
    return [(a,) + bufs + (zo, yo, wz) for (a, wz, _), zo, yo in zip(items, z_offs, y_offs)]


def step_kernel(plan, dif_ref, val_ref, *refs):
    hbm = refs[:20]
    fo_ref, co_ref, f_ref, p_ref, s_ref, c_ref, fa, fb, w_ref, sems = refs[20:]
    targets = (f_ref, p_ref, s_ref, c_ref)
    copies = [[] for _ in targets]
    count = 0
    for k, (lead, z_off, y_off, wz, r0) in enumerate(plan):
        inner_ref, z_lo, z_hi, y_lo, y_hi = hbm[5 * k:5 * k + 5]
        target = targets[k]
        span = 2 * wz + inner_ref.shape[-3]
        mid = slice(r0 + 8, r0 + 8 + inner_ref.shape[-2])
        moves = [(inner_ref, target.at[..., wz:span - wz, mid, :])]
        for s in range(lead):
            part = target.at[s] if lead > 1 or target.ndim == 4 else target
            zs = slice(z_off + s * wz, z_off + (s + 1) * wz)
            ys = slice(y_off + s * span, y_off + (s + 1) * span)
            moves += [
                (z_lo.at[zs], part.at[0:wz, mid, :]),
                (z_hi.at[zs], part.at[span - wz:span, mid, :]),
                (y_lo.at[ys], part.at[:, r0:r0 + 8, :]),
                (y_hi.at[ys], part.at[:, mid.stop:mid.stop + 8, :]),
            ]
        for src, dst in moves:
            copy = pltpu.make_async_copy(src, dst, sems.at[count])
            copy.start()
            copies[k].append(copy)
            count += 1

    def wait(k):
        for copy in copies[k]:
            copy.wait()

    planes, rows, lanes = p_ref.shape
    species, inner = c_ref.shape[0], c_ref.shape[1] - 2
    hz = (planes - inner) // 2
    hy = (rows - co_ref.shape[2]) // 2
    out_rows = co_ref.shape[2]
    lane = lax.broadcasted_iota(jnp.int32, (rows, lanes), 1)
    top = lane == lanes - 1
    bot = lane == 0

    def ysh(a, d):
        return pltpu.roll(a, (-d) % rows, 0)

    def xsh(a, d):
        return pltpu.roll(a, (-d) % lanes, 1)

    def weights(z, carry):
        pc = p_ref[z]
        ws = (
            0.5 * (pc + p_ref[z + 1]),
            0.5 * (pc + p_ref[z - 1]),
            0.5 * (pc + ysh(pc, 1)),
            0.5 * (pc + ysh(pc, -1)),
            0.5 * (pc + jnp.where(top, pc, xsh(pc, 1))),
            0.5 * (pc + jnp.where(bot, pc, xsh(pc, -1))),
        )
        den = jnp.zeros_like(pc)
        for w in ws:
            den = den + w
        inv = 1.0 / den
        for k in range(4):
            w_ref[k, z] = ws[k] * inv
        w_ref[4, z] = jnp.where(top, 0.0, ws[4]) * inv
        w_ref[5, z] = jnp.where(bot, 0.0, ws[5]) * inv
        w_ref[6, z] = s_ref[z - 1] * inv
        return carry

    wait(1)
    wait(2)
    lax.fori_loop(1, planes - 1, weights, 0, unroll=2)
    wait(0)
    pad = jnp.zeros((planes, 8, lanes), jnp.float32)
    for buf in (f_ref, fa, fb):
        buf[:, 0:8, :] = pad
        buf[:, 88:96, :] = pad
    bufs = (fa, fb)
    sweeps = hz - 1
    for k in range(sweeps):
        rd = f_ref if k == 0 else bufs[(k - 1) % 2]
        wr = bufs[k % 2]

        def sweep(z, carry, rd=rd, wr=wr):
            fc = rd[z, 8:88]
            near_z = (w_ref[6, z] + w_ref[0, z] * rd[z + 1, 8:88]) + w_ref[1, z] * rd[z - 1, 8:88]
            near_y = w_ref[2, z] * rd[z, pl.ds(9, rows)] + w_ref[3, z] * rd[z, pl.ds(7, rows)]
            near_x = w_ref[4, z] * xsh(fc, 1) + w_ref[5, z] * xsh(fc, -1)
            wr[z, 8:88] = near_z + (near_y + near_x)
            return carry

        lax.fori_loop(k + 1, planes - k - 1, sweep, 0, unroll=2)
    final = bufs[(sweeps - 1) % 2]
    wait(3)

    def move(z, carry):
        zf = z + hz
        fc = final[zf, 8:88]
        fo_ref[z] = fc[hy:hy + out_rows]
        pairs_field = (final[zf + 1, 8:88], final[zf - 1, 8:88], ysh(fc, 1), ysh(fc, -1))
        fr = xsh(fc, 1)
        for s in range(species):
            drift = val_ref[s]
            c = c_ref[s, z + 1]
            others = (c_ref[s, z + 2], c_ref[s, z], ysh(c, 1), ysh(c, -1))
            total = jnp.zeros_like(c)
            for other, other_field in zip(others, pairs_field):
                total = total + (c - other) - drift * 0.5 * (c + other) * (other_field - fc)
            right = xsh(c, 1)
            across = c - right - drift * 0.5 * (c + right) * (fr - fc)
            across = jnp.where(top, 0.0, across)
            total = total + across
            total = total - xsh(across, -1)
            new = c - dif_ref[s] * total
            co_ref[s, z] = new[hy:hy + out_rows]
        return carry

    lax.fori_loop(0, inner, move, 0, unroll=2)


def time_step(diffusivity, charge_num, field_p, perm_p, source_p, species_p):
    species, inner, out_rows, lanes = species_p[0].shape
    planes = inner + 2 * field_p[7]
    rows = out_rows + 2 * (SWEEPS + 2)
    plan, operands, boxes = [], [], []
    for pieces, r0 in ((field_p, 8), (perm_p, 0), (source_p, 0), (species_p, 0)):
        inner_arr, z_lo, z_hi, y_lo, y_hi, z_off, y_off, wz = pieces
        lead = inner_arr.shape[0] if inner_arr.ndim == 4 else 1
        plan.append((lead, z_off, y_off, wz, r0))
        operands += [inner_arr, z_lo, z_hi, y_lo, y_hi]
        box_shape = (inner + 2 * wz, rows + 2 * r0, lanes)
        boxes.append(box_shape if inner_arr.ndim == 3 else (lead,) + box_shape)
    smem = pl.BlockSpec(memory_space=pltpu.SMEM)
    vmem = pl.BlockSpec(memory_space=pltpu.VMEM)
    hbm = pl.BlockSpec(memory_space=pl.ANY)
    points = planes * rows * lanes
    moves = sum(1 + 4 * p[0] for p in plan)
    return pl.pallas_call(
        functools.partial(step_kernel, tuple(plan)),
        out_shape=(
            jax.ShapeDtypeStruct((inner, out_rows, lanes), jnp.float32),
            jax.ShapeDtypeStruct((species, inner, out_rows, lanes), jnp.float32),
        ),
        in_specs=[smem, smem] + [hbm] * len(operands),
        out_specs=(vmem, vmem),
        scratch_shapes=[pltpu.VMEM(shape, jnp.float32) for shape in boxes]
        + [
            pltpu.VMEM((planes, rows + 16, lanes), jnp.float32),
            pltpu.VMEM((planes, rows + 16, lanes), jnp.float32),
            pltpu.VMEM((7, planes, rows, lanes), jnp.float32),
            pltpu.SemaphoreType.DMA((moves,)),
        ],
        cost_estimate=pl.CostEstimate(
            flops=points * (20 * SWEEPS + 20) + species * (inner + 2) * rows * lanes * 30,
            transcendentals=0,
            bytes_accessed=4 * (3 * points + inner * out_rows * lanes * (2 * species + 1)),
        ),
    )(diffusivity, charge_num, *operands)


def box(a, have, want):
    cut = have - want
    if cut == 0:
        return a
    return a[..., cut:a.shape[-3] - cut, cut:a.shape[-2] - cut, :]


def per_device(
    concentration,
    potential,
    permittivity,
    diffusivity,
    valence,
    charge_pos,
    charge_q,
    charge_tile,
    near_index,
    brick_mask,
):
    depth, height, width = potential.shape
    bands = lax.axis_size("narrow")
    rows_total = float(height * bands)
    tiles_all = float(TILES_DEV * bands)
    tile_rows = height // TILES_DEV
    slab = lax.axis_index("wide")
    band = lax.axis_index("narrow")
    index = near_index[0, 0]
    local_z = index // (height * width)
    local_y = index // width % height
    local_x = index % width
    global_z = slab * depth + local_z
    global_y = band * height + local_y
    node_z = global_z.astype(jnp.float32)
    node_y = global_y.astype(jnp.float32)
    node_x = local_x.astype(jnp.float32)
    node_tile = (global_y // tile_rows).astype(jnp.float32)
    slab_float = slab.astype(jnp.float32)
    deep = SWEEPS + 1
    wide_y = SWEEPS + 2
    charges = jnp.concatenate([charge_pos, charge_q, charge_tile.astype(jnp.float32)], axis=0)
    gathered = lax.all_gather(charges, "narrow", axis=1, tiled=True)
    gathered, potential, permittivity, concentration = lax.optimization_barrier(
        (gathered, potential, permittivity, concentration)
    )
    first = deep_halo(
        [(potential, deep, wide_y), (permittivity, deep, wide_y), (concentration, 1, wide_y)],
        "wide",
        "narrow",
    )
    values = pair_field(
        node_z,
        node_y,
        node_x,
        node_tile,
        gathered,
        slab_float,
        depth,
        rows_total,
        width,
        float(tile_rows),
        tiles_all,
    )
    values = values * brick_mask[0, 0].astype(jnp.float32)
    node_row = index // width
    picks = jnp.where(
        node_row[None, :] == jnp.arange(depth * height, dtype=jnp.int32)[:, None], values[None, :], 0.0
    )
    lanes_of = (local_x[:, None] == jnp.arange(width, dtype=jnp.int32)[None, :]).astype(jnp.float32)
    electrode = jnp.dot(picks, lanes_of, precision=lax.Precision.HIGHEST, preferred_element_type=jnp.float32)
    electrode = electrode.reshape(depth, height, width)
    charge_num = valence.astype(jnp.float32)
    field = potential
    species = concentration
    perm_p = first[1]
    for step in range(STEPS):
        source = jnp.sum(charge_num[:, None, None, None] * species, axis=0) + electrode
        if step == 0:
            field_p, species_p = first[0], first[2]
            (source_p,) = deep_halo([(source, deep - 1, wide_y)], "wide", "narrow")
        else:
            field_p, source_p, species_p = deep_halo(
                [(field, deep, wide_y), (source, deep - 1, wide_y), (species, 1, wide_y)], "wide", "narrow"
            )
        field, species = time_step(diffusivity, charge_num, field_p, perm_p, source_p, species_p)
    return (species, field)


def solution(mesh):
    in_specs = (
        P(None, "wide", "narrow", None),
        P("wide", "narrow", None),
        P("wide", "narrow", None),
        P(),
        P(),
        P(None, ("wide", "narrow")),
        P(None, ("wide", "narrow")),
        P(None, ("wide", "narrow")),
        P("wide", "narrow", None),
        P("wide", "narrow"),
    )
    out_specs = (P(None, "wide", "narrow", None), P("wide", "narrow", None))
    return jax.shard_map(
        per_device, mesh=mesh, in_specs=in_specs, out_specs=out_specs, check_vma=False
    )
```

```python
import functools

import jax
import jax.numpy as jnp
from jax import lax
from jax.sharding import PartitionSpec as P
from jax.experimental import pallas as pl
from jax.experimental.pallas import tpu as pltpu

TILES_DEV = 4
STEPS = 2
SWEEPS = 6


def with_halo(cells, sides, width):
    for axis, dim in sides:
        count = lax.axis_size(axis)
        head = lax.slice_in_dim(cells, 0, width, axis=dim)
        tail = lax.slice_in_dim(cells, cells.shape[dim] - width, cells.shape[dim], axis=dim)
        cells = jnp.concatenate(
            [
                lax.ppermute(tail, axis, [(i, (i + 1) % count) for i in range(count)]),
                cells,
                lax.ppermute(head, axis, [((i + 1) % count, i) for i in range(count)]),
            ],
            axis=dim,
        )
    return cells


def relax(field_pad, perm_pad, source):
    centre = field_pad[1:-1, 1:-1]
    perm_centre = perm_pad[1:-1, 1:-1]
    numer = source
    denom = jnp.zeros_like(source)
    pairs = (
        (field_pad[2:, 1:-1], perm_pad[2:, 1:-1]),
        (field_pad[:-2, 1:-1], perm_pad[:-2, 1:-1]),
        (field_pad[1:-1, 2:], perm_pad[1:-1, 2:]),
        (field_pad[1:-1, :-2], perm_pad[1:-1, :-2]),
    )
    for other_field, other_perm in pairs:
        weight = 0.5 * (perm_centre + other_perm)
        numer = numer + weight * other_field
        denom = denom + weight
    zeros_edge = jnp.zeros_like(centre[..., :1])
    upper_field = jnp.concatenate([centre[..., 1:], zeros_edge], axis=-1)
    lower_field = jnp.concatenate([zeros_edge, centre[..., :-1]], axis=-1)
    upper_perm = jnp.concatenate([perm_centre[..., 1:], perm_centre[..., -1:]], axis=-1)
    lower_perm = jnp.concatenate([perm_centre[..., :1], perm_centre[..., :-1]], axis=-1)
    for other_field, other_perm in ((upper_field, upper_perm), (lower_field, lower_perm)):
        weight = 0.5 * (perm_centre + other_perm)
        numer = numer + weight * other_field
        denom = denom + weight
    return numer / denom


def transport(species_pad, field_pad, diffusivity, charge_num):
    centre = species_pad[:, 1:-1, 1:-1]
    field_centre = field_pad[1:-1, 1:-1]
    drift = charge_num[:, None, None, None]
    total = jnp.zeros_like(centre)
    pairs = (
        (species_pad[:, 2:, 1:-1], field_pad[2:, 1:-1]),
        (species_pad[:, :-2, 1:-1], field_pad[:-2, 1:-1]),
        (species_pad[:, 1:-1, 2:], field_pad[1:-1, 2:]),
        (species_pad[:, 1:-1, :-2], field_pad[1:-1, :-2]),
    )
    for other, other_field in pairs:
        total = (
            total + (centre - other) - drift * 0.5 * (centre + other) * (other_field - field_centre)
        )
    left = centre[..., :-1]
    right = centre[..., 1:]
    across = (
        left
        - right
        - drift * 0.5 * (left + right) * (field_centre[..., 1:] - field_centre[..., :-1])
    )
    zeros_edge = jnp.zeros_like(centre[..., :1])
    total = total + jnp.concatenate([across, zeros_edge], axis=-1)
    total = total - jnp.concatenate([zeros_edge, across], axis=-1)
    return centre - diffusivity[:, None, None, None] * total


def pair_field(
    node_z,
    node_y,
    node_x,
    node_tile,
    block,
    slab_float,
    depth,
    rows_total,
    width,
    tile_rows,
    tiles_all,
):
    charge_x = block[0] * width
    charge_y = (block[4] + block[1]) * tile_rows
    charge_z = (slab_float + block[2]) * depth
    strength = block[3]
    label = block[4]

    def one_block(nodes):
        pos_z, pos_y, pos_x, pos_tile = nodes
        offset_z = pos_z[:, None] - charge_z[None, :]
        offset_y = pos_y[:, None] - charge_y[None, :]
        offset_y = offset_y - rows_total * jnp.floor(offset_y / rows_total + 0.5)
        offset_x = pos_x[:, None] - charge_x[None, :]
        squared = offset_z * offset_z + offset_y * offset_y + offset_x * offset_x
        distance = jnp.sqrt(squared)
        tile_gap = jnp.abs(pos_tile[:, None] - label[None, :])
        adjacent = (tile_gap <= 1.0) | (tile_gap >= tiles_all - 1.0)
        term = strength[None, :] * jnp.exp(-distance / tile_rows) * lax.rsqrt(squared + 1.0)
        return jnp.sum(jnp.where(adjacent, term, 0.0), axis=1)

    half = node_z.shape[0] // 2
    parts = [one_block(tuple(arr[k * half:(k + 1) * half] for arr in (node_z, node_y, node_x, node_tile))) for k in range(2)]
    return jnp.concatenate(parts)


def ring(x, axis, shift):
    count = lax.axis_size(axis)
    return lax.ppermute(x, axis, [(i, (i + shift) % count) for i in range(count)])


def deep_halo(items, axis_z, axis_y):
    minor = items[0][0].shape[-1]
    rows = items[0][0].shape[-2]
    tops, bots = [], []
    for a, wz, _ in items:
        dim = a.ndim - 3
        n = a.shape[dim]
        tops.append(lax.slice_in_dim(a, n - wz, n, axis=dim))
        bots.append(lax.slice_in_dim(a, 0, wz, axis=dim))
    z_lo = ring(jnp.concatenate([t.reshape(-1, minor) for t in tops], axis=0), axis_z, 1)
    z_hi = ring(jnp.concatenate([t.reshape(-1, minor) for t in bots], axis=0), axis_z, -1)
    y_tops, y_bots, z_offs, at = [], [], [], 0
    for (a, wz, wy), t in zip(items, tops):
        size = t.size // minor
        z_offs.append(at // rows)
        ext = jnp.concatenate(
            [z_lo[at:at + size].reshape(t.shape), a, z_hi[at:at + size].reshape(t.shape)], axis=a.ndim - 3
        )
        at += size
        y_tops.append(ext[..., rows - wy:rows, :])
        y_bots.append(ext[..., 0:wy, :])
    wy = items[0][2]
    y_lo = ring(jnp.concatenate([t.reshape(-1, minor) for t in y_tops], axis=0), axis_y, 1)
    y_hi = ring(jnp.concatenate([t.reshape(-1, minor) for t in y_bots], axis=0), axis_y, -1)
    y_offs, at = [], 0
    for t in y_tops:
        y_offs.append(at // wy)
        at += t.size // minor
    bufs = (
        z_lo.reshape(-1, rows, minor),
        z_hi.reshape(-1, rows, minor),
        y_lo.reshape(-1, wy, minor),
        y_hi.reshape(-1, wy, minor),
    )
    return [(a,) + bufs + (zo, yo, wz) for (a, wz, _), zo, yo in zip(items, z_offs, y_offs)]


def step_kernel(plan, with_source, dif_ref, val_ref, *refs):
    hbm = refs[:20]
    rest = list(refs[20:])
    e_ref = rest.pop(0) if with_source else None
    fo_ref, co_ref = rest[0], rest[1]
    so_ref = rest.pop(2) if with_source else None
    f_ref, p_ref, s_ref, c_ref, fa, fb, w_ref, sems = rest[2:]
    targets = (f_ref, p_ref, s_ref, c_ref)
    copies = [[] for _ in targets]
    count = 0
    for k, (lead, z_off, y_off, wz, r0) in enumerate(plan):
        inner_ref, z_lo, z_hi, y_lo, y_hi = hbm[5 * k:5 * k + 5]
        target = targets[k]
        span = 2 * wz + inner_ref.shape[-3]
        mid = slice(r0 + 8, r0 + 8 + inner_ref.shape[-2])
        moves = [(inner_ref, target.at[..., wz:span - wz, mid, :])]
        for s in range(lead):
            part = target.at[s] if lead > 1 or target.ndim == 4 else target
            zs = slice(z_off + s * wz, z_off + (s + 1) * wz)
            ys = slice(y_off + s * span, y_off + (s + 1) * span)
            moves += [
                (z_lo.at[zs], part.at[0:wz, mid, :]),
                (z_hi.at[zs], part.at[span - wz:span, mid, :]),
                (y_lo.at[ys], part.at[:, r0:r0 + 8, :]),
                (y_hi.at[ys], part.at[:, mid.stop:mid.stop + 8, :]),
            ]
        for src, dst in moves:
            copy = pltpu.make_async_copy(src, dst, sems.at[count])
            copy.start()
            copies[k].append(copy)
            count += 1

    def wait(k):
        for copy in copies[k]:
            copy.wait()

    planes, rows, lanes = p_ref.shape
    species, inner = c_ref.shape[0], c_ref.shape[1] - 2
    hz = (planes - inner) // 2
    hy = (rows - co_ref.shape[2]) // 2
    out_rows = co_ref.shape[2]
    lane = lax.broadcasted_iota(jnp.int32, (rows, lanes), 1)
    top = lane == lanes - 1
    bot = lane == 0

    def ysh(a, d):
        return pltpu.roll(a, (-d) % rows, 0)

    def xsh(a, d):
        return pltpu.roll(a, (-d) % lanes, 1)

    def weights(z, carry):
        pc = p_ref[z]
        ws = (
            0.5 * (pc + p_ref[z + 1]),
            0.5 * (pc + p_ref[z - 1]),
            0.5 * (pc + ysh(pc, 1)),
            0.5 * (pc + ysh(pc, -1)),
            0.5 * (pc + jnp.where(top, pc, xsh(pc, 1))),
            0.5 * (pc + jnp.where(bot, pc, xsh(pc, -1))),
        )
        den = jnp.zeros_like(pc)
        for w in ws:
            den = den + w
        inv = 1.0 / den
        for k in range(4):
            w_ref[k, z] = ws[k] * inv
        w_ref[4, z] = jnp.where(top, 0.0, ws[4]) * inv
        w_ref[5, z] = jnp.where(bot, 0.0, ws[5]) * inv
        w_ref[6, z] = s_ref[z - 1] * inv
        return carry

    wait(1)
    wait(2)
    lax.fori_loop(1, planes - 1, weights, 0, unroll=2)
    wait(0)
    pad = jnp.zeros((planes, 8, lanes), jnp.float32)
    for buf in (f_ref, fa, fb):
        buf[:, 0:8, :] = pad
        buf[:, 88:96, :] = pad
    bufs = (fa, fb)
    sweeps = hz - 1
    for k in range(sweeps):
        rd = f_ref if k == 0 else bufs[(k - 1) % 2]
        wr = bufs[k % 2]

        def sweep(z, carry, rd=rd, wr=wr):
            fc = rd[z, 8:88]
            near_z = (w_ref[6, z] + w_ref[0, z] * rd[z + 1, 8:88]) + w_ref[1, z] * rd[z - 1, 8:88]
            near_y = w_ref[2, z] * rd[z, pl.ds(9, rows)] + w_ref[3, z] * rd[z, pl.ds(7, rows)]
            near_x = w_ref[4, z] * xsh(fc, 1) + w_ref[5, z] * xsh(fc, -1)
            wr[z, 8:88] = near_z + (near_y + near_x)
            return carry

        lax.fori_loop(k + 1, planes - k - 1, sweep, 0, unroll=2)
    final = bufs[(sweeps - 1) % 2]
    wait(3)

    def move(z, carry):
        zf = z + hz
        fc = final[zf, 8:88]
        fo_ref[z] = fc[hy:hy + out_rows]
        pairs_field = (final[zf + 1, 8:88], final[zf - 1, 8:88], ysh(fc, 1), ysh(fc, -1))
        fr = xsh(fc, 1)
        for s in range(species):
            drift = val_ref[s]
            c = c_ref[s, z + 1]
            others = (c_ref[s, z + 2], c_ref[s, z], ysh(c, 1), ysh(c, -1))
            total = jnp.zeros_like(c)
            for other, other_field in zip(others, pairs_field):
                total = total + (c - other) - drift * 0.5 * (c + other) * (other_field - fc)
            right = xsh(c, 1)
            across = c - right - drift * 0.5 * (c + right) * (fr - fc)
            across = jnp.where(top, 0.0, across)
            total = total + across
            total = total - xsh(across, -1)
            new = c - dif_ref[s] * total
            co_ref[s, z] = new[hy:hy + out_rows]
            if with_source:
                charged = drift * new[hy:hy + out_rows]
                mix = charged if s == 0 else mix + charged
        if with_source:
            so_ref[z] = mix + e_ref[z]
        return carry

    lax.fori_loop(0, inner, move, 0, unroll=2)


def time_step(diffusivity, charge_num, field_p, perm_p, source_p, species_p, electrode=None):
    species, inner, out_rows, lanes = species_p[0].shape
    planes = inner + 2 * field_p[7]
    rows = out_rows + 2 * (SWEEPS + 2)
    plan, operands, boxes = [], [], []
    for pieces, r0 in ((field_p, 8), (perm_p, 0), (source_p, 0), (species_p, 0)):
        inner_arr, z_lo, z_hi, y_lo, y_hi, z_off, y_off, wz = pieces
        lead = inner_arr.shape[0] if inner_arr.ndim == 4 else 1
        plan.append((lead, z_off, y_off, wz, r0))
        operands += [inner_arr, z_lo, z_hi, y_lo, y_hi]
        box_shape = (inner + 2 * wz, rows + 2 * r0, lanes)
        boxes.append(box_shape if inner_arr.ndim == 3 else (lead,) + box_shape)
    smem = pl.BlockSpec(memory_space=pltpu.SMEM)
    vmem = pl.BlockSpec(memory_space=pltpu.VMEM)
    hbm = pl.BlockSpec(memory_space=pl.ANY)
    points = planes * rows * lanes
    moves = sum(1 + 4 * p[0] for p in plan)
    with_source = electrode is not None
    out_shape = [
        jax.ShapeDtypeStruct((inner, out_rows, lanes), jnp.float32),
        jax.ShapeDtypeStruct((species, inner, out_rows, lanes), jnp.float32),
    ]
    extra = []
    if with_source:
        out_shape.append(jax.ShapeDtypeStruct((inner, out_rows, lanes), jnp.float32))
        extra = [electrode]
    return pl.pallas_call(
        functools.partial(step_kernel, tuple(plan), with_source),
        out_shape=tuple(out_shape),
        in_specs=[smem, smem] + [hbm] * len(operands) + [vmem] * len(extra),
        out_specs=tuple([vmem] * len(out_shape)),
        scratch_shapes=[pltpu.VMEM(shape, jnp.float32) for shape in boxes]
        + [
            pltpu.VMEM((planes, rows + 16, lanes), jnp.float32),
            pltpu.VMEM((planes, rows + 16, lanes), jnp.float32),
            pltpu.VMEM((7, planes, rows, lanes), jnp.float32),
            pltpu.SemaphoreType.DMA((moves,)),
        ],
        cost_estimate=pl.CostEstimate(
            flops=points * (20 * SWEEPS + 20) + species * (inner + 2) * rows * lanes * 30,
            transcendentals=0,
            bytes_accessed=4 * (3 * points + inner * out_rows * lanes * (2 * species + 1)),
        ),
    )(diffusivity, charge_num, *operands, *extra)


def box(a, have, want):
    cut = have - want
    if cut == 0:
        return a
    return a[..., cut:a.shape[-3] - cut, cut:a.shape[-2] - cut, :]


def per_device(
    concentration,
    potential,
    permittivity,
    diffusivity,
    valence,
    charge_pos,
    charge_q,
    charge_tile,
    near_index,
    brick_mask,
):
    depth, height, width = potential.shape
    bands = lax.axis_size("narrow")
    rows_total = float(height * bands)
    tiles_all = float(TILES_DEV * bands)
    tile_rows = height // TILES_DEV
    slab = lax.axis_index("wide")
    band = lax.axis_index("narrow")
    index = near_index[0, 0]
    local_z = index // (height * width)
    local_y = index // width % height
    local_x = index % width
    global_z = slab * depth + local_z
    global_y = band * height + local_y
    node_z = global_z.astype(jnp.float32)
    node_y = global_y.astype(jnp.float32)
    node_x = local_x.astype(jnp.float32)
    node_tile = (global_y // tile_rows).astype(jnp.float32)
    slab_float = slab.astype(jnp.float32)
    deep = SWEEPS + 1
    wide_y = SWEEPS + 2
    charges = jnp.concatenate([charge_pos, charge_q, charge_tile.astype(jnp.float32)], axis=0)
    gathered = lax.all_gather(charges, "narrow", axis=1, tiled=True)
    gathered, potential, permittivity, concentration = lax.optimization_barrier(
        (gathered, potential, permittivity, concentration)
    )
    first = deep_halo(
        [(potential, deep, wide_y), (permittivity, deep, wide_y), (concentration, 1, wide_y)],
        "wide",
        "narrow",
    )
    values = pair_field(
        node_z,
        node_y,
        node_x,
        node_tile,
        gathered,
        slab_float,
        depth,
        rows_total,
        width,
        float(tile_rows),
        tiles_all,
    )
    values = values * brick_mask[0, 0].astype(jnp.float32)
    node_row = index // width
    picks = jnp.where(
        node_row[None, :] == jnp.arange(depth * height, dtype=jnp.int32)[:, None], values[None, :], 0.0
    )
    lanes_of = (local_x[:, None] == jnp.arange(width, dtype=jnp.int32)[None, :]).astype(jnp.float32)
    electrode = jnp.dot(picks, lanes_of, precision=lax.Precision.HIGHEST, preferred_element_type=jnp.float32)
    electrode = electrode.reshape(depth, height, width)
    charge_num = valence.astype(jnp.float32)
    field = potential
    species = concentration
    perm_p = first[1]
    for step in range(STEPS):
        if step == 0:
            source = jnp.sum(charge_num[:, None, None, None] * species, axis=0) + electrode
            field_p, species_p = first[0], first[2]
            (source_p,) = deep_halo([(source, deep - 1, wide_y)], "wide", "narrow")
        else:
            field_p, source_p, species_p = deep_halo(
                [(field, deep, wide_y), (source, deep - 1, wide_y), (species, 1, wide_y)], "wide", "narrow"
            )
        if step + 1 < STEPS:
            field, species, source = time_step(
                diffusivity, charge_num, field_p, perm_p, source_p, species_p, electrode
            )
        else:
            field, species = time_step(diffusivity, charge_num, field_p, perm_p, source_p, species_p)
    return (species, field)


def solution(mesh):
    in_specs = (
        P(None, "wide", "narrow", None),
        P("wide", "narrow", None),
        P("wide", "narrow", None),
        P(),
        P(),
        P(None, ("wide", "narrow")),
        P(None, ("wide", "narrow")),
        P(None, ("wide", "narrow")),
        P("wide", "narrow", None),
        P("wide", "narrow"),
    )
    out_specs = (P(None, "wide", "narrow", None), P("wide", "narrow", None))
    return jax.shard_map(
        per_device, mesh=mesh, in_specs=in_specs, out_specs=out_specs, check_vma=False
    )
```

```python
import functools

import jax
import jax.numpy as jnp
from jax import lax
from jax.sharding import PartitionSpec as P
from jax.experimental import pallas as pl
from jax.experimental.pallas import tpu as pltpu

TILES_DEV = 4
STEPS = 2
SWEEPS = 6


def with_halo(cells, sides, width):
    for axis, dim in sides:
        count = lax.axis_size(axis)
        head = lax.slice_in_dim(cells, 0, width, axis=dim)
        tail = lax.slice_in_dim(cells, cells.shape[dim] - width, cells.shape[dim], axis=dim)
        cells = jnp.concatenate(
            [
                lax.ppermute(tail, axis, [(i, (i + 1) % count) for i in range(count)]),
                cells,
                lax.ppermute(head, axis, [((i + 1) % count, i) for i in range(count)]),
            ],
            axis=dim,
        )
    return cells


def relax(field_pad, perm_pad, source):
    centre = field_pad[1:-1, 1:-1]
    perm_centre = perm_pad[1:-1, 1:-1]
    numer = source
    denom = jnp.zeros_like(source)
    pairs = (
        (field_pad[2:, 1:-1], perm_pad[2:, 1:-1]),
        (field_pad[:-2, 1:-1], perm_pad[:-2, 1:-1]),
        (field_pad[1:-1, 2:], perm_pad[1:-1, 2:]),
        (field_pad[1:-1, :-2], perm_pad[1:-1, :-2]),
    )
    for other_field, other_perm in pairs:
        weight = 0.5 * (perm_centre + other_perm)
        numer = numer + weight * other_field
        denom = denom + weight
    zeros_edge = jnp.zeros_like(centre[..., :1])
    upper_field = jnp.concatenate([centre[..., 1:], zeros_edge], axis=-1)
    lower_field = jnp.concatenate([zeros_edge, centre[..., :-1]], axis=-1)
    upper_perm = jnp.concatenate([perm_centre[..., 1:], perm_centre[..., -1:]], axis=-1)
    lower_perm = jnp.concatenate([perm_centre[..., :1], perm_centre[..., :-1]], axis=-1)
    for other_field, other_perm in ((upper_field, upper_perm), (lower_field, lower_perm)):
        weight = 0.5 * (perm_centre + other_perm)
        numer = numer + weight * other_field
        denom = denom + weight
    return numer / denom


def transport(species_pad, field_pad, diffusivity, charge_num):
    centre = species_pad[:, 1:-1, 1:-1]
    field_centre = field_pad[1:-1, 1:-1]
    drift = charge_num[:, None, None, None]
    total = jnp.zeros_like(centre)
    pairs = (
        (species_pad[:, 2:, 1:-1], field_pad[2:, 1:-1]),
        (species_pad[:, :-2, 1:-1], field_pad[:-2, 1:-1]),
        (species_pad[:, 1:-1, 2:], field_pad[1:-1, 2:]),
        (species_pad[:, 1:-1, :-2], field_pad[1:-1, :-2]),
    )
    for other, other_field in pairs:
        total = (
            total + (centre - other) - drift * 0.5 * (centre + other) * (other_field - field_centre)
        )
    left = centre[..., :-1]
    right = centre[..., 1:]
    across = (
        left
        - right
        - drift * 0.5 * (left + right) * (field_centre[..., 1:] - field_centre[..., :-1])
    )
    zeros_edge = jnp.zeros_like(centre[..., :1])
    total = total + jnp.concatenate([across, zeros_edge], axis=-1)
    total = total - jnp.concatenate([zeros_edge, across], axis=-1)
    return centre - diffusivity[:, None, None, None] * total


def pair_field(
    node_z,
    node_y,
    node_x,
    node_tile,
    block,
    slab_float,
    depth,
    rows_total,
    width,
    tile_rows,
    tiles_all,
):
    charge_x = block[0] * width
    charge_y = (block[4] + block[1]) * tile_rows
    charge_z = (slab_float + block[2]) * depth
    strength = block[3]
    label = block[4]

    def one_block(nodes):
        pos_z, pos_y, pos_x, pos_tile = nodes
        offset_z = pos_z[:, None] - charge_z[None, :]
        offset_y = pos_y[:, None] - charge_y[None, :]
        offset_y = offset_y - rows_total * jnp.floor(offset_y / rows_total + 0.5)
        offset_x = pos_x[:, None] - charge_x[None, :]
        squared = offset_z * offset_z + offset_y * offset_y + offset_x * offset_x
        distance = jnp.sqrt(squared)
        tile_gap = jnp.abs(pos_tile[:, None] - label[None, :])
        adjacent = (tile_gap <= 1.0) | (tile_gap >= tiles_all - 1.0)
        term = strength[None, :] * jnp.exp(-distance / tile_rows) * lax.rsqrt(squared + 1.0)
        return jnp.sum(jnp.where(adjacent, term, 0.0), axis=1)

    half = node_z.shape[0] // 2
    parts = [one_block(tuple(arr[k * half:(k + 1) * half] for arr in (node_z, node_y, node_x, node_tile))) for k in range(2)]
    return jnp.concatenate(parts)


def ring(x, axis, shift):
    count = lax.axis_size(axis)
    return lax.ppermute(x, axis, [(i, (i + shift) % count) for i in range(count)])


def deep_halo(items, axis_z, axis_y, sends=None):
    minor = items[0][0].shape[-1]
    rows = items[0][0].shape[-2]
    tops, bots = [], []
    for a, wz, _ in items:
        dim = a.ndim - 3
        n = a.shape[dim]
        tops.append(lax.slice_in_dim(a, n - wz, n, axis=dim))
        bots.append(lax.slice_in_dim(a, 0, wz, axis=dim))
    if sends is None:
        top = jnp.concatenate([t.reshape(-1, minor) for t in tops], axis=0)
        bot = jnp.concatenate([t.reshape(-1, minor) for t in bots], axis=0)
    else:
        top, bot = (s.reshape(-1, minor) for s in sends)
    z_lo = ring(top, axis_z, 1)
    z_hi = ring(bot, axis_z, -1)
    y_tops, y_bots, z_offs, at = [], [], [], 0
    for (a, wz, wy), t in zip(items, tops):
        size = t.size // minor
        z_offs.append(at // rows)
        ext = jnp.concatenate(
            [z_lo[at:at + size].reshape(t.shape), a, z_hi[at:at + size].reshape(t.shape)], axis=a.ndim - 3
        )
        at += size
        y_tops.append(ext[..., rows - wy:rows, :])
        y_bots.append(ext[..., 0:wy, :])
    wy = items[0][2]
    y_lo = ring(jnp.concatenate([t.reshape(-1, minor) for t in y_tops], axis=0), axis_y, 1)
    y_hi = ring(jnp.concatenate([t.reshape(-1, minor) for t in y_bots], axis=0), axis_y, -1)
    y_offs, at = [], 0
    for t in y_tops:
        y_offs.append(at // wy)
        at += t.size // minor
    bufs = (
        z_lo.reshape(-1, rows, minor),
        z_hi.reshape(-1, rows, minor),
        y_lo.reshape(-1, wy, minor),
        y_hi.reshape(-1, wy, minor),
    )
    return [(a,) + bufs + (zo, yo, wz) for (a, wz, _), zo, yo in zip(items, z_offs, y_offs)]


def step_kernel(plan, with_source, dif_ref, val_ref, *refs):
    hbm = refs[:20]
    rest = list(refs[20:])
    e_ref = rest.pop(0) if with_source else None
    fo_ref, co_ref = rest[0], rest[1]
    if with_source:
        so_ref, top_ref, bot_ref = rest.pop(2), rest.pop(2), rest.pop(2)
    f_ref, p_ref, s_ref, c_ref, fa, fb, w_ref, sems = rest[2:]
    targets = (f_ref, p_ref, s_ref, c_ref)
    copies = [[] for _ in targets]
    count = 0
    for k, (lead, z_off, y_off, wz, r0) in enumerate(plan):
        inner_ref, z_lo, z_hi, y_lo, y_hi = hbm[5 * k:5 * k + 5]
        target = targets[k]
        span = 2 * wz + inner_ref.shape[-3]
        mid = slice(r0 + 8, r0 + 8 + inner_ref.shape[-2])
        moves = [(inner_ref, target.at[..., wz:span - wz, mid, :])]
        for s in range(lead):
            part = target.at[s] if lead > 1 or target.ndim == 4 else target
            zs = slice(z_off + s * wz, z_off + (s + 1) * wz)
            ys = slice(y_off + s * span, y_off + (s + 1) * span)
            moves += [
                (z_lo.at[zs], part.at[0:wz, mid, :]),
                (z_hi.at[zs], part.at[span - wz:span, mid, :]),
                (y_lo.at[ys], part.at[:, r0:r0 + 8, :]),
                (y_hi.at[ys], part.at[:, mid.stop:mid.stop + 8, :]),
            ]
        for src, dst in moves:
            copy = pltpu.make_async_copy(src, dst, sems.at[count])
            copy.start()
            copies[k].append(copy)
            count += 1

    def wait(k):
        for copy in copies[k]:
            copy.wait()

    planes, rows, lanes = p_ref.shape
    species, inner = c_ref.shape[0], c_ref.shape[1] - 2
    hz = (planes - inner) // 2
    hy = (rows - co_ref.shape[2]) // 2
    out_rows = co_ref.shape[2]
    lane = lax.broadcasted_iota(jnp.int32, (rows, lanes), 1)
    top = lane == lanes - 1
    bot = lane == 0

    def ysh(a, d):
        return pltpu.roll(a, (-d) % rows, 0)

    def xsh(a, d):
        return pltpu.roll(a, (-d) % lanes, 1)

    def weights(z, carry):
        pc = p_ref[z]
        ws = (
            0.5 * (pc + p_ref[z + 1]),
            0.5 * (pc + p_ref[z - 1]),
            0.5 * (pc + ysh(pc, 1)),
            0.5 * (pc + ysh(pc, -1)),
            0.5 * (pc + jnp.where(top, pc, xsh(pc, 1))),
            0.5 * (pc + jnp.where(bot, pc, xsh(pc, -1))),
        )
        den = jnp.zeros_like(pc)
        for w in ws:
            den = den + w
        inv = 1.0 / den
        for k in range(4):
            w_ref[k, z] = ws[k] * inv
        w_ref[4, z] = jnp.where(top, 0.0, ws[4]) * inv
        w_ref[5, z] = jnp.where(bot, 0.0, ws[5]) * inv
        w_ref[6, z] = s_ref[z - 1] * inv
        return carry

    wait(1)
    wait(2)
    lax.fori_loop(1, planes - 1, weights, 0, unroll=2)
    wait(0)
    pad = jnp.zeros((planes, 8, lanes), jnp.float32)
    for buf in (f_ref, fa, fb):
        buf[:, 0:8, :] = pad
        buf[:, 88:96, :] = pad
    bufs = (fa, fb)
    sweeps = hz - 1
    for k in range(sweeps):
        rd = f_ref if k == 0 else bufs[(k - 1) % 2]
        wr = bufs[k % 2]

        def sweep(z, carry, rd=rd, wr=wr):
            fc = rd[z, 8:88]
            near_z = (w_ref[6, z] + w_ref[0, z] * rd[z + 1, 8:88]) + w_ref[1, z] * rd[z - 1, 8:88]
            near_y = w_ref[2, z] * rd[z, pl.ds(9, rows)] + w_ref[3, z] * rd[z, pl.ds(7, rows)]
            near_x = w_ref[4, z] * xsh(fc, 1) + w_ref[5, z] * xsh(fc, -1)
            wr[z, 8:88] = near_z + (near_y + near_x)
            return carry

        lax.fori_loop(k + 1, planes - k - 1, sweep, 0, unroll=2)
    final = bufs[(sweeps - 1) % 2]
    wait(3)

    def move(z, carry):
        zf = z + hz
        fc = final[zf, 8:88]
        fo_ref[z] = fc[hy:hy + out_rows]
        pairs_field = (final[zf + 1, 8:88], final[zf - 1, 8:88], ysh(fc, 1), ysh(fc, -1))
        fr = xsh(fc, 1)
        for s in range(species):
            drift = val_ref[s]
            c = c_ref[s, z + 1]
            others = (c_ref[s, z + 2], c_ref[s, z], ysh(c, 1), ysh(c, -1))
            total = jnp.zeros_like(c)
            for other, other_field in zip(others, pairs_field):
                total = total + (c - other) - drift * 0.5 * (c + other) * (other_field - fc)
            right = xsh(c, 1)
            across = c - right - drift * 0.5 * (c + right) * (fr - fc)
            across = jnp.where(top, 0.0, across)
            total = total + across
            total = total - xsh(across, -1)
            new = c - dif_ref[s] * total
            co_ref[s, z] = new[hy:hy + out_rows]
            if with_source:
                charged = drift * new[hy:hy + out_rows]
                mix = charged if s == 0 else mix + charged
        if with_source:
            so_ref[z] = mix + e_ref[z]
        return carry

    lax.fori_loop(0, inner, move, 0, unroll=2)
    if with_source:
        wf, wsrc = hz, hz - 1
        top_ref[0:wf] = fo_ref[inner - wf:inner]
        bot_ref[0:wf] = fo_ref[0:wf]
        top_ref[wf:wf + wsrc] = so_ref[inner - wsrc:inner]
        bot_ref[wf:wf + wsrc] = so_ref[0:wsrc]
        for s in range(species):
            top_ref[wf + wsrc + s] = co_ref[s, inner - 1]
            bot_ref[wf + wsrc + s] = co_ref[s, 0]


def time_step(diffusivity, charge_num, field_p, perm_p, source_p, species_p, electrode=None):
    species, inner, out_rows, lanes = species_p[0].shape
    planes = inner + 2 * field_p[7]
    rows = out_rows + 2 * (SWEEPS + 2)
    plan, operands, boxes = [], [], []
    for pieces, r0 in ((field_p, 8), (perm_p, 0), (source_p, 0), (species_p, 0)):
        inner_arr, z_lo, z_hi, y_lo, y_hi, z_off, y_off, wz = pieces
        lead = inner_arr.shape[0] if inner_arr.ndim == 4 else 1
        plan.append((lead, z_off, y_off, wz, r0))
        operands += [inner_arr, z_lo, z_hi, y_lo, y_hi]
        box_shape = (inner + 2 * wz, rows + 2 * r0, lanes)
        boxes.append(box_shape if inner_arr.ndim == 3 else (lead,) + box_shape)
    smem = pl.BlockSpec(memory_space=pltpu.SMEM)
    vmem = pl.BlockSpec(memory_space=pltpu.VMEM)
    hbm = pl.BlockSpec(memory_space=pl.ANY)
    points = planes * rows * lanes
    moves = sum(1 + 4 * p[0] for p in plan)
    with_source = electrode is not None
    out_shape = [
        jax.ShapeDtypeStruct((inner, out_rows, lanes), jnp.float32),
        jax.ShapeDtypeStruct((species, inner, out_rows, lanes), jnp.float32),
    ]
    extra = []
    if with_source:
        out_shape.append(jax.ShapeDtypeStruct((inner, out_rows, lanes), jnp.float32))
        send = jax.ShapeDtypeStruct((2 * SWEEPS + 1 + species, out_rows, lanes), jnp.float32)
        out_shape += [send, send]
        extra = [electrode]
    return pl.pallas_call(
        functools.partial(step_kernel, tuple(plan), with_source),
        out_shape=tuple(out_shape),
        in_specs=[smem, smem] + [hbm] * len(operands) + [vmem] * len(extra),
        out_specs=tuple([vmem] * len(out_shape)),
        scratch_shapes=[pltpu.VMEM(shape, jnp.float32) for shape in boxes]
        + [
            pltpu.VMEM((planes, rows + 16, lanes), jnp.float32),
            pltpu.VMEM((planes, rows + 16, lanes), jnp.float32),
            pltpu.VMEM((7, planes, rows, lanes), jnp.float32),
            pltpu.SemaphoreType.DMA((moves,)),
        ],
        cost_estimate=pl.CostEstimate(
            flops=points * (20 * SWEEPS + 20) + species * (inner + 2) * rows * lanes * 30,
            transcendentals=0,
            bytes_accessed=4 * (3 * points + inner * out_rows * lanes * (2 * species + 1)),
        ),
    )(diffusivity, charge_num, *operands, *extra)


def box(a, have, want):
    cut = have - want
    if cut == 0:
        return a
    return a[..., cut:a.shape[-3] - cut, cut:a.shape[-2] - cut, :]


def per_device(
    concentration,
    potential,
    permittivity,
    diffusivity,
    valence,
    charge_pos,
    charge_q,
    charge_tile,
    near_index,
    brick_mask,
):
    depth, height, width = potential.shape
    bands = lax.axis_size("narrow")
    rows_total = float(height * bands)
    tiles_all = float(TILES_DEV * bands)
    tile_rows = height // TILES_DEV
    slab = lax.axis_index("wide")
    band = lax.axis_index("narrow")
    index = near_index[0, 0]
    local_z = index // (height * width)
    local_y = index // width % height
    local_x = index % width
    global_z = slab * depth + local_z
    global_y = band * height + local_y
    node_z = global_z.astype(jnp.float32)
    node_y = global_y.astype(jnp.float32)
    node_x = local_x.astype(jnp.float32)
    node_tile = (global_y // tile_rows).astype(jnp.float32)
    slab_float = slab.astype(jnp.float32)
    deep = SWEEPS + 1
    wide_y = SWEEPS + 2
    charges = jnp.concatenate([charge_pos, charge_q, charge_tile.astype(jnp.float32)], axis=0)
    gathered = lax.all_gather(charges, "narrow", axis=1, tiled=True)
    gathered, potential, permittivity, concentration = lax.optimization_barrier(
        (gathered, potential, permittivity, concentration)
    )
    first = deep_halo(
        [(potential, deep, wide_y), (permittivity, deep, wide_y), (concentration, 1, wide_y)],
        "wide",
        "narrow",
    )
    values = pair_field(
        node_z,
        node_y,
        node_x,
        node_tile,
        gathered,
        slab_float,
        depth,
        rows_total,
        width,
        float(tile_rows),
        tiles_all,
    )
    values = values * brick_mask[0, 0].astype(jnp.float32)
    node_row = index // width
    picks = jnp.where(
        node_row[None, :] == jnp.arange(depth * height, dtype=jnp.int32)[:, None], values[None, :], 0.0
    )
    lanes_of = (local_x[:, None] == jnp.arange(width, dtype=jnp.int32)[None, :]).astype(jnp.float32)
    electrode = jnp.dot(picks, lanes_of, precision=lax.Precision.HIGHEST, preferred_element_type=jnp.float32)
    electrode = electrode.reshape(depth, height, width)
    charge_num = valence.astype(jnp.float32)
    field = potential
    species = concentration
    perm_p = first[1]
    for step in range(STEPS):
        if step == 0:
            source = jnp.sum(charge_num[:, None, None, None] * species, axis=0) + electrode
            field_p, species_p = first[0], first[2]
            (source_p,) = deep_halo([(source, deep - 1, wide_y)], "wide", "narrow")
        else:
            field_p, source_p, species_p = deep_halo(
                [(field, deep, wide_y), (source, deep - 1, wide_y), (species, 1, wide_y)],
                "wide",
                "narrow",
                sends,
            )
        if step + 1 < STEPS:
            field, species, source, *sends = time_step(
                diffusivity, charge_num, field_p, perm_p, source_p, species_p, electrode
            )
        else:
            field, species = time_step(diffusivity, charge_num, field_p, perm_p, source_p, species_p)
    return (species, field)


def solution(mesh):
    in_specs = (
        P(None, "wide", "narrow", None),
        P("wide", "narrow", None),
        P("wide", "narrow", None),
        P(),
        P(),
        P(None, ("wide", "narrow")),
        P(None, ("wide", "narrow")),
        P(None, ("wide", "narrow")),
        P("wide", "narrow", None),
        P("wide", "narrow"),
    )
    out_specs = (P(None, "wide", "narrow", None), P("wide", "narrow", None))
    return jax.shard_map(
        per_device, mesh=mesh, in_specs=in_specs, out_specs=out_specs, check_vma=False
    )
```

```python
import functools

import jax
import jax.numpy as jnp
from jax import lax
from jax.sharding import PartitionSpec as P
from jax.experimental import pallas as pl
from jax.experimental.pallas import tpu as pltpu

TILES_DEV = 4
STEPS = 2
SWEEPS = 6


def with_halo(cells, sides, width):
    for axis, dim in sides:
        count = lax.axis_size(axis)
        head = lax.slice_in_dim(cells, 0, width, axis=dim)
        tail = lax.slice_in_dim(cells, cells.shape[dim] - width, cells.shape[dim], axis=dim)
        cells = jnp.concatenate(
            [
                lax.ppermute(tail, axis, [(i, (i + 1) % count) for i in range(count)]),
                cells,
                lax.ppermute(head, axis, [((i + 1) % count, i) for i in range(count)]),
            ],
            axis=dim,
        )
    return cells


def relax(field_pad, perm_pad, source):
    centre = field_pad[1:-1, 1:-1]
    perm_centre = perm_pad[1:-1, 1:-1]
    numer = source
    denom = jnp.zeros_like(source)
    pairs = (
        (field_pad[2:, 1:-1], perm_pad[2:, 1:-1]),
        (field_pad[:-2, 1:-1], perm_pad[:-2, 1:-1]),
        (field_pad[1:-1, 2:], perm_pad[1:-1, 2:]),
        (field_pad[1:-1, :-2], perm_pad[1:-1, :-2]),
    )
    for other_field, other_perm in pairs:
        weight = 0.5 * (perm_centre + other_perm)
        numer = numer + weight * other_field
        denom = denom + weight
    zeros_edge = jnp.zeros_like(centre[..., :1])
    upper_field = jnp.concatenate([centre[..., 1:], zeros_edge], axis=-1)
    lower_field = jnp.concatenate([zeros_edge, centre[..., :-1]], axis=-1)
    upper_perm = jnp.concatenate([perm_centre[..., 1:], perm_centre[..., -1:]], axis=-1)
    lower_perm = jnp.concatenate([perm_centre[..., :1], perm_centre[..., :-1]], axis=-1)
    for other_field, other_perm in ((upper_field, upper_perm), (lower_field, lower_perm)):
        weight = 0.5 * (perm_centre + other_perm)
        numer = numer + weight * other_field
        denom = denom + weight
    return numer / denom


def transport(species_pad, field_pad, diffusivity, charge_num):
    centre = species_pad[:, 1:-1, 1:-1]
    field_centre = field_pad[1:-1, 1:-1]
    drift = charge_num[:, None, None, None]
    total = jnp.zeros_like(centre)
    pairs = (
        (species_pad[:, 2:, 1:-1], field_pad[2:, 1:-1]),
        (species_pad[:, :-2, 1:-1], field_pad[:-2, 1:-1]),
        (species_pad[:, 1:-1, 2:], field_pad[1:-1, 2:]),
        (species_pad[:, 1:-1, :-2], field_pad[1:-1, :-2]),
    )
    for other, other_field in pairs:
        total = (
            total + (centre - other) - drift * 0.5 * (centre + other) * (other_field - field_centre)
        )
    left = centre[..., :-1]
    right = centre[..., 1:]
    across = (
        left
        - right
        - drift * 0.5 * (left + right) * (field_centre[..., 1:] - field_centre[..., :-1])
    )
    zeros_edge = jnp.zeros_like(centre[..., :1])
    total = total + jnp.concatenate([across, zeros_edge], axis=-1)
    total = total - jnp.concatenate([zeros_edge, across], axis=-1)
    return centre - diffusivity[:, None, None, None] * total


def pair_field(
    node_z,
    node_y,
    node_x,
    node_tile,
    block,
    slab_float,
    depth,
    rows_total,
    width,
    tile_rows,
    tiles_all,
):
    charge_x = block[0] * width
    charge_y = (block[4] + block[1]) * tile_rows
    charge_z = (slab_float + block[2]) * depth
    strength = block[3]
    label = block[4]

    def one_block(nodes):
        pos_z, pos_y, pos_x, pos_tile = nodes
        offset_z = pos_z[:, None] - charge_z[None, :]
        offset_y = pos_y[:, None] - charge_y[None, :]
        offset_y = offset_y - rows_total * jnp.floor(offset_y / rows_total + 0.5)
        offset_x = pos_x[:, None] - charge_x[None, :]
        squared = offset_z * offset_z + offset_y * offset_y + offset_x * offset_x
        distance = jnp.sqrt(squared)
        tile_gap = jnp.abs(pos_tile[:, None] - label[None, :])
        adjacent = (tile_gap <= 1.0) | (tile_gap >= tiles_all - 1.0)
        term = strength[None, :] * jnp.exp(-distance / tile_rows) * lax.rsqrt(squared + 1.0)
        return jnp.sum(jnp.where(adjacent, term, 0.0), axis=1)

    half = node_z.shape[0] // 2
    parts = [one_block(tuple(arr[k * half:(k + 1) * half] for arr in (node_z, node_y, node_x, node_tile))) for k in range(2)]
    return jnp.concatenate(parts)


def ring(x, axis, shift):
    count = lax.axis_size(axis)
    return lax.ppermute(x, axis, [(i, (i + shift) % count) for i in range(count)])


def deep_halo(items, axis_z, axis_y):
    minor = items[0][0].shape[-1]
    rows = items[0][0].shape[-2]
    tops, bots = [], []
    for a, wz, _ in items:
        dim = a.ndim - 3
        n = a.shape[dim]
        tops.append(lax.slice_in_dim(a, n - wz, n, axis=dim))
        bots.append(lax.slice_in_dim(a, 0, wz, axis=dim))
    z_lo = ring(jnp.concatenate([t.reshape(-1, minor) for t in tops], axis=0), axis_z, 1)
    z_hi = ring(jnp.concatenate([t.reshape(-1, minor) for t in bots], axis=0), axis_z, -1)
    y_tops, y_bots, z_offs, at = [], [], [], 0
    for (a, wz, wy), t in zip(items, tops):
        size = t.size // minor
        z_offs.append(at // rows)
        ext = jnp.concatenate(
            [z_lo[at:at + size].reshape(t.shape), a, z_hi[at:at + size].reshape(t.shape)], axis=a.ndim - 3
        )
        at += size
        y_tops.append(ext[..., rows - wy:rows, :])
        y_bots.append(ext[..., 0:wy, :])
    wy = items[0][2]
    y_lo = ring(jnp.concatenate([t.reshape(-1, minor) for t in y_tops], axis=0), axis_y, 1)
    y_hi = ring(jnp.concatenate([t.reshape(-1, minor) for t in y_bots], axis=0), axis_y, -1)
    y_offs, at = [], 0
    for t in y_tops:
        y_offs.append(at // wy)
        at += t.size // minor
    bufs = (
        z_lo.reshape(-1, rows, minor),
        z_hi.reshape(-1, rows, minor),
        y_lo.reshape(-1, wy, minor),
        y_hi.reshape(-1, wy, minor),
    )
    return [(a,) + bufs + (zo, yo, wz) for (a, wz, _), zo, yo in zip(items, z_offs, y_offs)]


def step_kernel(plan, with_source, dif_ref, val_ref, *refs):
    hbm = refs[:20]
    rest = list(refs[20:])
    e_ref = rest.pop(0) if with_source else None
    fo_ref, co_ref = rest[0], rest[1]
    so_ref = rest.pop(2) if with_source else None
    f_ref, p_ref, s_ref, c_ref, fa, fb, w_ref, sems = rest[2:]
    targets = (f_ref, p_ref, s_ref, c_ref)
    copies = [[] for _ in targets]
    count = 0
    for k, (lead, z_off, y_off, wz, r0) in enumerate(plan):
        inner_ref, z_lo, z_hi, y_lo, y_hi = hbm[5 * k:5 * k + 5]
        target = targets[k]
        span = 2 * wz + inner_ref.shape[-3]
        mid = slice(r0 + 8, r0 + 8 + inner_ref.shape[-2])
        moves = [(inner_ref, target.at[..., wz:span - wz, mid, :])]
        for s in range(lead):
            part = target.at[s] if lead > 1 or target.ndim == 4 else target
            zs = slice(z_off + s * wz, z_off + (s + 1) * wz)
            ys = slice(y_off + s * span, y_off + (s + 1) * span)
            moves += [
                (z_lo.at[zs], part.at[0:wz, mid, :]),
                (z_hi.at[zs], part.at[span - wz:span, mid, :]),
                (y_lo.at[ys], part.at[:, r0:r0 + 8, :]),
                (y_hi.at[ys], part.at[:, mid.stop:mid.stop + 8, :]),
            ]
        for src, dst in moves:
            copy = pltpu.make_async_copy(src, dst, sems.at[count])
            copy.start()
            copies[k].append(copy)
            count += 1

    def wait(k):
        for copy in copies[k]:
            copy.wait()

    planes, rows, lanes = s_ref.shape[0] + 2, s_ref.shape[1], s_ref.shape[2]
    species, inner = c_ref.shape[0], c_ref.shape[1] - 2
    hz = (planes - inner) // 2
    hy = (rows - co_ref.shape[2]) // 2
    out_rows = co_ref.shape[2]
    lane = lax.broadcasted_iota(jnp.int32, (rows, lanes), 1)
    top = lane == lanes - 1
    bot = lane == 0

    def ysh(a, d):
        return pltpu.roll(a, (-d) % rows, 0)

    def xsh(a, d):
        return pltpu.roll(a, (-d) % lanes, 1)

    def weights(z, carry):
        pc = p_ref[z, 8:88]
        ws = (
            0.5 * (pc + p_ref[z + 1, 8:88]),
            0.5 * (pc + p_ref[z - 1, 8:88]),
            0.5 * (pc + p_ref[z, pl.ds(9, rows)]),
            0.5 * (pc + p_ref[z, pl.ds(7, rows)]),
            0.5 * (pc + jnp.where(top, pc, xsh(pc, 1))),
            0.5 * (pc + jnp.where(bot, pc, xsh(pc, -1))),
        )
        den = jnp.zeros_like(pc)
        for w in ws:
            den = den + w
        inv = 1.0 / den
        for k in range(4):
            w_ref[k, z] = ws[k] * inv
        w_ref[4, z] = jnp.where(top, 0.0, ws[4]) * inv
        w_ref[5, z] = jnp.where(bot, 0.0, ws[5]) * inv
        w_ref[6, z] = s_ref[z - 1] * inv
        return carry

    wait(1)
    wait(2)
    edge = jnp.zeros((planes, 8, lanes), jnp.float32)
    p_ref[:, 0:8, :] = edge
    p_ref[:, 88:96, :] = edge
    lax.fori_loop(1, planes - 1, weights, 0, unroll=2)
    wait(0)
    pad = jnp.zeros((planes, 8, lanes), jnp.float32)
    for buf in (f_ref, fa, fb):
        buf[:, 0:8, :] = pad
        buf[:, 88:96, :] = pad
    bufs = (fa, fb)
    sweeps = hz - 1
    for k in range(sweeps):
        rd = f_ref if k == 0 else bufs[(k - 1) % 2]
        wr = bufs[k % 2]

        def sweep(z, carry, rd=rd, wr=wr):
            fc = rd[z, 8:88]
            near_z = (w_ref[6, z] + w_ref[0, z] * rd[z + 1, 8:88]) + w_ref[1, z] * rd[z - 1, 8:88]
            near_y = w_ref[2, z] * rd[z, pl.ds(9, rows)] + w_ref[3, z] * rd[z, pl.ds(7, rows)]
            near_x = w_ref[4, z] * xsh(fc, 1) + w_ref[5, z] * xsh(fc, -1)
            wr[z, 8:88] = near_z + (near_y + near_x)
            return carry

        lax.fori_loop(k + 1, planes - k - 1, sweep, 0, unroll=2)
    final = bufs[(sweeps - 1) % 2]
    wait(3)

    def move(z, carry):
        zf = z + hz
        fc = final[zf, 8:88]
        fo_ref[z] = fc[hy:hy + out_rows]
        pairs_field = (final[zf + 1, 8:88], final[zf - 1, 8:88], ysh(fc, 1), ysh(fc, -1))
        fr = xsh(fc, 1)
        for s in range(species):
            drift = val_ref[s]
            c = c_ref[s, z + 1]
            others = (c_ref[s, z + 2], c_ref[s, z], ysh(c, 1), ysh(c, -1))
            total = jnp.zeros_like(c)
            for other, other_field in zip(others, pairs_field):
                total = total + (c - other) - drift * 0.5 * (c + other) * (other_field - fc)
            right = xsh(c, 1)
            across = c - right - drift * 0.5 * (c + right) * (fr - fc)
            across = jnp.where(top, 0.0, across)
            total = total + across
            total = total - xsh(across, -1)
            new = c - dif_ref[s] * total
            co_ref[s, z] = new[hy:hy + out_rows]
            if with_source:
                charged = drift * new[hy:hy + out_rows]
                mix = charged if s == 0 else mix + charged
        if with_source:
            so_ref[z] = mix + e_ref[z]
        return carry

    lax.fori_loop(0, inner, move, 0, unroll=2)


def time_step(diffusivity, charge_num, field_p, perm_p, source_p, species_p, electrode=None):
    species, inner, out_rows, lanes = species_p[0].shape
    planes = inner + 2 * field_p[7]
    rows = out_rows + 2 * (SWEEPS + 2)
    plan, operands, boxes = [], [], []
    for pieces, r0 in ((field_p, 8), (perm_p, 8), (source_p, 0), (species_p, 0)):
        inner_arr, z_lo, z_hi, y_lo, y_hi, z_off, y_off, wz = pieces
        lead = inner_arr.shape[0] if inner_arr.ndim == 4 else 1
        plan.append((lead, z_off, y_off, wz, r0))
        operands += [inner_arr, z_lo, z_hi, y_lo, y_hi]
        box_shape = (inner + 2 * wz, rows + 2 * r0, lanes)
        boxes.append(box_shape if inner_arr.ndim == 3 else (lead,) + box_shape)
    smem = pl.BlockSpec(memory_space=pltpu.SMEM)
    vmem = pl.BlockSpec(memory_space=pltpu.VMEM)
    hbm = pl.BlockSpec(memory_space=pl.ANY)
    points = planes * rows * lanes
    moves = sum(1 + 4 * p[0] for p in plan)
    with_source = electrode is not None
    out_shape = [
        jax.ShapeDtypeStruct((inner, out_rows, lanes), jnp.float32),
        jax.ShapeDtypeStruct((species, inner, out_rows, lanes), jnp.float32),
    ]
    extra = []
    if with_source:
        out_shape.append(jax.ShapeDtypeStruct((inner, out_rows, lanes), jnp.float32))
        extra = [electrode]
    return pl.pallas_call(
        functools.partial(step_kernel, tuple(plan), with_source),
        out_shape=tuple(out_shape),
        in_specs=[smem, smem] + [hbm] * len(operands) + [vmem] * len(extra),
        out_specs=tuple([vmem] * len(out_shape)),
        scratch_shapes=[pltpu.VMEM(shape, jnp.float32) for shape in boxes]
        + [
            pltpu.VMEM((planes, rows + 16, lanes), jnp.float32),
            pltpu.VMEM((planes, rows + 16, lanes), jnp.float32),
            pltpu.VMEM((7, planes, rows, lanes), jnp.float32),
            pltpu.SemaphoreType.DMA((moves,)),
        ],
        cost_estimate=pl.CostEstimate(
            flops=points * (20 * SWEEPS + 20) + species * (inner + 2) * rows * lanes * 30,
            transcendentals=0,
            bytes_accessed=4 * (3 * points + inner * out_rows * lanes * (2 * species + 1)),
        ),
    )(diffusivity, charge_num, *operands, *extra)


def box(a, have, want):
    cut = have - want
    if cut == 0:
        return a
    return a[..., cut:a.shape[-3] - cut, cut:a.shape[-2] - cut, :]


def per_device(
    concentration,
    potential,
    permittivity,
    diffusivity,
    valence,
    charge_pos,
    charge_q,
    charge_tile,
    near_index,
    brick_mask,
):
    depth, height, width = potential.shape
    bands = lax.axis_size("narrow")
    rows_total = float(height * bands)
    tiles_all = float(TILES_DEV * bands)
    tile_rows = height // TILES_DEV
    slab = lax.axis_index("wide")
    band = lax.axis_index("narrow")
    index = near_index[0, 0]
    local_z = index // (height * width)
    local_y = index // width % height
    local_x = index % width
    global_z = slab * depth + local_z
    global_y = band * height + local_y
    node_z = global_z.astype(jnp.float32)
    node_y = global_y.astype(jnp.float32)
    node_x = local_x.astype(jnp.float32)
    node_tile = (global_y // tile_rows).astype(jnp.float32)
    slab_float = slab.astype(jnp.float32)
    deep = SWEEPS + 1
    wide_y = SWEEPS + 2
    charges = jnp.concatenate([charge_pos, charge_q, charge_tile.astype(jnp.float32)], axis=0)
    gathered = lax.all_gather(charges, "narrow", axis=1, tiled=True)
    gathered, potential, permittivity, concentration = lax.optimization_barrier(
        (gathered, potential, permittivity, concentration)
    )
    first = deep_halo(
        [(potential, deep, wide_y), (permittivity, deep, wide_y), (concentration, 1, wide_y)],
        "wide",
        "narrow",
    )
    values = pair_field(
        node_z,
        node_y,
        node_x,
        node_tile,
        gathered,
        slab_float,
        depth,
        rows_total,
        width,
        float(tile_rows),
        tiles_all,
    )
    values = values * brick_mask[0, 0].astype(jnp.float32)
    node_row = index // width
    picks = jnp.where(
        node_row[None, :] == jnp.arange(depth * height, dtype=jnp.int32)[:, None], values[None, :], 0.0
    )
    lanes_of = (local_x[:, None] == jnp.arange(width, dtype=jnp.int32)[None, :]).astype(jnp.float32)
    electrode = jnp.dot(picks, lanes_of, precision=lax.Precision.HIGHEST, preferred_element_type=jnp.float32)
    electrode = electrode.reshape(depth, height, width)
    charge_num = valence.astype(jnp.float32)
    field = potential
    species = concentration
    perm_p = first[1]
    for step in range(STEPS):
        if step == 0:
            source = jnp.sum(charge_num[:, None, None, None] * species, axis=0) + electrode
            field_p, species_p = first[0], first[2]
            (source_p,) = deep_halo([(source, deep - 1, wide_y)], "wide", "narrow")
        else:
            field_p, source_p, species_p = deep_halo(
                [(field, deep, wide_y), (source, deep - 1, wide_y), (species, 1, wide_y)], "wide", "narrow"
            )
        if step + 1 < STEPS:
            field, species, source = time_step(
                diffusivity, charge_num, field_p, perm_p, source_p, species_p, electrode
            )
        else:
            field, species = time_step(diffusivity, charge_num, field_p, perm_p, source_p, species_p)
    return (species, field)


def solution(mesh):
    in_specs = (
        P(None, "wide", "narrow", None),
        P("wide", "narrow", None),
        P("wide", "narrow", None),
        P(),
        P(),
        P(None, ("wide", "narrow")),
        P(None, ("wide", "narrow")),
        P(None, ("wide", "narrow")),
        P("wide", "narrow", None),
        P("wide", "narrow"),
    )
    out_specs = (P(None, "wide", "narrow", None), P("wide", "narrow", None))
    return jax.shard_map(
        per_device, mesh=mesh, in_specs=in_specs, out_specs=out_specs, check_vma=False
    )
```

```python
import functools

import jax
import jax.numpy as jnp
from jax import lax
from jax.sharding import PartitionSpec as P
from jax.experimental import pallas as pl
from jax.experimental.pallas import tpu as pltpu

TILES_DEV = 4
STEPS = 2
SWEEPS = 6


def with_halo(cells, sides, width):
    for axis, dim in sides:
        count = lax.axis_size(axis)
        head = lax.slice_in_dim(cells, 0, width, axis=dim)
        tail = lax.slice_in_dim(cells, cells.shape[dim] - width, cells.shape[dim], axis=dim)
        cells = jnp.concatenate(
            [
                lax.ppermute(tail, axis, [(i, (i + 1) % count) for i in range(count)]),
                cells,
                lax.ppermute(head, axis, [((i + 1) % count, i) for i in range(count)]),
            ],
            axis=dim,
        )
    return cells


def relax(field_pad, perm_pad, source):
    centre = field_pad[1:-1, 1:-1]
    perm_centre = perm_pad[1:-1, 1:-1]
    numer = source
    denom = jnp.zeros_like(source)
    pairs = (
        (field_pad[2:, 1:-1], perm_pad[2:, 1:-1]),
        (field_pad[:-2, 1:-1], perm_pad[:-2, 1:-1]),
        (field_pad[1:-1, 2:], perm_pad[1:-1, 2:]),
        (field_pad[1:-1, :-2], perm_pad[1:-1, :-2]),
    )
    for other_field, other_perm in pairs:
        weight = 0.5 * (perm_centre + other_perm)
        numer = numer + weight * other_field
        denom = denom + weight
    zeros_edge = jnp.zeros_like(centre[..., :1])
    upper_field = jnp.concatenate([centre[..., 1:], zeros_edge], axis=-1)
    lower_field = jnp.concatenate([zeros_edge, centre[..., :-1]], axis=-1)
    upper_perm = jnp.concatenate([perm_centre[..., 1:], perm_centre[..., -1:]], axis=-1)
    lower_perm = jnp.concatenate([perm_centre[..., :1], perm_centre[..., :-1]], axis=-1)
    for other_field, other_perm in ((upper_field, upper_perm), (lower_field, lower_perm)):
        weight = 0.5 * (perm_centre + other_perm)
        numer = numer + weight * other_field
        denom = denom + weight
    return numer / denom


def transport(species_pad, field_pad, diffusivity, charge_num):
    centre = species_pad[:, 1:-1, 1:-1]
    field_centre = field_pad[1:-1, 1:-1]
    drift = charge_num[:, None, None, None]
    total = jnp.zeros_like(centre)
    pairs = (
        (species_pad[:, 2:, 1:-1], field_pad[2:, 1:-1]),
        (species_pad[:, :-2, 1:-1], field_pad[:-2, 1:-1]),
        (species_pad[:, 1:-1, 2:], field_pad[1:-1, 2:]),
        (species_pad[:, 1:-1, :-2], field_pad[1:-1, :-2]),
    )
    for other, other_field in pairs:
        total = (
            total + (centre - other) - drift * 0.5 * (centre + other) * (other_field - field_centre)
        )
    left = centre[..., :-1]
    right = centre[..., 1:]
    across = (
        left
        - right
        - drift * 0.5 * (left + right) * (field_centre[..., 1:] - field_centre[..., :-1])
    )
    zeros_edge = jnp.zeros_like(centre[..., :1])
    total = total + jnp.concatenate([across, zeros_edge], axis=-1)
    total = total - jnp.concatenate([zeros_edge, across], axis=-1)
    return centre - diffusivity[:, None, None, None] * total


def pair_field(
    node_z,
    node_y,
    node_x,
    node_tile,
    block,
    slab_float,
    depth,
    rows_total,
    width,
    tile_rows,
    tiles_all,
):
    charge_x = block[0] * width
    charge_y = (block[4] + block[1]) * tile_rows
    charge_z = (slab_float + block[2]) * depth
    strength = block[3]
    label = block[4]

    def one_block(nodes):
        pos_z, pos_y, pos_x, pos_tile = nodes
        offset_z = pos_z[:, None] - charge_z[None, :]
        offset_y = pos_y[:, None] - charge_y[None, :]
        offset_y = offset_y - rows_total * jnp.floor(offset_y / rows_total + 0.5)
        offset_x = pos_x[:, None] - charge_x[None, :]
        squared = offset_z * offset_z + offset_y * offset_y + offset_x * offset_x
        distance = jnp.sqrt(squared)
        tile_gap = jnp.abs(pos_tile[:, None] - label[None, :])
        adjacent = (tile_gap <= 1.0) | (tile_gap >= tiles_all - 1.0)
        term = strength[None, :] * jnp.exp(-distance / tile_rows) * lax.rsqrt(squared + 1.0)
        return jnp.sum(jnp.where(adjacent, term, 0.0), axis=1)

    half = node_z.shape[0] // 2
    parts = [one_block(tuple(arr[k * half:(k + 1) * half] for arr in (node_z, node_y, node_x, node_tile))) for k in range(2)]
    return jnp.concatenate(parts)


def ring(x, axis, shift):
    count = lax.axis_size(axis)
    return lax.ppermute(x, axis, [(i, (i + shift) % count) for i in range(count)])


def deep_halo(items, axis_z, axis_y):
    minor = items[0][0].shape[-1]
    rows = items[0][0].shape[-2]
    tops, bots = [], []
    for a, wz, _ in items:
        dim = a.ndim - 3
        n = a.shape[dim]
        tops.append(lax.slice_in_dim(a, n - wz, n, axis=dim))
        bots.append(lax.slice_in_dim(a, 0, wz, axis=dim))
    z_lo = ring(jnp.concatenate([t.reshape(-1, minor) for t in tops], axis=0), axis_z, 1)
    z_hi = ring(jnp.concatenate([t.reshape(-1, minor) for t in bots], axis=0), axis_z, -1)
    y_tops, y_bots, z_offs, at = [], [], [], 0
    for (a, wz, wy), t in zip(items, tops):
        wy = 1 if a.ndim == 4 else wy
        size = t.size // minor
        z_offs.append(at // rows)
        ext = jnp.concatenate(
            [z_lo[at:at + size].reshape(t.shape), a, z_hi[at:at + size].reshape(t.shape)], axis=a.ndim - 3
        )
        at += size
        y_tops.append(ext[..., rows - wy:rows, :])
        y_bots.append(ext[..., 0:wy, :])
    wy = items[0][2]

    def pack(parts):
        flat = [t.reshape(-1, minor) for t in parts]
        flat = [jnp.pad(f, ((0, -f.shape[0] % wy), (0, 0))) for f in flat]
        return jnp.concatenate(flat, axis=0)

    y_lo = ring(pack(y_tops), axis_y, 1)
    y_hi = ring(pack(y_bots), axis_y, -1)
    y_offs, at = [], 0
    for t in y_tops:
        y_offs.append(at if t.ndim == 4 else at // wy)
        at += -(-(t.size // minor) // wy) * wy
    bufs = (
        z_lo.reshape(-1, rows, minor),
        z_hi.reshape(-1, rows, minor),
        y_lo.reshape(-1, wy, minor),
        y_hi.reshape(-1, wy, minor),
    )
    thin = (y_lo.reshape(-1, 1, minor), y_hi.reshape(-1, 1, minor))
    out = []
    for (a, wz, _), zo, yo in zip(items, z_offs, y_offs):
        y_pair = thin if a.ndim == 4 else bufs[2:]
        out.append((a,) + bufs[:2] + y_pair + (zo, yo, wz))
    return out


def step_kernel(plan, with_source, dif_ref, val_ref, *refs):
    hbm = refs[:20]
    rest = list(refs[20:])
    e_ref = rest.pop(0) if with_source else None
    fo_ref, co_ref = rest[0], rest[1]
    so_ref = rest.pop(2) if with_source else None
    f_ref, p_ref, s_ref, c_ref, fa, fb, w_ref, sems = rest[2:]
    targets = (f_ref, p_ref, s_ref, c_ref)
    copies = [[] for _ in targets]
    count = 0
    for k, (lead, z_off, y_off, wz, r0) in enumerate(plan):
        inner_ref, z_lo, z_hi, y_lo, y_hi = hbm[5 * k:5 * k + 5]
        target = targets[k]
        span = 2 * wz + inner_ref.shape[-3]
        mid = slice(r0 + 8, r0 + 8 + inner_ref.shape[-2])
        moves = [(inner_ref, target.at[..., wz:span - wz, mid, :])]
        for s in range(lead):
            part = target.at[s] if lead > 1 or target.ndim == 4 else target
            zs = slice(z_off + s * wz, z_off + (s + 1) * wz)
            ys = slice(y_off + s * span, y_off + (s + 1) * span)
            moves += [
                (z_lo.at[zs], part.at[0:wz, mid, :]),
                (z_hi.at[zs], part.at[span - wz:span, mid, :]),
                (y_lo.at[ys], part.at[:, r0 + 8 - y_lo.shape[1]:r0 + 8, :]),
                (y_hi.at[ys], part.at[:, mid.stop:mid.stop + y_hi.shape[1], :]),
            ]
        for src, dst in moves:
            copy = pltpu.make_async_copy(src, dst, sems.at[count])
            copy.start()
            copies[k].append(copy)
            count += 1

    def wait(k):
        for copy in copies[k]:
            copy.wait()

    planes, rows, lanes = p_ref.shape
    species, inner = c_ref.shape[0], c_ref.shape[1] - 2
    hz = (planes - inner) // 2
    hy = (rows - co_ref.shape[2]) // 2
    out_rows = co_ref.shape[2]
    lane = lax.broadcasted_iota(jnp.int32, (rows, lanes), 1)
    top = lane == lanes - 1
    bot = lane == 0

    def ysh(a, d):
        return pltpu.roll(a, (-d) % rows, 0)

    def xsh(a, d):
        return pltpu.roll(a, (-d) % lanes, 1)

    def weights(z, carry):
        pc = p_ref[z]
        ws = (
            0.5 * (pc + p_ref[z + 1]),
            0.5 * (pc + p_ref[z - 1]),
            0.5 * (pc + ysh(pc, 1)),
            0.5 * (pc + ysh(pc, -1)),
            0.5 * (pc + jnp.where(top, pc, xsh(pc, 1))),
            0.5 * (pc + jnp.where(bot, pc, xsh(pc, -1))),
        )
        den = jnp.zeros_like(pc)
        for w in ws:
            den = den + w
        inv = 1.0 / den
        for k in range(4):
            w_ref[k, z] = ws[k] * inv
        w_ref[4, z] = jnp.where(top, 0.0, ws[4]) * inv
        w_ref[5, z] = jnp.where(bot, 0.0, ws[5]) * inv
        w_ref[6, z] = s_ref[z - 1] * inv
        return carry

    wait(1)
    wait(2)
    lax.fori_loop(1, planes - 1, weights, 0, unroll=2)
    wait(0)
    pad = jnp.zeros((planes, 8, lanes), jnp.float32)
    for buf in (f_ref, fa, fb):
        buf[:, 0:8, :] = pad
        buf[:, 88:96, :] = pad
    bufs = (fa, fb)
    sweeps = hz - 1
    for k in range(sweeps):
        rd = f_ref if k == 0 else bufs[(k - 1) % 2]
        wr = bufs[k % 2]

        def sweep(z, carry, rd=rd, wr=wr):
            fc = rd[z, 8:88]
            near_z = (w_ref[6, z] + w_ref[0, z] * rd[z + 1, 8:88]) + w_ref[1, z] * rd[z - 1, 8:88]
            near_y = w_ref[2, z] * rd[z, pl.ds(9, rows)] + w_ref[3, z] * rd[z, pl.ds(7, rows)]
            near_x = w_ref[4, z] * xsh(fc, 1) + w_ref[5, z] * xsh(fc, -1)
            wr[z, 8:88] = near_z + (near_y + near_x)
            return carry

        lax.fori_loop(k + 1, planes - k - 1, sweep, 0, unroll=2)
    final = bufs[(sweeps - 1) % 2]
    wait(3)

    def move(z, carry):
        zf = z + hz
        fc = final[zf, 8:88]
        fo_ref[z] = fc[hy:hy + out_rows]
        pairs_field = (final[zf + 1, 8:88], final[zf - 1, 8:88], ysh(fc, 1), ysh(fc, -1))
        fr = xsh(fc, 1)
        for s in range(species):
            drift = val_ref[s]
            c = c_ref[s, z + 1]
            others = (c_ref[s, z + 2], c_ref[s, z], ysh(c, 1), ysh(c, -1))
            total = jnp.zeros_like(c)
            for other, other_field in zip(others, pairs_field):
                total = total + (c - other) - drift * 0.5 * (c + other) * (other_field - fc)
            right = xsh(c, 1)
            across = c - right - drift * 0.5 * (c + right) * (fr - fc)
            across = jnp.where(top, 0.0, across)
            total = total + across
            total = total - xsh(across, -1)
            new = c - dif_ref[s] * total
            co_ref[s, z] = new[hy:hy + out_rows]
            if with_source:
                charged = drift * new[hy:hy + out_rows]
                mix = charged if s == 0 else mix + charged
        if with_source:
            so_ref[z] = mix + e_ref[z]
        return carry

    lax.fori_loop(0, inner, move, 0, unroll=2)


def time_step(diffusivity, charge_num, field_p, perm_p, source_p, species_p, electrode=None):
    species, inner, out_rows, lanes = species_p[0].shape
    planes = inner + 2 * field_p[7]
    rows = out_rows + 2 * (SWEEPS + 2)
    plan, operands, boxes = [], [], []
    for pieces, r0 in ((field_p, 8), (perm_p, 0), (source_p, 0), (species_p, 0)):
        inner_arr, z_lo, z_hi, y_lo, y_hi, z_off, y_off, wz = pieces
        lead = inner_arr.shape[0] if inner_arr.ndim == 4 else 1
        plan.append((lead, z_off, y_off, wz, r0))
        operands += [inner_arr, z_lo, z_hi, y_lo, y_hi]
        box_shape = (inner + 2 * wz, rows + 2 * r0, lanes)
        boxes.append(box_shape if inner_arr.ndim == 3 else (lead,) + box_shape)
    smem = pl.BlockSpec(memory_space=pltpu.SMEM)
    vmem = pl.BlockSpec(memory_space=pltpu.VMEM)
    hbm = pl.BlockSpec(memory_space=pl.ANY)
    points = planes * rows * lanes
    moves = sum(1 + 4 * p[0] for p in plan)
    with_source = electrode is not None
    out_shape = [
        jax.ShapeDtypeStruct((inner, out_rows, lanes), jnp.float32),
        jax.ShapeDtypeStruct((species, inner, out_rows, lanes), jnp.float32),
    ]
    extra = []
    if with_source:
        out_shape.append(jax.ShapeDtypeStruct((inner, out_rows, lanes), jnp.float32))
        extra = [electrode]
    return pl.pallas_call(
        functools.partial(step_kernel, tuple(plan), with_source),
        out_shape=tuple(out_shape),
        in_specs=[smem, smem] + [hbm] * len(operands) + [vmem] * len(extra),
        out_specs=tuple([vmem] * len(out_shape)),
        scratch_shapes=[pltpu.VMEM(shape, jnp.float32) for shape in boxes]
        + [
            pltpu.VMEM((planes, rows + 16, lanes), jnp.float32),
            pltpu.VMEM((planes, rows + 16, lanes), jnp.float32),
            pltpu.VMEM((7, planes, rows, lanes), jnp.float32),
            pltpu.SemaphoreType.DMA((moves,)),
        ],
        cost_estimate=pl.CostEstimate(
            flops=points * (20 * SWEEPS + 20) + species * (inner + 2) * rows * lanes * 30,
            transcendentals=0,
            bytes_accessed=4 * (3 * points + inner * out_rows * lanes * (2 * species + 1)),
        ),
    )(diffusivity, charge_num, *operands, *extra)


def box(a, have, want):
    cut = have - want
    if cut == 0:
        return a
    return a[..., cut:a.shape[-3] - cut, cut:a.shape[-2] - cut, :]


def per_device(
    concentration,
    potential,
    permittivity,
    diffusivity,
    valence,
    charge_pos,
    charge_q,
    charge_tile,
    near_index,
    brick_mask,
):
    depth, height, width = potential.shape
    bands = lax.axis_size("narrow")
    rows_total = float(height * bands)
    tiles_all = float(TILES_DEV * bands)
    tile_rows = height // TILES_DEV
    slab = lax.axis_index("wide")
    band = lax.axis_index("narrow")
    index = near_index[0, 0]
    local_z = index // (height * width)
    local_y = index // width % height
    local_x = index % width
    global_z = slab * depth + local_z
    global_y = band * height + local_y
    node_z = global_z.astype(jnp.float32)
    node_y = global_y.astype(jnp.float32)
    node_x = local_x.astype(jnp.float32)
    node_tile = (global_y // tile_rows).astype(jnp.float32)
    slab_float = slab.astype(jnp.float32)
    deep = SWEEPS + 1
    wide_y = SWEEPS + 2
    charges = jnp.concatenate([charge_pos, charge_q, charge_tile.astype(jnp.float32)], axis=0)
    gathered = lax.all_gather(charges, "narrow", axis=1, tiled=True)
    gathered, potential, permittivity, concentration = lax.optimization_barrier(
        (gathered, potential, permittivity, concentration)
    )
    first = deep_halo(
        [(potential, deep, wide_y), (permittivity, deep, wide_y), (concentration, 1, wide_y)],
        "wide",
        "narrow",
    )
    values = pair_field(
        node_z,
        node_y,
        node_x,
        node_tile,
        gathered,
        slab_float,
        depth,
        rows_total,
        width,
        float(tile_rows),
        tiles_all,
    )
    values = values * brick_mask[0, 0].astype(jnp.float32)
    node_row = index // width
    picks = jnp.where(
        node_row[None, :] == jnp.arange(depth * height, dtype=jnp.int32)[:, None], values[None, :], 0.0
    )
    lanes_of = (local_x[:, None] == jnp.arange(width, dtype=jnp.int32)[None, :]).astype(jnp.float32)
    electrode = jnp.dot(picks, lanes_of, precision=lax.Precision.HIGHEST, preferred_element_type=jnp.float32)
    electrode = electrode.reshape(depth, height, width)
    charge_num = valence.astype(jnp.float32)
    field = potential
    species = concentration
    perm_p = first[1]
    for step in range(STEPS):
        if step == 0:
            source = jnp.sum(charge_num[:, None, None, None] * species, axis=0) + electrode
            field_p, species_p = first[0], first[2]
            (source_p,) = deep_halo([(source, deep - 1, wide_y)], "wide", "narrow")
        else:
            field_p, source_p, species_p = deep_halo(
                [(field, deep, wide_y), (source, deep - 1, wide_y), (species, 1, wide_y)], "wide", "narrow"
            )
        if step + 1 < STEPS:
            field, species, source = time_step(
                diffusivity, charge_num, field_p, perm_p, source_p, species_p, electrode
            )
        else:
            field, species = time_step(diffusivity, charge_num, field_p, perm_p, source_p, species_p)
    return (species, field)


def solution(mesh):
    in_specs = (
        P(None, "wide", "narrow", None),
        P("wide", "narrow", None),
        P("wide", "narrow", None),
        P(),
        P(),
        P(None, ("wide", "narrow")),
        P(None, ("wide", "narrow")),
        P(None, ("wide", "narrow")),
        P("wide", "narrow", None),
        P("wide", "narrow"),
    )
    out_specs = (P(None, "wide", "narrow", None), P("wide", "narrow", None))
    return jax.shard_map(
        per_device, mesh=mesh, in_specs=in_specs, out_specs=out_specs, check_vma=False
    )
```

```python
import functools

import jax
import jax.numpy as jnp
from jax import lax
from jax.sharding import PartitionSpec as P
from jax.experimental import pallas as pl
from jax.experimental.pallas import tpu as pltpu

TILES_DEV = 4
STEPS = 2
SWEEPS = 6


def with_halo(cells, sides, width):
    for axis, dim in sides:
        count = lax.axis_size(axis)
        head = lax.slice_in_dim(cells, 0, width, axis=dim)
        tail = lax.slice_in_dim(cells, cells.shape[dim] - width, cells.shape[dim], axis=dim)
        cells = jnp.concatenate(
            [
                lax.ppermute(tail, axis, [(i, (i + 1) % count) for i in range(count)]),
                cells,
                lax.ppermute(head, axis, [((i + 1) % count, i) for i in range(count)]),
            ],
            axis=dim,
        )
    return cells


def relax(field_pad, perm_pad, source):
    centre = field_pad[1:-1, 1:-1]
    perm_centre = perm_pad[1:-1, 1:-1]
    numer = source
    denom = jnp.zeros_like(source)
    pairs = (
        (field_pad[2:, 1:-1], perm_pad[2:, 1:-1]),
        (field_pad[:-2, 1:-1], perm_pad[:-2, 1:-1]),
        (field_pad[1:-1, 2:], perm_pad[1:-1, 2:]),
        (field_pad[1:-1, :-2], perm_pad[1:-1, :-2]),
    )
    for other_field, other_perm in pairs:
        weight = 0.5 * (perm_centre + other_perm)
        numer = numer + weight * other_field
        denom = denom + weight
    zeros_edge = jnp.zeros_like(centre[..., :1])
    upper_field = jnp.concatenate([centre[..., 1:], zeros_edge], axis=-1)
    lower_field = jnp.concatenate([zeros_edge, centre[..., :-1]], axis=-1)
    upper_perm = jnp.concatenate([perm_centre[..., 1:], perm_centre[..., -1:]], axis=-1)
    lower_perm = jnp.concatenate([perm_centre[..., :1], perm_centre[..., :-1]], axis=-1)
    for other_field, other_perm in ((upper_field, upper_perm), (lower_field, lower_perm)):
        weight = 0.5 * (perm_centre + other_perm)
        numer = numer + weight * other_field
        denom = denom + weight
    return numer / denom


def transport(species_pad, field_pad, diffusivity, charge_num):
    centre = species_pad[:, 1:-1, 1:-1]
    field_centre = field_pad[1:-1, 1:-1]
    drift = charge_num[:, None, None, None]
    total = jnp.zeros_like(centre)
    pairs = (
        (species_pad[:, 2:, 1:-1], field_pad[2:, 1:-1]),
        (species_pad[:, :-2, 1:-1], field_pad[:-2, 1:-1]),
        (species_pad[:, 1:-1, 2:], field_pad[1:-1, 2:]),
        (species_pad[:, 1:-1, :-2], field_pad[1:-1, :-2]),
    )
    for other, other_field in pairs:
        total = (
            total + (centre - other) - drift * 0.5 * (centre + other) * (other_field - field_centre)
        )
    left = centre[..., :-1]
    right = centre[..., 1:]
    across = (
        left
        - right
        - drift * 0.5 * (left + right) * (field_centre[..., 1:] - field_centre[..., :-1])
    )
    zeros_edge = jnp.zeros_like(centre[..., :1])
    total = total + jnp.concatenate([across, zeros_edge], axis=-1)
    total = total - jnp.concatenate([zeros_edge, across], axis=-1)
    return centre - diffusivity[:, None, None, None] * total


def pair_field(
    node_z,
    node_y,
    node_x,
    node_tile,
    block,
    slab_float,
    depth,
    rows_total,
    width,
    tile_rows,
    tiles_all,
):
    charge_x = block[0] * width
    charge_y = (block[4] + block[1]) * tile_rows
    charge_z = (slab_float + block[2]) * depth
    strength = block[3]
    label = block[4]

    def one_block(nodes):
        pos_z, pos_y, pos_x, pos_tile = nodes
        offset_z = pos_z[:, None] - charge_z[None, :]
        offset_y = pos_y[:, None] - charge_y[None, :]
        offset_y = offset_y - rows_total * jnp.floor(offset_y / rows_total + 0.5)
        offset_x = pos_x[:, None] - charge_x[None, :]
        squared = offset_z * offset_z + offset_y * offset_y + offset_x * offset_x
        distance = jnp.sqrt(squared)
        tile_gap = jnp.abs(pos_tile[:, None] - label[None, :])
        adjacent = (tile_gap <= 1.0) | (tile_gap >= tiles_all - 1.0)
        term = strength[None, :] * jnp.exp(-distance / tile_rows) * lax.rsqrt(squared + 1.0)
        return jnp.sum(jnp.where(adjacent, term, 0.0), axis=1)

    half = node_z.shape[0] // 2
    parts = [one_block(tuple(arr[k * half:(k + 1) * half] for arr in (node_z, node_y, node_x, node_tile))) for k in range(2)]
    return jnp.concatenate(parts)


def ring(x, axis, shift):
    count = lax.axis_size(axis)
    return lax.ppermute(x, axis, [(i, (i + shift) % count) for i in range(count)])


def deep_halo(items, axis_z, axis_y):
    minor = items[0][0].shape[-1]
    rows = items[0][0].shape[-2]
    tops, bots = [], []
    for a, wz, _ in items:
        dim = a.ndim - 3
        n = a.shape[dim]
        tops.append(lax.slice_in_dim(a, n - wz, n, axis=dim))
        bots.append(lax.slice_in_dim(a, 0, wz, axis=dim))
    z_lo = ring(jnp.concatenate([t.reshape(-1, minor) for t in tops], axis=0), axis_z, 1)
    z_hi = ring(jnp.concatenate([t.reshape(-1, minor) for t in bots], axis=0), axis_z, -1)
    y_tops, y_bots, z_offs, at = [], [], [], 0
    for (a, wz, wy), t in zip(items, tops):
        wy = 1 if a.ndim == 4 else wy
        size = t.size // minor
        z_offs.append(at // rows)
        ext = jnp.concatenate(
            [z_lo[at:at + size].reshape(t.shape), a, z_hi[at:at + size].reshape(t.shape)], axis=a.ndim - 3
        )
        at += size
        y_tops.append(ext[..., rows - wy:rows, :])
        y_bots.append(ext[..., 0:wy, :])
    wy = items[0][2]

    def pack(parts):
        flat = [t.reshape(-1, minor) for t in parts]
        flat = [jnp.pad(f, ((0, -f.shape[0] % wy), (0, 0))) for f in flat]
        return jnp.concatenate(flat, axis=0)

    y_lo = ring(pack(y_tops), axis_y, 1)
    y_hi = ring(pack(y_bots), axis_y, -1)
    y_offs, at = [], 0
    for t in y_tops:
        y_offs.append(at if t.ndim == 4 else at // wy)
        at += -(-(t.size // minor) // wy) * wy
    bufs = (
        z_lo.reshape(-1, rows, minor),
        z_hi.reshape(-1, rows, minor),
        y_lo.reshape(-1, wy, minor),
        y_hi.reshape(-1, wy, minor),
    )
    thin = (y_lo.reshape(-1, 1, minor), y_hi.reshape(-1, 1, minor))
    out = []
    for (a, wz, _), zo, yo in zip(items, z_offs, y_offs):
        y_pair = thin if a.ndim == 4 else bufs[2:]
        out.append((a,) + bufs[:2] + y_pair + (zo, yo, wz))
    return out


def step_kernel(plan, with_source, dif_ref, val_ref, *refs):
    hbm = refs[:20]
    rest = list(refs[20:])
    e_ref = rest.pop(0) if with_source else None
    fo_ref, co_ref = rest[0], rest[1]
    so_ref = rest.pop(2) if with_source else None
    f_ref, p_ref, s_ref, c_ref, fa, fb, w_ref, sems = rest[2:]
    targets = (f_ref, p_ref, s_ref, c_ref)
    copies = [[] for _ in targets]
    count = 0
    for k, (lead, z_off, y_off, wz, r0) in enumerate(plan):
        inner_ref, z_lo, z_hi, y_lo, y_hi = hbm[5 * k:5 * k + 5]
        target = targets[k]
        span = 2 * wz + inner_ref.shape[-3]
        mid = slice(r0 + 8, r0 + 8 + inner_ref.shape[-2])
        moves = [(inner_ref, target.at[..., wz:span - wz, mid, :])]
        for s in range(lead):
            part = target.at[s] if lead > 1 or target.ndim == 4 else target
            zs = slice(z_off + s * wz, z_off + (s + 1) * wz)
            ys = slice(y_off + s * span, y_off + (s + 1) * span)
            moves += [
                (z_lo.at[zs], part.at[0:wz, mid, :]),
                (z_hi.at[zs], part.at[span - wz:span, mid, :]),
                (y_lo.at[ys], part.at[:, r0 + 8 - y_lo.shape[1]:r0 + 8, :]),
                (y_hi.at[ys], part.at[:, mid.stop:mid.stop + y_hi.shape[1], :]),
            ]
        for src, dst in moves:
            copy = pltpu.make_async_copy(src, dst, sems.at[count])
            copy.start()
            copies[k].append(copy)
            count += 1

    def wait(k):
        for copy in copies[k]:
            copy.wait()

    planes, rows, lanes = p_ref.shape
    species, inner = c_ref.shape[0], c_ref.shape[1] - 2
    hz = (planes - inner) // 2
    hy = (rows - co_ref.shape[2]) // 2
    out_rows = co_ref.shape[2]
    lane = lax.broadcasted_iota(jnp.int32, (rows, lanes), 1)
    top = lane == lanes - 1
    bot = lane == 0

    def ysh(a, d):
        return pltpu.roll(a, (-d) % rows, 0)

    def xsh(a, d):
        return pltpu.roll(a, (-d) % lanes, 1)

    def weights(z, carry):
        pc = p_ref[z]
        ws = (
            0.5 * (pc + p_ref[z + 1]),
            0.5 * (pc + p_ref[z - 1]),
            0.5 * (pc + ysh(pc, 1)),
            0.5 * (pc + ysh(pc, -1)),
            0.5 * (pc + jnp.where(top, pc, xsh(pc, 1))),
            0.5 * (pc + jnp.where(bot, pc, xsh(pc, -1))),
        )
        den = jnp.zeros_like(pc)
        for w in ws:
            den = den + w
        inv = 1.0 / den
        for k in range(4):
            w_ref[k, z] = ws[k] * inv
        w_ref[4, z] = jnp.where(top, 0.0, ws[4]) * inv
        w_ref[5, z] = jnp.where(bot, 0.0, ws[5]) * inv
        w_ref[6, z] = s_ref[z - 1] * inv
        return carry

    wait(1)
    wait(2)
    lax.fori_loop(1, planes - 1, weights, 0, unroll=4)
    wait(0)
    pad = jnp.zeros((planes, 8, lanes), jnp.float32)
    for buf in (f_ref, fa, fb):
        buf[:, 0:8, :] = pad
        buf[:, 88:96, :] = pad
    bufs = (fa, fb)
    sweeps = hz - 1
    for k in range(sweeps):
        rd = f_ref if k == 0 else bufs[(k - 1) % 2]
        wr = bufs[k % 2]

        def sweep(z, carry, rd=rd, wr=wr):
            fc = rd[z, 8:88]
            near_z = (w_ref[6, z] + w_ref[0, z] * rd[z + 1, 8:88]) + w_ref[1, z] * rd[z - 1, 8:88]
            near_y = w_ref[2, z] * rd[z, pl.ds(9, rows)] + w_ref[3, z] * rd[z, pl.ds(7, rows)]
            near_x = w_ref[4, z] * xsh(fc, 1) + w_ref[5, z] * xsh(fc, -1)
            wr[z, 8:88] = near_z + (near_y + near_x)
            return carry

        lax.fori_loop(k + 1, planes - k - 1, sweep, 0, unroll=2)
    final = bufs[(sweeps - 1) % 2]
    wait(3)

    def move(z, carry):
        zf = z + hz
        fc = final[zf, 8:88]
        fo_ref[z] = fc[hy:hy + out_rows]
        pairs_field = (final[zf + 1, 8:88], final[zf - 1, 8:88], ysh(fc, 1), ysh(fc, -1))
        fr = xsh(fc, 1)
        for s in range(species):
            drift = val_ref[s]
            c = c_ref[s, z + 1]
            others = (c_ref[s, z + 2], c_ref[s, z], ysh(c, 1), ysh(c, -1))
            total = jnp.zeros_like(c)
            for other, other_field in zip(others, pairs_field):
                total = total + (c - other) - drift * 0.5 * (c + other) * (other_field - fc)
            right = xsh(c, 1)
            across = c - right - drift * 0.5 * (c + right) * (fr - fc)
            across = jnp.where(top, 0.0, across)
            total = total + across
            total = total - xsh(across, -1)
            new = c - dif_ref[s] * total
            co_ref[s, z] = new[hy:hy + out_rows]
            if with_source:
                charged = drift * new[hy:hy + out_rows]
                mix = charged if s == 0 else mix + charged
        if with_source:
            so_ref[z] = mix + e_ref[z]
        return carry

    lax.fori_loop(0, inner, move, 0, unroll=4)


def time_step(diffusivity, charge_num, field_p, perm_p, source_p, species_p, electrode=None):
    species, inner, out_rows, lanes = species_p[0].shape
    planes = inner + 2 * field_p[7]
    rows = out_rows + 2 * (SWEEPS + 2)
    plan, operands, boxes = [], [], []
    for pieces, r0 in ((field_p, 8), (perm_p, 0), (source_p, 0), (species_p, 0)):
        inner_arr, z_lo, z_hi, y_lo, y_hi, z_off, y_off, wz = pieces
        lead = inner_arr.shape[0] if inner_arr.ndim == 4 else 1
        plan.append((lead, z_off, y_off, wz, r0))
        operands += [inner_arr, z_lo, z_hi, y_lo, y_hi]
        box_shape = (inner + 2 * wz, rows + 2 * r0, lanes)
        boxes.append(box_shape if inner_arr.ndim == 3 else (lead,) + box_shape)
    smem = pl.BlockSpec(memory_space=pltpu.SMEM)
    vmem = pl.BlockSpec(memory_space=pltpu.VMEM)
    hbm = pl.BlockSpec(memory_space=pl.ANY)
    points = planes * rows * lanes
    moves = sum(1 + 4 * p[0] for p in plan)
    with_source = electrode is not None
    out_shape = [
        jax.ShapeDtypeStruct((inner, out_rows, lanes), jnp.float32),
        jax.ShapeDtypeStruct((species, inner, out_rows, lanes), jnp.float32),
    ]
    extra = []
    if with_source:
        out_shape.append(jax.ShapeDtypeStruct((inner, out_rows, lanes), jnp.float32))
        extra = [electrode]
    return pl.pallas_call(
        functools.partial(step_kernel, tuple(plan), with_source),
        out_shape=tuple(out_shape),
        in_specs=[smem, smem] + [hbm] * len(operands) + [vmem] * len(extra),
        out_specs=tuple([vmem] * len(out_shape)),
        scratch_shapes=[pltpu.VMEM(shape, jnp.float32) for shape in boxes]
        + [
            pltpu.VMEM((planes, rows + 16, lanes), jnp.float32),
            pltpu.VMEM((planes, rows + 16, lanes), jnp.float32),
            pltpu.VMEM((7, planes, rows, lanes), jnp.float32),
            pltpu.SemaphoreType.DMA((moves,)),
        ],
        cost_estimate=pl.CostEstimate(
            flops=points * (20 * SWEEPS + 20) + species * (inner + 2) * rows * lanes * 30,
            transcendentals=0,
            bytes_accessed=4 * (3 * points + inner * out_rows * lanes * (2 * species + 1)),
        ),
    )(diffusivity, charge_num, *operands, *extra)


def box(a, have, want):
    cut = have - want
    if cut == 0:
        return a
    return a[..., cut:a.shape[-3] - cut, cut:a.shape[-2] - cut, :]


def per_device(
    concentration,
    potential,
    permittivity,
    diffusivity,
    valence,
    charge_pos,
    charge_q,
    charge_tile,
    near_index,
    brick_mask,
):
    depth, height, width = potential.shape
    bands = lax.axis_size("narrow")
    rows_total = float(height * bands)
    tiles_all = float(TILES_DEV * bands)
    tile_rows = height // TILES_DEV
    slab = lax.axis_index("wide")
    band = lax.axis_index("narrow")
    index = near_index[0, 0]
    local_z = index // (height * width)
    local_y = index // width % height
    local_x = index % width
    global_z = slab * depth + local_z
    global_y = band * height + local_y
    node_z = global_z.astype(jnp.float32)
    node_y = global_y.astype(jnp.float32)
    node_x = local_x.astype(jnp.float32)
    node_tile = (global_y // tile_rows).astype(jnp.float32)
    slab_float = slab.astype(jnp.float32)
    deep = SWEEPS + 1
    wide_y = SWEEPS + 2
    charges = jnp.concatenate([charge_pos, charge_q, charge_tile.astype(jnp.float32)], axis=0)
    gathered = lax.all_gather(charges, "narrow", axis=1, tiled=True)
    gathered, potential, permittivity, concentration = lax.optimization_barrier(
        (gathered, potential, permittivity, concentration)
    )
    first = deep_halo(
        [(potential, deep, wide_y), (permittivity, deep, wide_y), (concentration, 1, wide_y)],
        "wide",
        "narrow",
    )
    values = pair_field(
        node_z,
        node_y,
        node_x,
        node_tile,
        gathered,
        slab_float,
        depth,
        rows_total,
        width,
        float(tile_rows),
        tiles_all,
    )
    values = values * brick_mask[0, 0].astype(jnp.float32)
    node_row = index // width
    picks = jnp.where(
        node_row[None, :] == jnp.arange(depth * height, dtype=jnp.int32)[:, None], values[None, :], 0.0
    )
    lanes_of = (local_x[:, None] == jnp.arange(width, dtype=jnp.int32)[None, :]).astype(jnp.float32)
    electrode = jnp.dot(picks, lanes_of, precision=lax.Precision.HIGHEST, preferred_element_type=jnp.float32)
    electrode = electrode.reshape(depth, height, width)
    charge_num = valence.astype(jnp.float32)
    field = potential
    species = concentration
    perm_p = first[1]
    for step in range(STEPS):
        if step == 0:
            source = jnp.sum(charge_num[:, None, None, None] * species, axis=0) + electrode
            field_p, species_p = first[0], first[2]
            (source_p,) = deep_halo([(source, deep - 1, wide_y)], "wide", "narrow")
        else:
            field_p, source_p, species_p = deep_halo(
                [(field, deep, wide_y), (source, deep - 1, wide_y), (species, 1, wide_y)], "wide", "narrow"
            )
        if step + 1 < STEPS:
            field, species, source = time_step(
                diffusivity, charge_num, field_p, perm_p, source_p, species_p, electrode
            )
        else:
            field, species = time_step(diffusivity, charge_num, field_p, perm_p, source_p, species_p)
    return (species, field)


def solution(mesh):
    in_specs = (
        P(None, "wide", "narrow", None),
        P("wide", "narrow", None),
        P("wide", "narrow", None),
        P(),
        P(),
        P(None, ("wide", "narrow")),
        P(None, ("wide", "narrow")),
        P(None, ("wide", "narrow")),
        P("wide", "narrow", None),
        P("wide", "narrow"),
    )
    out_specs = (P(None, "wide", "narrow", None), P("wide", "narrow", None))
    return jax.shard_map(
        per_device, mesh=mesh, in_specs=in_specs, out_specs=out_specs, check_vma=False
    )
```
